32 devices in a mesh: seq: 8 (over z, x), dp: 4 (over y, core).
Axes of the slice: x: 2, y: 2, z: 4, core: 2. Of those that a mesh axis runs over, the one named last changes fastest.
Arguments:
- encoder_out: bfloat16 [4, 2560, 1536], P('dp', 'seq'), may hold values from -0.59765625 to 0.59765625
- out_grad: bfloat16 [4, 2560, 1536], P('dp', 'seq'), may hold values from -12 to 12
- segment_states: bfloat16 [4, 1024, 1536], P('dp', 'seq'), may hold values from -6 to 6
- segment_starts: int32 [4, 1024], P('dp', 'seq'), may hold values from 0 to 320, as said below
- segment_counts: int32 [4, 8], P('dp', 'seq'), may hold values from 32 to 128, as said below
- segment_probs: int32 [4, 1024], P('dp', 'seq'), may hold values from 0 to 65535, as said below
- query_weight: bfloat16 [1536, 1536], P('dp'), may hold values from -0.15625 to 0.15625
- key_weight: bfloat16 [1536, 1536], P('dp'), may hold values from -0.15625 to 0.15625
Outputs:
- x_grad: bfloat16 [4, 2560, 1536], P('dp', 'seq')
- segment_grad: bfloat16 [4, 1024, 1536], P('dp', 'seq')
The draws below stay inside these ranges and needn't reach their ends.
Inputs may be any that keep to these rules, and one draw needn't show every extreme that they name: `segment_starts`: for block s of sequence b, the entries s * 128 + j with j < segment_counts[b, s] hold distinct increasing local positions below 320 at which segments start; the other entries hold 320. Byte 0 of every sequence starts a segment. `segment_counts`: every sequence has one block with exactly 128 segments and another with exactly a quarter of 128. `segment_probs`: A slot holds 0 exactly when it is past its block's count; slot 0 of every sequence holds 65535.
All inputs are finite; a program needn't handle non-finite values.
Results may differ from the reference program's by a relative error of at most 0.0049.
Values may be sent and summed in bfloat16 or wider, within the bound.
No kernel may reach another device: no remote copies, remote signals or barrier semaphores. Data moves between devices by JAX's collectives and lax.ppermute only.
A program may use at most 64 MiB of HBM per device.

```python
import jax
import jax.numpy as jnp
from jax import lax

D = 1536
TOK_DEV = 320
SLOTS = 128
BATCH_TEXTS = 4
SEQ_LEN = 2560
PIECE_CAPACITY = 1024
N_SEQ = 8


def segment_layout(key):
    key_count = jax.random.fold_in(key, 101)
    key_full = jax.random.fold_in(key, 102)
    key_low = jax.random.fold_in(key, 103)
    key_place = jax.random.fold_in(key, 104)
    counts = jax.random.randint(key_count, (BATCH_TEXTS, N_SEQ), SLOTS // 4, SLOTS + 1)
    full_block = jax.random.randint(key_full, (BATCH_TEXTS, 1), 0, N_SEQ)
    low_block = (full_block + jax.random.randint(key_low, (BATCH_TEXTS, 1), 1, N_SEQ)) % N_SEQ
    block_index = jnp.arange(N_SEQ)[None, :]
    counts = jnp.where(block_index == full_block, SLOTS, counts)
    counts = jnp.where(block_index == low_block, SLOTS // 4, counts)
    position = jnp.arange(TOK_DEV)
    scores = jax.random.randint(key_place, (BATCH_TEXTS, N_SEQ, TOK_DEV), 0, 1 << 18) * TOK_DEV + position
    first_byte = (jnp.arange(N_SEQ)[:, None] == 0) & (position[None, :] == 0)
    scores = jnp.where(first_byte[None], -1, scores)
    ranking = jnp.argsort(jnp.argsort(scores, axis=-1), axis=-1)
    chosen = ranking < counts[:, :, None]
    placed = jnp.sort(jnp.where(chosen, position, TOK_DEV + position), axis=-1)[:, :, :SLOTS]
    starts = jnp.where(placed < TOK_DEV, placed, TOK_DEV)
    return (counts.astype(jnp.int32), starts.reshape(BATCH_TEXTS, PIECE_CAPACITY).astype(jnp.int32))


def draw_segment_starts(key, part):
    return segment_layout(key)[1]


def draw_segment_counts(key, part):
    return segment_layout(key)[0]


def draw_segment_probs(key, part):
    counts = segment_layout(key)[0]
    key_kind = jax.random.fold_in(key, 201)
    key_slow = jax.random.fold_in(key, 202)
    key_fast = jax.random.fold_in(key, 203)
    key_sharp = jax.random.fold_in(key, 204)
    key_sharp_level = jax.random.fold_in(key, 205)
    slow_seq = jax.random.randint(key_kind, (BATCH_TEXTS, 1), 0, 2) == 0
    slow_level = jax.random.randint(key_slow, (BATCH_TEXTS, PIECE_CAPACITY), 4, 17)
    fast_level = jax.random.randint(key_fast, (BATCH_TEXTS, PIECE_CAPACITY), 1311, 3277)
    sharp_boundary = jax.random.randint(key_sharp, (BATCH_TEXTS, PIECE_CAPACITY), 0, PIECE_CAPACITY) < 5
    sharp_level = jax.random.randint(key_sharp_level, (BATCH_TEXTS, PIECE_CAPACITY), 13107, 22938)
    prob_level = jnp.where(slow_seq, slow_level, fast_level)
    prob_level = jnp.where(sharp_boundary, sharp_level, prob_level)
    prob_level = jnp.where(jnp.arange(PIECE_CAPACITY)[None, :] == 0, 65535, prob_level)
    slot_used = (jnp.arange(SLOTS)[None, None, :] < counts[:, :, None]).reshape(BATCH_TEXTS, PIECE_CAPACITY)
    return jnp.where(slot_used, prob_level, 0).astype(jnp.int32)


def levels(stream_key, shape, cuts, low, largest):
    def one(dim, parts):
        heights = jax.random.uniform(jax.random.fold_in(jax.random.fold_in(stream_key, 6), dim), (parts,), jnp.float32, low / len(cuts), largest / len(cuts))
        return jnp.repeat(jnp.exp(heights), shape[dim] // parts).reshape((-1,) + (1,) * (len(shape) - dim - 1))

    loudness = one(*cuts[0])
    for cut in cuts[1:]:
        loudness = loudness * one(*cut)
    return loudness


def scatter_about(own_key, extent, scale, limit, shards=(), kind=jnp.bfloat16):
    level = levels(own_key, extent, shards, -0.22, 0.18) if shards else 1.0
    drawn = jax.random.normal(own_key, extent, jnp.float32) * scale * level
    return jnp.minimum(jnp.maximum(drawn, -limit), limit).astype(kind)


def setup_inputs(seed: int = 0) -> dict:
    seeds = jax.random.split(jax.random.key(seed), 9)
    encoder_out = scatter_about(seeds[0], (BATCH_TEXTS, SEQ_LEN, D), 0.1, 0.59765625, ((0, 4), (1, 8)))
    out_grad = scatter_about(seeds[1], (BATCH_TEXTS, SEQ_LEN, D), 2.0, 12.0, ((0, 4), (1, 8)))
    segment_states = scatter_about(seeds[2], (BATCH_TEXTS, PIECE_CAPACITY, D), 1.0, 6.0, ((0, 4), (1, 8)))
    segment_starts = draw_segment_starts(jax.random.fold_in(seeds[8], 71), 0)
    segment_counts = draw_segment_counts(jax.random.fold_in(seeds[8], 71), 0)
    segment_probs = draw_segment_probs(jax.random.fold_in(seeds[8], 71), 0)
    query_weight = scatter_about(seeds[6], (D, D), D ** -0.5, 0.15625, ((0, 4),))
    key_weight = scatter_about(seeds[7], (D, D), D ** -0.5, 0.15625, ((0, 4),))
    return dict(encoder_out=encoder_out, out_grad=out_grad, segment_states=segment_states, segment_starts=segment_starts, segment_counts=segment_counts, segment_probs=segment_probs, query_weight=query_weight, key_weight=key_weight)


prob_scale = 65536.0
norm_eps = 1e-06

def smooth_step(ema_state, packed):
    smoothing, state_row = packed
    ema_state = smoothing * state_row + (1.0 - smoothing) * ema_state
    return (ema_state, ema_state)

def grad_step(carried, packed):
    slot_grad, smoothing = packed
    grad_total = slot_grad + carried
    return ((1.0 - smoothing) * grad_total, grad_total)

def normalize_grad(vectors, scales, unit_grad):
    inner_prod = lax.optimization_barrier(jnp.sum(vectors * unit_grad, axis=-1, keepdims=True))
    return scales * unit_grad - scales * scales * scales * inner_prod * vectors

def one_sequence(packed, query_weight, key_weight):
    encoder_seq, grad_seq, states_seq, starts_seq, counts_seq, probs_seq = packed
    slot_index = jnp.arange(SLOTS, dtype=jnp.int32)
    slot_used = slot_index[None, :] < counts_seq[:, None]
    smoothing = jnp.where(slot_used.reshape(PIECE_CAPACITY), probs_seq.astype(jnp.float32) / prob_scale, 0.0)
    _, smoothed = lax.scan(smooth_step, jnp.zeros((D,), jnp.float32), (smoothing, states_seq.astype(jnp.float32)))
    start_grid = starts_seq.reshape(N_SEQ, SLOTS)
    position = jnp.arange(TOK_DEV, dtype=jnp.int32)
    reached = slot_used[:, None, :] & (start_grid[:, None, :] <= position[None, :, None])
    member_count = lax.optimization_barrier(jnp.sum(reached.astype(jnp.int32), axis=2))
    block_index = jnp.arange(N_SEQ, dtype=jnp.int32)[:, None]
    slot_owner = (block_index * SLOTS + member_count - 1).reshape(SEQ_LEN).astype(jnp.int32)
    slot_owner = jnp.maximum(slot_owner, 0).astype(jnp.int32)
    matched = slot_used[:, None, :] & (start_grid[:, None, :] == position[None, :, None])
    starts = jnp.any(matched, axis=2).reshape(SEQ_LEN)
    queries = jnp.dot(encoder_seq, query_weight, preferred_element_type=jnp.float32)
    key_rows = jnp.dot(encoder_seq, key_weight, preferred_element_type=jnp.float32)
    query_scale = lax.rsqrt(lax.optimization_barrier(jnp.sum(queries * queries, axis=1, keepdims=True)) + norm_eps)
    key_scale = lax.rsqrt(lax.optimization_barrier(jnp.sum(key_rows * key_rows, axis=1, keepdims=True)) + norm_eps)
    query_unit = queries * query_scale
    key_unit = key_rows * key_scale
    key_before = jnp.concatenate([jnp.zeros((1, D), jnp.float32), key_unit[:-1]], axis=0)
    cosine = lax.optimization_barrier(jnp.sum(query_unit * key_before, axis=1))
    later_rows = jnp.arange(SEQ_LEN) > 0
    boundary_prob = jnp.where(later_rows, 0.5 * (1.0 - cosine), 1.0)
    confidence = jnp.where(starts, boundary_prob, 1.0 - boundary_prob)
    grad_rows = grad_seq.astype(jnp.float32)
    picked = jnp.take(smoothed, slot_owner, axis=0)
    conf_grad = lax.optimization_barrier(jnp.sum(grad_rows * picked, axis=1))
    slot_grad = jax.ops.segment_sum(confidence[:, None] * grad_rows, slot_owner, num_segments=PIECE_CAPACITY)
    _, state_grad = lax.scan(grad_step, jnp.zeros((D,), jnp.float32), (slot_grad, smoothing), reverse=True)
    segment_grad = (smoothing[:, None] * state_grad).astype(jnp.bfloat16)
    cos_grad = jnp.where(later_rows, jnp.where(starts, -0.5 * conf_grad, 0.5 * conf_grad), 0.0)
    unit_q_grad = cos_grad[:, None] * key_before
    shifted = cos_grad[:, None] * query_unit
    unit_k_grad = jnp.concatenate([shifted[1:], jnp.zeros((1, D), jnp.float32)], axis=0)
    query_grad = normalize_grad(queries, query_scale, unit_q_grad).astype(jnp.bfloat16)
    key_grad = normalize_grad(key_rows, key_scale, unit_k_grad).astype(jnp.bfloat16)
    contract = (((1,), (1,)), ((), ()))
    x_grad = lax.dot_general(query_grad, query_weight, contract, preferred_element_type=jnp.float32)
    x_grad = x_grad + lax.dot_general(key_grad, key_weight, contract, preferred_element_type=jnp.float32)
    return (x_grad.astype(jnp.bfloat16), segment_grad)

def reference(encoder_out, out_grad, segment_states, segment_starts, segment_counts, segment_probs, query_weight, key_weight):

    def apply_sequence(packed):
        return one_sequence(packed, query_weight, key_weight)
    x_grad, segment_grad = lax.map(apply_sequence, (encoder_out, out_grad, segment_states, segment_starts, segment_counts, segment_probs))
    return (x_grad, segment_grad)
```

```python
import jax
import jax.numpy as jnp
from jax import lax
from jax.sharding import PartitionSpec as P

prob_scale = 65536.0
norm_eps = 1e-06
exact = lax.Precision.HIGHEST
contract_last = (((1,), (1,)), ((), ()))
contract_first = (((0,), (0,)), ((), ()))


def shifted(block, axis, distance):
    devices = range(lax.axis_size(axis))
    route = [(i - distance, i) for i in devices if i - distance in devices]
    return lax.ppermute(block, axis, route)


def normalize_grad(vectors, scales, unit_grad):
    inner_prod = jnp.sum(vectors * unit_grad, axis=-1, keepdims=True)
    return scales * unit_grad - scales * scales * scales * inner_prod * vectors


def seq_scan(log_keep, vectors, axis, from_lower):
    size = lax.axis_size(axis)
    step = 1
    incl_log, incl_vec = log_keep, vectors
    excl_log = jnp.zeros_like(log_keep)
    excl_vec = jnp.zeros_like(vectors)
    while step < size:
        packed = jnp.concatenate([incl_log, incl_vec], axis=-1)
        got = shifted(packed, axis, step if from_lower else -step)
        got_log, got_vec = got[:, :1], got[:, 1:]
        excl_vec = jnp.exp(excl_log) * got_vec + excl_vec
        excl_log = excl_log + got_log
        if 2 * step < size:
            incl_vec = jnp.exp(incl_log) * got_vec + incl_vec
            incl_log = incl_log + got_log
        step *= 2
    return excl_vec


def per_device(
    encoder_out,
    out_grad,
    segment_states,
    segment_starts,
    segment_counts,
    segment_probs,
    query_weight,
    key_weight,
):
    token_rows = encoder_out[0]
    grad_rows = out_grad[0]
    token_count = token_rows.shape[0]
    slot_count = segment_states.shape[1]
    shard_index = lax.axis_index("seq")
    full_query, full_key = (
        lax.all_gather(query_weight, "dp", axis=0, tiled=True),
        lax.all_gather(key_weight, "dp", axis=0, tiled=True),
    )
    key_rows = jnp.dot(token_rows, full_key, preferred_element_type=jnp.float32)
    queries = jnp.dot(token_rows, full_query, preferred_element_type=jnp.float32)
    query_scale = lax.rsqrt(jnp.sum(queries * queries, axis=1, keepdims=True) + norm_eps)
    key_scale = lax.rsqrt(jnp.sum(key_rows * key_rows, axis=1, keepdims=True) + norm_eps)
    query_unit = queries * query_scale
    key_unit = key_rows * key_scale
    position = jnp.arange(token_count)
    later_rows = (shard_index > 0) | (position > 0)
    key_before = shifted(key_unit[token_count - 1 :], "seq", 1)
    key_prior = jnp.concatenate([key_before, key_unit[:-1]], axis=0)
    cosine = jnp.sum(query_unit * key_prior, axis=1)
    segment_total = segment_counts[0, 0]
    slot_index = jnp.arange(slot_count)
    slot_used = slot_index < segment_total
    start_pos = segment_starts[0]
    smoothing = jnp.where(slot_used, segment_probs[0].astype(jnp.float32) / prob_scale, 0.0)
    reached = slot_used[None, :] & (start_pos[None, :] <= position[:, None])
    member_id = jnp.sum(reached.astype(jnp.int32), axis=1) - 1
    membership = (member_id[:, None] == slot_index[None, :]).astype(jnp.float32)
    leading = (member_id < 0).astype(jnp.float32)
    starts = jnp.any(slot_used[None, :] & (start_pos[None, :] == position[:, None]), axis=1)
    running = jnp.cumsum(jnp.log(1.0 - smoothing))
    lower = slot_index[None, :] <= slot_index[:, None]
    decay_table = jnp.where(
        lower, jnp.exp(jnp.where(lower, running[:, None] - running[None, :], 0.0)), 0.0
    )
    weighted_states = smoothing[:, None] * segment_states[0].astype(jnp.float32)
    local_state = jnp.dot(decay_table, weighted_states, precision=exact)
    keep_all = jnp.exp(running)
    boundary_prob = jnp.where(later_rows, 0.5 * (1.0 - cosine), 1.0)
    confidence = jnp.where(starts, boundary_prob, 1.0 - boundary_prob)
    weighted_grad = confidence[:, None] * grad_rows
    slot_grad = lax.dot_general(membership, weighted_grad, contract_first, precision=exact)
    lead_grad = jnp.dot(leading[None, :], weighted_grad, precision=exact)
    back_vector = lead_grad + jnp.dot(keep_all[None, :], slot_grad, precision=exact)
    last_log = running[slot_count - 1 :]
    last_state = local_state[slot_count - 1 :]
    state_in = seq_scan(last_log[None], last_state, "seq", True)
    grad_in = seq_scan(last_log[None], back_vector, "seq", False)
    smoothed = local_state + keep_all[:, None] * state_in
    picked = jnp.dot(membership, smoothed, precision=exact) + leading[:, None] * state_in
    conf_grad = jnp.sum(grad_rows * picked, axis=1)
    cos_grad = jnp.where(later_rows, jnp.where(starts, -0.5 * conf_grad, 0.5 * conf_grad), 0.0)
    reach_end = jnp.exp(running[slot_count - 1] - running)
    state_grad = (
        lax.dot_general(decay_table, slot_grad, contract_first, precision=exact)
        + reach_end[:, None] * grad_in
    )
    segment_grad = (smoothing[:, None] * state_grad).astype(jnp.bfloat16)
    unit_q_grad = cos_grad[:, None] * key_prior
    prior_grad = cos_grad[:, None] * query_unit
    query_grad = normalize_grad(queries, query_scale, unit_q_grad).astype(jnp.bfloat16)
    from_next = shifted(prior_grad[:1], "seq", -1)
    unit_k_grad = jnp.concatenate([prior_grad[1:], from_next], axis=0)
    key_grad = normalize_grad(key_rows, key_scale, unit_k_grad).astype(jnp.bfloat16)
    x_grad = lax.dot_general(
        query_grad, full_query, contract_last, preferred_element_type=jnp.float32
    )
    x_grad = x_grad + lax.dot_general(
        key_grad, full_key, contract_last, preferred_element_type=jnp.float32
    )
    return (x_grad.astype(jnp.bfloat16)[None], segment_grad[None])


def solution(mesh):
    placed = (
        P("dp", "seq", None),
        P("dp", "seq", None),
        P("dp", "seq", None),
        P("dp", "seq"),
        P("dp", "seq"),
        P("dp", "seq"),
        P("dp", None),
        P("dp", None),
    )
    return jax.shard_map(
        per_device,
        mesh=mesh,
        in_specs=placed,
        out_specs=(P("dp", "seq", None), P("dp", "seq", None)),
        check_vma=False,
    )
```

```python
import jax
import jax.numpy as jnp
from jax import lax
from jax.sharding import PartitionSpec as P

prob_scale = 65536.0
norm_eps = 1e-06
exact = lax.Precision.HIGHEST
contract_last = (((1,), (1,)), ((), ()))
contract_first = (((0,), (0,)), ((), ()))


def shifted(block, axis, distance):
    devices = range(lax.axis_size(axis))
    route = [(i - distance, i) for i in devices if i - distance in devices]
    return lax.ppermute(block, axis, route)


def normalize_grad(vectors, scales, unit_grad):
    inner_prod = jnp.sum(vectors * unit_grad, axis=-1, keepdims=True)
    return scales * unit_grad - scales * scales * scales * inner_prod * vectors


def seq_scan(log_keep, vectors, axis, from_lower):
    size = lax.axis_size(axis)
    step = 1
    incl_log, incl_vec = log_keep, vectors
    excl_log = jnp.zeros_like(log_keep)
    excl_vec = jnp.zeros_like(vectors)
    while step < size:
        packed = jnp.concatenate([incl_log, incl_vec], axis=-1)
        got = shifted(packed, axis, step if from_lower else -step)
        got_log, got_vec = got[:, :1], got[:, 1:]
        excl_vec = jnp.exp(excl_log) * got_vec + excl_vec
        excl_log = excl_log + got_log
        if 2 * step < size:
            incl_vec = jnp.exp(incl_log) * got_vec + incl_vec
            incl_log = incl_log + got_log
        step *= 2
    return excl_vec


def gather_blocks(blocks, axis):
    size = lax.axis_size(axis)
    own = lax.axis_index(axis)
    pairs = [blocks]
    index = [own]
    for k in range(1, size // 2):
        route = [(i, (i + 2 * k) % size) for i in range(size)]
        pairs.append(lax.ppermute(blocks, axis, route))
        index.append((own - 2 * k) % size)
    swap = [(i, i ^ 1) for i in range(size)]
    partner = lax.ppermute(pairs, axis, swap)
    pairs = pairs + partner
    index = index + [i ^ 1 for i in index]
    return pairs, index


def split_dot(rows, blocks, index, width):
    total = None
    for block, at in zip(blocks, index):
        part = lax.dynamic_slice_in_dim(rows, at * width, width, axis=1)
        term = jnp.dot(part, block, preferred_element_type=jnp.float32)
        total = term if total is None else total + term
    return total


def per_device(
    encoder_out,
    out_grad,
    segment_states,
    segment_starts,
    segment_counts,
    segment_probs,
    query_weight,
    key_weight,
):
    token_rows = encoder_out[0]
    grad_rows = out_grad[0]
    token_count = token_rows.shape[0]
    slot_count = segment_states.shape[1]
    shard_index = lax.axis_index("seq")
    pairs, index = gather_blocks((query_weight, key_weight), "dp")
    width = query_weight.shape[0]
    key_rows = split_dot(token_rows, [p[1] for p in pairs], index, width)
    queries = split_dot(token_rows, [p[0] for p in pairs], index, width)
    query_scale = lax.rsqrt(jnp.sum(queries * queries, axis=1, keepdims=True) + norm_eps)
    key_scale = lax.rsqrt(jnp.sum(key_rows * key_rows, axis=1, keepdims=True) + norm_eps)
    query_unit = queries * query_scale
    key_unit = key_rows * key_scale
    position = jnp.arange(token_count)
    later_rows = (shard_index > 0) | (position > 0)
    key_before = shifted(key_unit[token_count - 1 :], "seq", 1)
    key_prior = jnp.concatenate([key_before, key_unit[:-1]], axis=0)
    cosine = jnp.sum(query_unit * key_prior, axis=1)
    segment_total = segment_counts[0, 0]
    slot_index = jnp.arange(slot_count)
    slot_used = slot_index < segment_total
    start_pos = segment_starts[0]
    smoothing = jnp.where(slot_used, segment_probs[0].astype(jnp.float32) / prob_scale, 0.0)
    reached = slot_used[None, :] & (start_pos[None, :] <= position[:, None])
    member_id = jnp.sum(reached.astype(jnp.int32), axis=1) - 1
    membership = (member_id[:, None] == slot_index[None, :]).astype(jnp.float32)
    leading = (member_id < 0).astype(jnp.float32)
    starts = jnp.any(slot_used[None, :] & (start_pos[None, :] == position[:, None]), axis=1)
    running = jnp.cumsum(jnp.log(1.0 - smoothing))
    lower = slot_index[None, :] <= slot_index[:, None]
    decay_table = jnp.where(
        lower, jnp.exp(jnp.where(lower, running[:, None] - running[None, :], 0.0)), 0.0
    )
    weighted_states = smoothing[:, None] * segment_states[0].astype(jnp.float32)
    local_state = jnp.dot(decay_table, weighted_states, precision=exact)
    keep_all = jnp.exp(running)
    boundary_prob = jnp.where(later_rows, 0.5 * (1.0 - cosine), 1.0)
    confidence = jnp.where(starts, boundary_prob, 1.0 - boundary_prob)
    weighted_grad = confidence[:, None] * grad_rows
    slot_grad = lax.dot_general(membership, weighted_grad, contract_first, precision=exact)
    lead_grad = jnp.dot(leading[None, :], weighted_grad, precision=exact)
    back_vector = lead_grad + jnp.dot(keep_all[None, :], slot_grad, precision=exact)
    last_log = running[slot_count - 1 :]
    last_state = local_state[slot_count - 1 :]
    state_in = seq_scan(last_log[None], last_state, "seq", True)
    grad_in = seq_scan(last_log[None], back_vector, "seq", False)
    smoothed = local_state + keep_all[:, None] * state_in
    picked = jnp.dot(membership, smoothed, precision=exact) + leading[:, None] * state_in
    conf_grad = jnp.sum(grad_rows * picked, axis=1)
    cos_grad = jnp.where(later_rows, jnp.where(starts, -0.5 * conf_grad, 0.5 * conf_grad), 0.0)
    reach_end = jnp.exp(running[slot_count - 1] - running)
    state_grad = (
        lax.dot_general(decay_table, slot_grad, contract_first, precision=exact)
        + reach_end[:, None] * grad_in
    )
    segment_grad = (smoothing[:, None] * state_grad).astype(jnp.bfloat16)
    unit_q_grad = cos_grad[:, None] * key_prior
    prior_grad = cos_grad[:, None] * query_unit
    query_grad = normalize_grad(queries, query_scale, unit_q_grad).astype(jnp.bfloat16)
    from_next = shifted(prior_grad[:1], "seq", -1)
    unit_k_grad = jnp.concatenate([prior_grad[1:], from_next], axis=0)
    key_grad = normalize_grad(key_rows, key_scale, unit_k_grad).astype(jnp.bfloat16)
    parts = []
    for (q_block, k_block) in pairs:
        part = lax.dot_general(query_grad, q_block, contract_last, preferred_element_type=jnp.float32)
        part = part + lax.dot_general(key_grad, k_block, contract_last, preferred_element_type=jnp.float32)
        parts.append(part.astype(jnp.bfloat16))
    order = jnp.zeros((len(index),), jnp.int32).at[jnp.stack(index)].set(jnp.arange(len(index), dtype=jnp.int32))
    x_grad = jnp.stack(parts)[order]
    x_grad = jnp.transpose(x_grad, (1, 0, 2)).reshape(token_count, -1)
    return (x_grad[None], segment_grad[None])


def solution(mesh):
    placed = (
        P("dp", "seq", None),
        P("dp", "seq", None),
        P("dp", "seq", None),
        P("dp", "seq"),
        P("dp", "seq"),
        P("dp", "seq"),
        P("dp", None),
        P("dp", None),
    )
    return jax.shard_map(
        per_device,
        mesh=mesh,
        in_specs=placed,
        out_specs=(P("dp", "seq", None), P("dp", "seq", None)),
        check_vma=False,
    )
```

```python
import jax
import jax.numpy as jnp
from jax import lax
from jax.sharding import PartitionSpec as P

prob_scale = 65536.0
norm_eps = 1e-06
exact = lax.Precision.HIGHEST
contract_last = (((1,), (1,)), ((), ()))
contract_first = (((0,), (0,)), ((), ()))


def shifted(block, axis, distance):
    devices = range(lax.axis_size(axis))
    route = [(i - distance, i) for i in devices if i - distance in devices]
    return lax.ppermute(block, axis, route)


def normalize_grad(vectors, scales, unit_grad):
    inner_prod = jnp.sum(vectors * unit_grad, axis=-1, keepdims=True)
    return scales * unit_grad - scales * scales * scales * inner_prod * vectors


def seq_scan(log_keep, vectors, axis, from_lower):
    size = lax.axis_size(axis)
    step = 1
    incl_log, incl_vec = log_keep, vectors
    excl_log = jnp.zeros_like(log_keep)
    excl_vec = jnp.zeros_like(vectors)
    while step < size:
        packed = jnp.concatenate([incl_vec, incl_log], axis=-1)
        got = shifted(packed, axis, step if from_lower else -step)
        got_log, got_vec = got[:, -1:], got[:, :-1]
        excl_vec = jnp.exp(excl_log) * got_vec + excl_vec
        excl_log = excl_log + got_log
        if 2 * step < size:
            incl_vec = jnp.exp(incl_log) * got_vec + incl_vec
            incl_log = incl_log + got_log
        step *= 2
    return excl_vec


def gather_blocks(blocks, axis):
    size = lax.axis_size(axis)
    own = lax.axis_index(axis)
    pairs = [blocks]
    index = [own]
    for k in range(1, size // 2):
        route = [(i, (i + 2 * k) % size) for i in range(size)]
        pairs.append(lax.ppermute(blocks, axis, route))
        index.append((own - 2 * k) % size)
    swap = [(i, i ^ 1) for i in range(size)]
    partner = lax.ppermute(pairs, axis, swap)
    pairs = pairs + partner
    index = index + [i ^ 1 for i in index]
    return pairs, index


def direct_scan(log_keep, vectors, axis):
    size = lax.axis_size(axis)
    packed = jnp.concatenate([vectors, log_keep], axis=-1)
    total = jnp.zeros_like(vectors)
    gap = jnp.zeros_like(log_keep)
    for step in range(1, size):
        got = shifted(packed, axis, -step)
        total = total + jnp.exp(gap) * got[:, :-1]
        gap = gap + got[:, -1:]
    return total


def assemble(blocks, index, width):
    full = jnp.zeros((width * len(blocks),) + blocks[0].shape[1:], blocks[0].dtype)
    for block, at in zip(blocks, index):
        full = lax.dynamic_update_slice_in_dim(full, block, at * width, axis=0)
    return full


def split_dot(rows, blocks, index, width):
    total = None
    for block, at in zip(blocks, index):
        part = lax.dynamic_slice_in_dim(rows, at * width, width, axis=1)
        term = jnp.dot(part, block, preferred_element_type=jnp.float32)
        total = term if total is None else total + term
    return total


def per_device(
    encoder_out,
    out_grad,
    segment_states,
    segment_starts,
    segment_counts,
    segment_probs,
    query_weight,
    key_weight,
):
    token_rows = encoder_out[0]
    grad_rows = out_grad[0]
    token_count = token_rows.shape[0]
    slot_count = segment_states.shape[1]
    shard_index = lax.axis_index("seq")
    pairs, index = gather_blocks((query_weight, key_weight), "dp")
    width = query_weight.shape[0]
    full_query = assemble([p[0] for p in pairs], index, width)
    full_key = assemble([p[1] for p in pairs], index, width)
    key_rows = jnp.dot(token_rows, full_key, preferred_element_type=jnp.float32)
    queries = jnp.dot(token_rows, full_query, preferred_element_type=jnp.float32)
    query_scale = lax.rsqrt(jnp.sum(queries * queries, axis=1, keepdims=True) + norm_eps)
    key_scale = lax.rsqrt(jnp.sum(key_rows * key_rows, axis=1, keepdims=True) + norm_eps)
    query_unit = queries * query_scale
    key_unit = key_rows * key_scale
    position = jnp.arange(token_count)
    later_rows = (shard_index > 0) | (position > 0)
    key_before = shifted(key_unit[token_count - 1 :], "seq", 1)
    key_prior = jnp.concatenate([key_before, key_unit[:-1]], axis=0)
    cosine = jnp.sum(query_unit * key_prior, axis=1)
    segment_total = segment_counts[0, 0]
    slot_index = jnp.arange(slot_count)
    slot_used = slot_index < segment_total
    start_pos = segment_starts[0]
    smoothing = jnp.where(slot_used, segment_probs[0].astype(jnp.float32) / prob_scale, 0.0)
    reached = slot_used[None, :] & (start_pos[None, :] <= position[:, None])
    member_id = jnp.sum(reached.astype(jnp.int32), axis=1) - 1
    membership = (member_id[:, None] == slot_index[None, :]).astype(jnp.float32)
    leading = (member_id < 0).astype(jnp.float32)
    starts = jnp.any(slot_used[None, :] & (start_pos[None, :] == position[:, None]), axis=1)
    running = jnp.cumsum(jnp.log(1.0 - smoothing))
    lower = slot_index[None, :] <= slot_index[:, None]
    decay_table = jnp.where(
        lower, jnp.exp(jnp.where(lower, running[:, None] - running[None, :], 0.0)), 0.0
    )
    weighted_states = smoothing[:, None] * segment_states[0].astype(jnp.float32)
    local_state = jnp.dot(decay_table, weighted_states, precision=exact)
    keep_all = jnp.exp(running)
    boundary_prob = jnp.where(later_rows, 0.5 * (1.0 - cosine), 1.0)
    confidence = jnp.where(starts, boundary_prob, 1.0 - boundary_prob)
    weighted_grad = confidence[:, None] * grad_rows
    slot_grad = lax.dot_general(membership, weighted_grad, contract_first, precision=exact)
    lead_grad = jnp.dot(leading[None, :], weighted_grad, precision=exact)
    back_vector = lead_grad + jnp.dot(keep_all[None, :], slot_grad, precision=exact)
    last_log = running[slot_count - 1 :]
    last_state = local_state[slot_count - 1 :]
    state_in = seq_scan(last_log[None], last_state, "seq", True)
    if lax.axis_size("seq") <= 8:
        grad_in = direct_scan(last_log[None], back_vector, "seq")
    else:
        grad_in = seq_scan(last_log[None], back_vector, "seq", False)
    smoothed = local_state + keep_all[:, None] * state_in
    picked = jnp.dot(membership, smoothed, precision=exact) + leading[:, None] * state_in
    conf_grad = jnp.sum(grad_rows * picked, axis=1)
    cos_grad = jnp.where(later_rows, jnp.where(starts, -0.5 * conf_grad, 0.5 * conf_grad), 0.0)
    reach_end = jnp.exp(running[slot_count - 1] - running)
    state_grad = (
        lax.dot_general(decay_table, slot_grad, contract_first, precision=exact)
        + reach_end[:, None] * grad_in
    )
    segment_grad = (smoothing[:, None] * state_grad).astype(jnp.bfloat16)
    unit_q_grad = cos_grad[:, None] * key_prior
    prior_grad = cos_grad[:, None] * query_unit
    query_grad = normalize_grad(queries, query_scale, unit_q_grad).astype(jnp.bfloat16)
    from_next = shifted(prior_grad[:1], "seq", -1)
    unit_k_grad = jnp.concatenate([prior_grad[1:], from_next], axis=0)
    key_grad = normalize_grad(key_rows, key_scale, unit_k_grad).astype(jnp.bfloat16)
    x_grad = lax.dot_general(
        query_grad, full_query, contract_last, preferred_element_type=jnp.float32
    )
    x_grad = x_grad + lax.dot_general(
        key_grad, full_key, contract_last, preferred_element_type=jnp.float32
    )
    x_grad = x_grad.astype(jnp.bfloat16)
    return (x_grad[None], segment_grad[None])


def solution(mesh):
    placed = (
        P("dp", "seq", None),
        P("dp", "seq", None),
        P("dp", "seq", None),
        P("dp", "seq"),
        P("dp", "seq"),
        P("dp", "seq"),
        P("dp", None),
        P("dp", None),
    )
    return jax.shard_map(
        per_device,
        mesh=mesh,
        in_specs=placed,
        out_specs=(P("dp", "seq", None), P("dp", "seq", None)),
        check_vma=False,
    )
```

```python
import jax
import jax.numpy as jnp
from jax import lax
from jax.sharding import PartitionSpec as P

prob_scale = 65536.0
norm_eps = 1e-06
exact = lax.Precision.HIGHEST
contract_last = (((1,), (1,)), ((), ()))
contract_first = (((0,), (0,)), ((), ()))


def shifted(block, axis, distance):
    devices = range(lax.axis_size(axis))
    route = [(i - distance, i) for i in devices if i - distance in devices]
    return lax.ppermute(block, axis, route)


def normalize_grad(vectors, scales, unit_grad):
    inner_prod = jnp.sum(vectors * unit_grad, axis=-1, keepdims=True)
    return scales * unit_grad - scales * scales * scales * inner_prod * vectors


def seq_scan(log_keep, vectors, axis, from_lower):
    size = lax.axis_size(axis)
    step = 1
    incl_log, incl_vec = log_keep, vectors
    excl_log = jnp.zeros_like(log_keep)
    excl_vec = jnp.zeros_like(vectors)
    while step < size:
        packed = jnp.concatenate([incl_vec, incl_log], axis=-1)
        got = shifted(packed, axis, step if from_lower else -step)
        got_log, got_vec = got[:, -1:], got[:, :-1]
        excl_vec = jnp.exp(excl_log) * got_vec + excl_vec
        excl_log = excl_log + got_log
        if 2 * step < size:
            incl_vec = jnp.exp(incl_log) * got_vec + incl_vec
            incl_log = incl_log + got_log
        step *= 2
    return excl_vec


def gather_blocks(blocks, axis):
    size = lax.axis_size(axis)
    own = lax.axis_index(axis)
    pairs = [blocks]
    index = [own]
    for k in range(1, size // 2):
        route = [(i, (i + 2 * k) % size) for i in range(size)]
        pairs.append(lax.ppermute(blocks, axis, route))
        index.append((own - 2 * k) % size)
    swap = [(i, i ^ 1) for i in range(size)]
    partner = lax.ppermute(pairs, axis, swap)
    pairs = pairs + partner
    index = index + [i ^ 1 for i in index]
    return pairs, index


def direct_scan(log_keep, vectors, axis):
    size = lax.axis_size(axis)
    packed = jnp.concatenate([vectors, log_keep], axis=-1)
    total = jnp.zeros_like(vectors)
    gap = jnp.zeros_like(log_keep)
    for step in range(1, size):
        got = shifted(packed, axis, -step)
        total = total + jnp.exp(gap) * got[:, :-1]
        gap = gap + got[:, -1:]
    return total


def permute_cols(rows, index, width):
    return jnp.concatenate(
        [lax.dynamic_slice_in_dim(rows, at * width, width, axis=1) for at in index], axis=1
    )


def unit_of(rows):
    scale = lax.rsqrt(jnp.sum(rows * rows, axis=1, keepdims=True) + norm_eps)
    return rows * scale, scale


def per_device(
    encoder_out,
    out_grad,
    segment_states,
    segment_starts,
    segment_counts,
    segment_probs,
    query_weight,
    key_weight,
):
    token_rows = encoder_out[0]
    grad_rows = out_grad[0]
    token_count = token_rows.shape[0]
    slot_count = segment_states.shape[1]
    width = query_weight.shape[0]
    shard_index = lax.axis_index("seq")
    pairs, index = gather_blocks((query_weight, key_weight), "dp")
    full_query = jnp.concatenate([p[0] for p in pairs], axis=0)
    full_key = jnp.concatenate([p[1] for p in pairs], axis=0)
    position = jnp.arange(token_count)
    later_rows = (shard_index > 0) | (position > 0)
    segment_total = segment_counts[0, 0]
    slot_index = jnp.arange(slot_count)
    slot_used = slot_index < segment_total
    start_pos = segment_starts[0]
    smoothing = jnp.where(slot_used, segment_probs[0].astype(jnp.float32) / prob_scale, 0.0)
    reached = slot_used[None, :] & (start_pos[None, :] <= position[:, None])
    member_id = jnp.sum(reached.astype(jnp.int32), axis=1) - 1
    membership = (member_id[:, None] == slot_index[None, :]).astype(jnp.float32)
    leading = (member_id < 0).astype(jnp.float32)
    starts = jnp.any(slot_used[None, :] & (start_pos[None, :] == position[:, None]), axis=1)
    running = jnp.cumsum(jnp.log(1.0 - smoothing))
    lower = slot_index[None, :] <= slot_index[:, None]
    decay_table = jnp.where(
        lower, jnp.exp(jnp.where(lower, running[:, None] - running[None, :], 0.0)), 0.0
    )
    weighted_states = smoothing[:, None] * segment_states[0].astype(jnp.float32)
    local_state = jnp.dot(decay_table, weighted_states, precision=exact)
    keep_all = jnp.exp(running)
    last_log = running[slot_count - 1 :][None]
    state_in = seq_scan(last_log, local_state[slot_count - 1 :], "seq", True)
    smoothed = local_state + keep_all[:, None] * state_in
    picked = jnp.dot(membership, smoothed, precision=exact) + leading[:, None] * state_in
    conf_grad = jnp.sum(grad_rows * picked, axis=1)
    cos_grad = jnp.where(later_rows, jnp.where(starts, -0.5 * conf_grad, 0.5 * conf_grad), 0.0)
    to_prev = jnp.concatenate([token_rows[:1].astype(jnp.float32), cos_grad[:1][None]], axis=1)
    from_next = shifted(to_prev, "seq", -1)
    prev_row = shifted(token_rows[token_count - 1 :], "seq", 1)
    next_row = from_next[:, :-1].astype(token_rows.dtype)
    next_cos_grad = from_next[:, -1:]
    rows_ext = jnp.concatenate([token_rows, prev_row, next_row], axis=0)
    rows_perm = permute_cols(rows_ext, index, width)
    queries_ext = jnp.dot(rows_perm, full_query, preferred_element_type=jnp.float32)
    keys_ext = jnp.dot(rows_perm, full_key, preferred_element_type=jnp.float32)
    queries = queries_ext[:token_count]
    key_rows = keys_ext[:token_count]
    query_unit, query_scale = unit_of(queries)
    key_unit, key_scale = unit_of(key_rows)
    key_before, _ = unit_of(keys_ext[token_count : token_count + 1])
    query_next, _ = unit_of(queries_ext[token_count + 1 :])
    key_prior = jnp.concatenate([key_before, key_unit[:-1]], axis=0)
    cosine = jnp.sum(query_unit * key_prior, axis=1)
    boundary_prob = jnp.where(later_rows, 0.5 * (1.0 - cosine), 1.0)
    confidence = jnp.where(starts, boundary_prob, 1.0 - boundary_prob)
    weighted_grad = confidence[:, None] * grad_rows
    slot_grad = lax.dot_general(membership, weighted_grad, contract_first, precision=exact)
    lead_grad = jnp.dot(leading[None, :], weighted_grad, precision=exact)
    back_vector = lead_grad + jnp.dot(keep_all[None, :], slot_grad, precision=exact)
    if lax.axis_size("seq") <= 8:
        grad_in = direct_scan(last_log, back_vector, "seq")
    else:
        grad_in = seq_scan(last_log, back_vector, "seq", False)
    reach_end = jnp.exp(running[slot_count - 1] - running)
    state_grad = (
        lax.dot_general(decay_table, slot_grad, contract_first, precision=exact)
        + reach_end[:, None] * grad_in
    )
    segment_grad = (smoothing[:, None] * state_grad).astype(jnp.bfloat16)
    unit_q_grad = cos_grad[:, None] * key_prior
    prior_grad = cos_grad[:, None] * query_unit
    query_grad = normalize_grad(queries, query_scale, unit_q_grad).astype(jnp.bfloat16)
    unit_k_grad = jnp.concatenate([prior_grad[1:], next_cos_grad * query_next], axis=0)
    key_grad = normalize_grad(key_rows, key_scale, unit_k_grad).astype(jnp.bfloat16)
    x_grad = lax.dot_general(
        query_grad, full_query, contract_last, preferred_element_type=jnp.float32
    )
    x_grad = x_grad + lax.dot_general(
        key_grad, full_key, contract_last, preferred_element_type=jnp.float32
    )
    x_grad = x_grad.astype(jnp.bfloat16)
    slots = jnp.arange(len(index), dtype=jnp.int32)
    order = jnp.sum(jnp.where(jnp.stack(index)[None, :] == slots[:, None], slots[None, :], 0), axis=1)
    x_grad = permute_cols(x_grad, [order[j] for j in range(len(index))], width)
    return (x_grad[None], segment_grad[None])


def solution(mesh):
    placed = (
        P("dp", "seq", None),
        P("dp", "seq", None),
        P("dp", "seq", None),
        P("dp", "seq"),
        P("dp", "seq"),
        P("dp", "seq"),
        P("dp", None),
        P("dp", None),
    )
    return jax.shard_map(
        per_device,
        mesh=mesh,
        in_specs=placed,
        out_specs=(P("dp", "seq", None), P("dp", "seq", None)),
        check_vma=False,
    )
```

```python
import jax
import jax.numpy as jnp
from jax import lax
from jax.sharding import PartitionSpec as P

prob_scale = 65536.0
norm_eps = 1e-06
exact = lax.Precision.HIGHEST
contract_last = (((1,), (1,)), ((), ()))
contract_first = (((0,), (0,)), ((), ()))


def shifted(block, axis, distance):
    devices = range(lax.axis_size(axis))
    route = [(i - distance, i) for i in devices if i - distance in devices]
    return lax.ppermute(block, axis, route)


def normalize_grad(vectors, scales, unit_grad):
    inner_prod = jnp.sum(vectors * unit_grad, axis=-1, keepdims=True)
    return scales * unit_grad - scales * scales * scales * inner_prod * vectors


def seq_scan(log_keep, vectors, axis, from_lower):
    size = lax.axis_size(axis)
    step = 1
    incl_log, incl_vec = log_keep, vectors
    excl_log = jnp.zeros_like(log_keep)
    excl_vec = jnp.zeros_like(vectors)
    while step < size:
        packed = jnp.concatenate([incl_vec, incl_log], axis=-1)
        got = shifted(packed, axis, step if from_lower else -step)
        got_log, got_vec = got[:, -1:], got[:, :-1]
        excl_vec = jnp.exp(excl_log) * got_vec + excl_vec
        excl_log = excl_log + got_log
        if 2 * step < size:
            incl_vec = jnp.exp(incl_log) * got_vec + incl_vec
            incl_log = incl_log + got_log
        step *= 2
    return excl_vec


def gather_blocks(blocks, axis, pair_axis):
    size = lax.axis_size(axis)
    own = lax.axis_index(axis)
    side = lax.axis_index(pair_axis) % 2
    cols = blocks[0].shape[1] // 2
    halves = tuple(lax.dynamic_slice_in_dim(b, side * cols, cols, axis=1) for b in blocks)
    swap_pair = [(i, i ^ 1) for i in range(lax.axis_size(pair_axis))]
    pairs = [blocks]
    index = [own]
    for k in range(1, size // 2):
        route = [(i, (i + 2 * k) % size) for i in range(size)]
        fetched = lax.ppermute(halves, axis, route)
        other = lax.ppermute(fetched, pair_axis, swap_pair)
        whole = tuple(
            jnp.where(side == 0, jnp.concatenate([a, b], axis=1), jnp.concatenate([b, a], axis=1))
            for a, b in zip(fetched, other)
        )
        pairs.append(whole)
        index.append((own - 2 * k) % size)
    swap = [(i, i ^ 1) for i in range(size)]
    partner = lax.ppermute(pairs, axis, swap)
    pairs = pairs + partner
    index = index + [i ^ 1 for i in index]
    return pairs, index


def direct_scan(log_keep, vectors, axis):
    size = lax.axis_size(axis)
    packed = jnp.concatenate([vectors, log_keep], axis=-1)
    total = jnp.zeros_like(vectors)
    gap = jnp.zeros_like(log_keep)
    for step in range(1, size):
        got = shifted(packed, axis, -step)
        total = total + jnp.exp(gap) * got[:, :-1]
        gap = gap + got[:, -1:]
    return total


def permute_cols(rows, index, width):
    return jnp.concatenate(
        [lax.dynamic_slice_in_dim(rows, at * width, width, axis=1) for at in index], axis=1
    )


def unit_of(rows):
    scale = lax.rsqrt(jnp.sum(rows * rows, axis=1, keepdims=True) + norm_eps)
    return rows * scale, scale


def per_device(
    encoder_out,
    out_grad,
    segment_states,
    segment_starts,
    segment_counts,
    segment_probs,
    query_weight,
    key_weight,
):
    token_rows = encoder_out[0]
    grad_rows = out_grad[0]
    token_count = token_rows.shape[0]
    slot_count = segment_states.shape[1]
    width = query_weight.shape[0]
    shard_index = lax.axis_index("seq")
    pairs, index = gather_blocks((query_weight, key_weight), "dp", "seq")
    full_query = jnp.concatenate([p[0] for p in pairs], axis=0)
    full_key = jnp.concatenate([p[1] for p in pairs], axis=0)
    position = jnp.arange(token_count)
    later_rows = (shard_index > 0) | (position > 0)
    segment_total = segment_counts[0, 0]
    slot_index = jnp.arange(slot_count)
    slot_used = slot_index < segment_total
    start_pos = segment_starts[0]
    smoothing = jnp.where(slot_used, segment_probs[0].astype(jnp.float32) / prob_scale, 0.0)
    reached = slot_used[None, :] & (start_pos[None, :] <= position[:, None])
    member_id = jnp.sum(reached.astype(jnp.int32), axis=1) - 1
    membership = (member_id[:, None] == slot_index[None, :]).astype(jnp.float32)
    leading = (member_id < 0).astype(jnp.float32)
    starts = jnp.any(slot_used[None, :] & (start_pos[None, :] == position[:, None]), axis=1)
    running = jnp.cumsum(jnp.log(1.0 - smoothing))
    lower = slot_index[None, :] <= slot_index[:, None]
    decay_table = jnp.where(
        lower, jnp.exp(jnp.where(lower, running[:, None] - running[None, :], 0.0)), 0.0
    )
    weighted_states = smoothing[:, None] * segment_states[0].astype(jnp.float32)
    local_state = jnp.dot(decay_table, weighted_states, precision=exact)
    keep_all = jnp.exp(running)
    last_log = running[slot_count - 1 :][None]
    state_in = seq_scan(last_log, local_state[slot_count - 1 :], "seq", True)
    smoothed = local_state + keep_all[:, None] * state_in
    picked = jnp.dot(membership, smoothed, precision=exact) + leading[:, None] * state_in
    conf_grad = jnp.sum(grad_rows * picked, axis=1)
    cos_grad = jnp.where(later_rows, jnp.where(starts, -0.5 * conf_grad, 0.5 * conf_grad), 0.0)
    to_prev = jnp.concatenate([token_rows[:1].astype(jnp.float32), cos_grad[:1][None]], axis=1)
    from_next = shifted(to_prev, "seq", -1)
    prev_row = shifted(token_rows[token_count - 1 :], "seq", 1)
    next_row = from_next[:, :-1].astype(token_rows.dtype)
    next_cos_grad = from_next[:, -1:]
    rows_ext = jnp.concatenate([token_rows, prev_row, next_row], axis=0)
    rows_perm = permute_cols(rows_ext, index, width)
    queries_ext = jnp.dot(rows_perm, full_query, preferred_element_type=jnp.float32)
    keys_ext = jnp.dot(rows_perm, full_key, preferred_element_type=jnp.float32)
    queries = queries_ext[:token_count]
    key_rows = keys_ext[:token_count]
    query_unit, query_scale = unit_of(queries)
    key_unit, key_scale = unit_of(key_rows)
    key_before, _ = unit_of(keys_ext[token_count : token_count + 1])
    query_next, _ = unit_of(queries_ext[token_count + 1 :])
    key_prior = jnp.concatenate([key_before, key_unit[:-1]], axis=0)
    cosine = jnp.sum(query_unit * key_prior, axis=1)
    boundary_prob = jnp.where(later_rows, 0.5 * (1.0 - cosine), 1.0)
    confidence = jnp.where(starts, boundary_prob, 1.0 - boundary_prob)
    weighted_grad = confidence[:, None] * grad_rows
    slot_grad = lax.dot_general(membership, weighted_grad, contract_first, precision=exact)
    lead_grad = jnp.dot(leading[None, :], weighted_grad, precision=exact)
    back_vector = lead_grad + jnp.dot(keep_all[None, :], slot_grad, precision=exact)
    if lax.axis_size("seq") <= 8:
        grad_in = direct_scan(last_log, back_vector, "seq")
    else:
        grad_in = seq_scan(last_log, back_vector, "seq", False)
    reach_end = jnp.exp(running[slot_count - 1] - running)
    state_grad = (
        lax.dot_general(decay_table, slot_grad, contract_first, precision=exact)
        + reach_end[:, None] * grad_in
    )
    segment_grad = (smoothing[:, None] * state_grad).astype(jnp.bfloat16)
    unit_q_grad = cos_grad[:, None] * key_prior
    prior_grad = cos_grad[:, None] * query_unit
    query_grad = normalize_grad(queries, query_scale, unit_q_grad).astype(jnp.bfloat16)
    unit_k_grad = jnp.concatenate([prior_grad[1:], next_cos_grad * query_next], axis=0)
    key_grad = normalize_grad(key_rows, key_scale, unit_k_grad).astype(jnp.bfloat16)
    x_grad = lax.dot_general(
        query_grad, full_query, contract_last, preferred_element_type=jnp.float32
    )
    x_grad = x_grad + lax.dot_general(
        key_grad, full_key, contract_last, preferred_element_type=jnp.float32
    )
    x_grad = x_grad.astype(jnp.bfloat16)
    slots = jnp.arange(len(index), dtype=jnp.int32)
    order = jnp.sum(jnp.where(jnp.stack(index)[None, :] == slots[:, None], slots[None, :], 0), axis=1)
    x_grad = permute_cols(x_grad, [order[j] for j in range(len(index))], width)
    return (x_grad[None], segment_grad[None])


def solution(mesh):
    placed = (
        P("dp", "seq", None),
        P("dp", "seq", None),
        P("dp", "seq", None),
        P("dp", "seq"),
        P("dp", "seq"),
        P("dp", "seq"),
        P("dp", None),
        P("dp", None),
    )
    return jax.shard_map(
        per_device,
        mesh=mesh,
        in_specs=placed,
        out_specs=(P("dp", "seq", None), P("dp", "seq", None)),
        check_vma=False,
    )
```

```python
import jax
import jax.numpy as jnp
from jax import lax
from jax.sharding import PartitionSpec as P

prob_scale = 65536.0
norm_eps = 1e-06
exact = lax.Precision.HIGHEST
contract_last = (((1,), (1,)), ((), ()))
contract_first = (((0,), (0,)), ((), ()))


def shifted(block, axis, distance):
    devices = range(lax.axis_size(axis))
    route = [(i - distance, i) for i in devices if i - distance in devices]
    return lax.ppermute(block, axis, route)


def normalize_grad(vectors, scales, unit_grad):
    inner_prod = jnp.sum(vectors * unit_grad, axis=-1, keepdims=True)
    return scales * unit_grad - scales * scales * scales * inner_prod * vectors


def seq_scan(log_keep, vectors, axis, from_lower):
    size = lax.axis_size(axis)
    step = 1
    incl_log, incl_vec = log_keep, vectors
    excl_log = jnp.zeros_like(log_keep)
    excl_vec = jnp.zeros_like(vectors)
    while step < size:
        packed = jnp.concatenate([incl_vec, incl_log], axis=-1)
        got = shifted(packed, axis, step if from_lower else -step)
        got_log, got_vec = got[:, -1:], got[:, :-1]
        excl_vec = jnp.exp(excl_log) * got_vec + excl_vec
        excl_log = excl_log + got_log
        if 2 * step < size:
            incl_vec = jnp.exp(incl_log) * got_vec + incl_vec
            incl_log = incl_log + got_log
        step *= 2
    return excl_vec


def gather_blocks(blocks, axis):
    size = lax.axis_size(axis)
    own = lax.axis_index(axis)
    pairs = [blocks]
    index = [own]
    for k in range(1, size // 2):
        route = [(i, (i + 2 * k) % size) for i in range(size)]
        pairs.append(lax.ppermute(blocks, axis, route))
        index.append((own - 2 * k) % size)
    swap = [(i, i ^ 1) for i in range(size)]
    partner = lax.ppermute(pairs, axis, swap)
    pairs = pairs + partner
    index = index + [i ^ 1 for i in index]
    return pairs, index


def direct_scan(log_keep, vectors, axis):
    size = lax.axis_size(axis)
    packed = jnp.concatenate([vectors, log_keep], axis=-1)
    total = jnp.zeros_like(vectors)
    gap = jnp.zeros_like(log_keep)
    for step in range(1, size):
        got = shifted(packed, axis, -step)
        total = total + jnp.exp(gap) * got[:, :-1]
        gap = gap + got[:, -1:]
    return total


def permute_cols(rows, index, width):
    return jnp.concatenate(
        [lax.dynamic_slice_in_dim(rows, at * width, width, axis=1) for at in index], axis=1
    )


def unit_of(rows):
    scale = lax.rsqrt(jnp.sum(rows * rows, axis=1, keepdims=True) + norm_eps)
    return rows * scale, scale


def per_device(
    encoder_out,
    out_grad,
    segment_states,
    segment_starts,
    segment_counts,
    segment_probs,
    query_weight,
    key_weight,
):
    token_rows = encoder_out[0]
    grad_rows = out_grad[0]
    token_count = token_rows.shape[0]
    slot_count = segment_states.shape[1]
    width = query_weight.shape[0]
    shard_index = lax.axis_index("seq")
    seq_count = lax.axis_size("seq")
    piece = width // seq_count
    full_query, full_key = (
        lax.all_gather(
            lax.dynamic_slice_in_dim(w, shard_index * piece, piece, axis=0), ("dp", "seq"), axis=0, tiled=True
        )
        for w in (query_weight, key_weight)
    )
    position = jnp.arange(token_count)
    later_rows = (shard_index > 0) | (position > 0)
    segment_total = segment_counts[0, 0]
    slot_index = jnp.arange(slot_count)
    slot_used = slot_index < segment_total
    start_pos = segment_starts[0]
    smoothing = jnp.where(slot_used, segment_probs[0].astype(jnp.float32) / prob_scale, 0.0)
    reached = slot_used[None, :] & (start_pos[None, :] <= position[:, None])
    member_id = jnp.sum(reached.astype(jnp.int32), axis=1) - 1
    membership = (member_id[:, None] == slot_index[None, :]).astype(jnp.float32)
    leading = (member_id < 0).astype(jnp.float32)
    starts = jnp.any(slot_used[None, :] & (start_pos[None, :] == position[:, None]), axis=1)
    running = jnp.cumsum(jnp.log(1.0 - smoothing))
    lower = slot_index[None, :] <= slot_index[:, None]
    decay_table = jnp.where(
        lower, jnp.exp(jnp.where(lower, running[:, None] - running[None, :], 0.0)), 0.0
    )
    weighted_states = smoothing[:, None] * segment_states[0].astype(jnp.float32)
    local_state = jnp.dot(decay_table, weighted_states, precision=exact)
    keep_all = jnp.exp(running)
    last_log = running[slot_count - 1 :][None]
    state_in = seq_scan(last_log, local_state[slot_count - 1 :], "seq", True)
    smoothed = local_state + keep_all[:, None] * state_in
    picked = jnp.dot(membership, smoothed, precision=exact) + leading[:, None] * state_in
    conf_grad = jnp.sum(grad_rows * picked, axis=1)
    cos_grad = jnp.where(later_rows, jnp.where(starts, -0.5 * conf_grad, 0.5 * conf_grad), 0.0)
    to_prev = jnp.concatenate([token_rows[:1].astype(jnp.float32), cos_grad[:1][None]], axis=1)
    from_next = shifted(to_prev, "seq", -1)
    prev_row = shifted(token_rows[token_count - 1 :], "seq", 1)
    next_row = from_next[:, :-1].astype(token_rows.dtype)
    next_cos_grad = from_next[:, -1:]
    rows_ext = jnp.concatenate([token_rows, prev_row, next_row], axis=0)
    rows_perm = rows_ext
    queries_ext = jnp.dot(rows_perm, full_query, preferred_element_type=jnp.float32)
    keys_ext = jnp.dot(rows_perm, full_key, preferred_element_type=jnp.float32)
    queries = queries_ext[:token_count]
    key_rows = keys_ext[:token_count]
    query_unit, query_scale = unit_of(queries)
    key_unit, key_scale = unit_of(key_rows)
    key_before, _ = unit_of(keys_ext[token_count : token_count + 1])
    query_next, _ = unit_of(queries_ext[token_count + 1 :])
    key_prior = jnp.concatenate([key_before, key_unit[:-1]], axis=0)
    cosine = jnp.sum(query_unit * key_prior, axis=1)
    boundary_prob = jnp.where(later_rows, 0.5 * (1.0 - cosine), 1.0)
    confidence = jnp.where(starts, boundary_prob, 1.0 - boundary_prob)
    weighted_grad = confidence[:, None] * grad_rows
    slot_grad = lax.dot_general(membership, weighted_grad, contract_first, precision=exact)
    lead_grad = jnp.dot(leading[None, :], weighted_grad, precision=exact)
    back_vector = lead_grad + jnp.dot(keep_all[None, :], slot_grad, precision=exact)
    if lax.axis_size("seq") <= 8:
        grad_in = direct_scan(last_log, back_vector, "seq")
    else:
        grad_in = seq_scan(last_log, back_vector, "seq", False)
    reach_end = jnp.exp(running[slot_count - 1] - running)
    state_grad = (
        lax.dot_general(decay_table, slot_grad, contract_first, precision=exact)
        + reach_end[:, None] * grad_in
    )
    segment_grad = (smoothing[:, None] * state_grad).astype(jnp.bfloat16)
    unit_q_grad = cos_grad[:, None] * key_prior
    prior_grad = cos_grad[:, None] * query_unit
    query_grad = normalize_grad(queries, query_scale, unit_q_grad).astype(jnp.bfloat16)
    unit_k_grad = jnp.concatenate([prior_grad[1:], next_cos_grad * query_next], axis=0)
    key_grad = normalize_grad(key_rows, key_scale, unit_k_grad).astype(jnp.bfloat16)
    x_grad = lax.dot_general(
        query_grad, full_query, contract_last, preferred_element_type=jnp.float32
    )
    x_grad = x_grad + lax.dot_general(
        key_grad, full_key, contract_last, preferred_element_type=jnp.float32
    )
    x_grad = x_grad.astype(jnp.bfloat16)
    return (x_grad[None], segment_grad[None])


def solution(mesh):
    placed = (
        P("dp", "seq", None),
        P("dp", "seq", None),
        P("dp", "seq", None),
        P("dp", "seq"),
        P("dp", "seq"),
        P("dp", "seq"),
        P("dp", None),
        P("dp", None),
    )
    return jax.shard_map(
        per_device,
        mesh=mesh,
        in_specs=placed,
        out_specs=(P("dp", "seq", None), P("dp", "seq", None)),
        check_vma=False,
    )
```

```python
import jax
import jax.numpy as jnp
from jax import lax
from jax.sharding import PartitionSpec as P

prob_scale = 65536.0
norm_eps = 1e-06
exact = lax.Precision.HIGHEST
contract_last = (((1,), (1,)), ((), ()))
contract_first = (((0,), (0,)), ((), ()))


def shifted(block, axis, distance):
    devices = range(lax.axis_size(axis))
    route = [(i - distance, i) for i in devices if i - distance in devices]
    return lax.ppermute(block, axis, route)


def normalize_grad(vectors, scales, unit_grad):
    inner_prod = jnp.sum(vectors * unit_grad, axis=-1, keepdims=True)
    return scales * unit_grad - scales * scales * scales * inner_prod * vectors


def seq_scan(log_keep, vectors, axis, from_lower):
    size = lax.axis_size(axis)
    step = 1
    incl_log, incl_vec = log_keep, vectors
    excl_log = jnp.zeros_like(log_keep)
    excl_vec = jnp.zeros_like(vectors)
    while step < size:
        packed = jnp.concatenate([incl_vec, incl_log], axis=-1)
        got = shifted(packed, axis, step if from_lower else -step)
        got_log, got_vec = got[:, -1:], got[:, :-1]
        excl_vec = jnp.exp(excl_log) * got_vec + excl_vec
        excl_log = excl_log + got_log
        if 2 * step < size:
            incl_vec = jnp.exp(incl_log) * got_vec + incl_vec
            incl_log = incl_log + got_log
        step *= 2
    return excl_vec


def gather_blocks(blocks, axis):
    size = lax.axis_size(axis)
    own = lax.axis_index(axis)
    pairs = [blocks]
    index = [own]
    for k in range(1, size // 2):
        route = [(i, (i + 2 * k) % size) for i in range(size)]
        pairs.append(lax.ppermute(blocks, axis, route))
        index.append((own - 2 * k) % size)
    swap = [(i, i ^ 1) for i in range(size)]
    partner = lax.ppermute(pairs, axis, swap)
    pairs = pairs + partner
    index = index + [i ^ 1 for i in index]
    return pairs, index


def direct_scan(log_keep, vectors, axis):
    size = lax.axis_size(axis)
    packed = jnp.concatenate([vectors, log_keep], axis=-1)
    total = jnp.zeros_like(vectors)
    gap = jnp.zeros_like(log_keep)
    for step in range(1, size):
        got = shifted(packed, axis, -step)
        total = total + jnp.exp(gap) * got[:, :-1]
        gap = gap + got[:, -1:]
    return total


def split_dot(rows, blocks, index, width):
    total = None
    for block, at in zip(blocks, index):
        part = lax.dynamic_slice_in_dim(rows, at * width, width, axis=1)
        term = jnp.dot(part, block, preferred_element_type=jnp.float32)
        total = term if total is None else total + term
    return total


def permute_cols(rows, index, width):
    return jnp.concatenate(
        [lax.dynamic_slice_in_dim(rows, at * width, width, axis=1) for at in index], axis=1
    )


def unit_of(rows):
    scale = lax.rsqrt(jnp.sum(rows * rows, axis=1, keepdims=True) + norm_eps)
    return rows * scale, scale


def per_device(
    encoder_out,
    out_grad,
    segment_states,
    segment_starts,
    segment_counts,
    segment_probs,
    query_weight,
    key_weight,
):
    token_rows = encoder_out[0]
    grad_rows = out_grad[0]
    token_count = token_rows.shape[0]
    slot_count = segment_states.shape[1]
    width = query_weight.shape[0]
    shard_index = lax.axis_index("seq")
    pairs, index = gather_blocks((query_weight, key_weight), "dp")
    query_blocks = [p[0] for p in pairs]
    key_blocks = [p[1] for p in pairs]
    position = jnp.arange(token_count)
    later_rows = (shard_index > 0) | (position > 0)
    segment_total = segment_counts[0, 0]
    slot_index = jnp.arange(slot_count)
    slot_used = slot_index < segment_total
    start_pos = segment_starts[0]
    smoothing = jnp.where(slot_used, segment_probs[0].astype(jnp.float32) / prob_scale, 0.0)
    reached = slot_used[None, :] & (start_pos[None, :] <= position[:, None])
    member_id = jnp.sum(reached.astype(jnp.int32), axis=1) - 1
    membership = (member_id[:, None] == slot_index[None, :]).astype(jnp.float32)
    leading = (member_id < 0).astype(jnp.float32)
    starts = jnp.any(slot_used[None, :] & (start_pos[None, :] == position[:, None]), axis=1)
    running = jnp.cumsum(jnp.log(1.0 - smoothing))
    lower = slot_index[None, :] <= slot_index[:, None]
    decay_table = jnp.where(
        lower, jnp.exp(jnp.where(lower, running[:, None] - running[None, :], 0.0)), 0.0
    )
    weighted_states = smoothing[:, None] * segment_states[0].astype(jnp.float32)
    local_state = jnp.dot(decay_table, weighted_states, precision=exact)
    keep_all = jnp.exp(running)
    last_log = running[slot_count - 1 :][None]
    state_in = seq_scan(last_log, local_state[slot_count - 1 :], "seq", True)
    smoothed = local_state + keep_all[:, None] * state_in
    picked = jnp.dot(membership, smoothed, precision=exact) + leading[:, None] * state_in
    conf_grad = jnp.sum(grad_rows * picked, axis=1)
    cos_grad = jnp.where(later_rows, jnp.where(starts, -0.5 * conf_grad, 0.5 * conf_grad), 0.0)
    to_prev = jnp.concatenate([token_rows[:1].astype(jnp.float32), cos_grad[:1][None]], axis=1)
    from_next = shifted(to_prev, "seq", -1)
    prev_row = shifted(token_rows[token_count - 1 :], "seq", 1)
    next_row = from_next[:, :-1].astype(token_rows.dtype)
    next_cos_grad = from_next[:, -1:]
    rows_ext = jnp.concatenate([token_rows, prev_row, next_row], axis=0)
    queries_ext = split_dot(rows_ext, query_blocks, index, width)
    keys_ext = split_dot(rows_ext, key_blocks, index, width)
    queries = queries_ext[:token_count]
    key_rows = keys_ext[:token_count]
    query_unit, query_scale = unit_of(queries)
    key_unit, key_scale = unit_of(key_rows)
    key_before, _ = unit_of(keys_ext[token_count : token_count + 1])
    query_next, _ = unit_of(queries_ext[token_count + 1 :])
    key_prior = jnp.concatenate([key_before, key_unit[:-1]], axis=0)
    cosine = jnp.sum(query_unit * key_prior, axis=1)
    boundary_prob = jnp.where(later_rows, 0.5 * (1.0 - cosine), 1.0)
    confidence = jnp.where(starts, boundary_prob, 1.0 - boundary_prob)
    weighted_grad = confidence[:, None] * grad_rows
    slot_grad = lax.dot_general(membership, weighted_grad, contract_first, precision=exact)
    lead_grad = jnp.dot(leading[None, :], weighted_grad, precision=exact)
    back_vector = lead_grad + jnp.dot(keep_all[None, :], slot_grad, precision=exact)
    if lax.axis_size("seq") <= 8:
        grad_in = direct_scan(last_log, back_vector, "seq")
    else:
        grad_in = seq_scan(last_log, back_vector, "seq", False)
    reach_end = jnp.exp(running[slot_count - 1] - running)
    state_grad = (
        lax.dot_general(decay_table, slot_grad, contract_first, precision=exact)
        + reach_end[:, None] * grad_in
    )
    segment_grad = (smoothing[:, None] * state_grad).astype(jnp.bfloat16)
    unit_q_grad = cos_grad[:, None] * key_prior
    prior_grad = cos_grad[:, None] * query_unit
    query_grad = normalize_grad(queries, query_scale, unit_q_grad).astype(jnp.bfloat16)
    unit_k_grad = jnp.concatenate([prior_grad[1:], next_cos_grad * query_next], axis=0)
    key_grad = normalize_grad(key_rows, key_scale, unit_k_grad).astype(jnp.bfloat16)
    parts = []
    for q_block, k_block in zip(query_blocks, key_blocks):
        part = lax.dot_general(query_grad, q_block, contract_last, preferred_element_type=jnp.float32)
        part = part + lax.dot_general(key_grad, k_block, contract_last, preferred_element_type=jnp.float32)
        parts.append(part.astype(jnp.bfloat16))
    x_grad = jnp.concatenate(parts, axis=1)
    slots = jnp.arange(len(index), dtype=jnp.int32)
    order = jnp.sum(jnp.where(jnp.stack(index)[None, :] == slots[:, None], slots[None, :], 0), axis=1)
    x_grad = permute_cols(x_grad, [order[j] for j in range(len(index))], width)
    return (x_grad[None], segment_grad[None])


def solution(mesh):
    placed = (
        P("dp", "seq", None),
        P("dp", "seq", None),
        P("dp", "seq", None),
        P("dp", "seq"),
        P("dp", "seq"),
        P("dp", "seq"),
        P("dp", None),
        P("dp", None),
    )
    return jax.shard_map(
        per_device,
        mesh=mesh,
        in_specs=placed,
        out_specs=(P("dp", "seq", None), P("dp", "seq", None)),
        check_vma=False,
    )
```

```python
import jax
import jax.numpy as jnp
from jax import lax
from jax.sharding import PartitionSpec as P

prob_scale = 65536.0
norm_eps = 1e-06
exact = lax.Precision.HIGHEST
contract_last = (((1,), (1,)), ((), ()))
contract_first = (((0,), (0,)), ((), ()))


def shifted(block, axis, distance):
    devices = range(lax.axis_size(axis))
    route = [(i - distance, i) for i in devices if i - distance in devices]
    return lax.ppermute(block, axis, route)


def normalize_grad(vectors, scales, unit_grad):
    inner_prod = jnp.sum(vectors * unit_grad, axis=-1, keepdims=True)
    return scales * unit_grad - scales * scales * scales * inner_prod * vectors


def seq_scan(log_keep, vectors, axis, from_lower):
    size = lax.axis_size(axis)
    step = 1
    incl_log, incl_vec = log_keep, vectors
    excl_log = jnp.zeros_like(log_keep)
    excl_vec = jnp.zeros_like(vectors)
    while step < size:
        packed = jnp.concatenate([incl_vec, incl_log], axis=-1)
        got = shifted(packed, axis, step if from_lower else -step)
        got_log, got_vec = got[:, -1:], got[:, :-1]
        excl_vec = jnp.exp(excl_log) * got_vec + excl_vec
        excl_log = excl_log + got_log
        if 2 * step < size:
            incl_vec = jnp.exp(incl_log) * got_vec + incl_vec
            incl_log = incl_log + got_log
        step *= 2
    return excl_vec


def gather_blocks(blocks, axis):
    size = lax.axis_size(axis)
    own = lax.axis_index(axis)
    pairs = [blocks]
    index = [own]
    for k in range(1, size // 2):
        route = [(i, (i + 2 * k) % size) for i in range(size)]
        pairs.append(lax.ppermute(blocks, axis, route))
        index.append((own - 2 * k) % size)
    swap = [(i, i ^ 1) for i in range(size)]
    partner = lax.ppermute(pairs, axis, swap)
    pairs = pairs + partner
    index = index + [i ^ 1 for i in index]
    return pairs, index


def direct_scan(log_keep, vectors, axis):
    size = lax.axis_size(axis)
    packed = jnp.concatenate([vectors, log_keep], axis=-1)
    total = jnp.zeros_like(vectors)
    gap = jnp.zeros_like(log_keep)
    for step in range(1, size):
        got = shifted(packed, axis, -step)
        total = total + jnp.exp(gap) * got[:, :-1]
        gap = gap + got[:, -1:]
    return total


def split_dot(rows, blocks, index, width):
    total = None
    for block, at in zip(blocks, index):
        part = lax.dynamic_slice_in_dim(rows, at * width, width, axis=1)
        term = jnp.dot(part, block, preferred_element_type=jnp.float32)
        total = term if total is None else total + term
    return total


def permute_cols(rows, index, width):
    return jnp.concatenate(
        [lax.dynamic_slice_in_dim(rows, at * width, width, axis=1) for at in index], axis=1
    )


def unit_of(rows):
    scale = lax.rsqrt(jnp.sum(rows * rows, axis=1, keepdims=True) + norm_eps)
    return rows * scale, scale


def per_device(
    encoder_out,
    out_grad,
    segment_states,
    segment_starts,
    segment_counts,
    segment_probs,
    query_weight,
    key_weight,
):
    token_rows = encoder_out[0]
    grad_rows = out_grad[0]
    token_count = token_rows.shape[0]
    slot_count = segment_states.shape[1]
    width = query_weight.shape[0]
    shard_index = lax.axis_index("seq")
    pairs, index = gather_blocks((query_weight, key_weight), "dp")
    query_blocks = [p[0] for p in pairs]
    key_blocks = [p[1] for p in pairs]
    position = jnp.arange(token_count)
    later_rows = (shard_index > 0) | (position > 0)
    segment_total = segment_counts[0, 0]
    slot_index = jnp.arange(slot_count)
    slot_used = slot_index < segment_total
    start_pos = segment_starts[0]
    smoothing = jnp.where(slot_used, segment_probs[0].astype(jnp.float32) / prob_scale, 0.0)
    reached = slot_used[None, :] & (start_pos[None, :] <= position[:, None])
    member_id = jnp.sum(reached.astype(jnp.int32), axis=1) - 1
    membership = (member_id[:, None] == slot_index[None, :]).astype(jnp.float32)
    leading = (member_id < 0).astype(jnp.float32)
    starts = jnp.any(slot_used[None, :] & (start_pos[None, :] == position[:, None]), axis=1)
    running = jnp.cumsum(jnp.log(1.0 - smoothing))
    lower = slot_index[None, :] <= slot_index[:, None]
    decay_table = jnp.where(
        lower, jnp.exp(jnp.where(lower, running[:, None] - running[None, :], 0.0)), 0.0
    )
    weighted_states = smoothing[:, None] * segment_states[0].astype(jnp.float32)
    local_state = jnp.dot(decay_table, weighted_states, precision=exact)
    keep_all = jnp.exp(running)
    last_log = running[slot_count - 1 :][None]
    state_in = seq_scan(last_log, local_state[slot_count - 1 :], "seq", True)
    smoothed = local_state + keep_all[:, None] * state_in
    picked = jnp.dot(membership, smoothed, precision=exact) + leading[:, None] * state_in
    conf_grad = jnp.sum(grad_rows * picked, axis=1)
    cos_grad = jnp.where(later_rows, jnp.where(starts, -0.5 * conf_grad, 0.5 * conf_grad), 0.0)
    to_prev = jnp.concatenate([token_rows[:1].astype(jnp.float32), cos_grad[:1][None]], axis=1)
    from_next = shifted(to_prev, "seq", -1)
    prev_row = shifted(token_rows[token_count - 1 :], "seq", 1)
    next_row = from_next[:, :-1].astype(token_rows.dtype)
    next_cos_grad = from_next[:, -1:]
    rows_ext = jnp.concatenate([token_rows, prev_row, next_row], axis=0)
    queries_ext = split_dot(rows_ext, query_blocks, index, width)
    keys_ext = split_dot(rows_ext, key_blocks, index, width)
    queries = queries_ext[:token_count]
    key_rows = keys_ext[:token_count]
    query_unit, query_scale = unit_of(queries)
    key_unit, key_scale = unit_of(key_rows)
    key_before, _ = unit_of(keys_ext[token_count : token_count + 1])
    query_next, _ = unit_of(queries_ext[token_count + 1 :])
    key_prior = jnp.concatenate([key_before, key_unit[:-1]], axis=0)
    cosine = jnp.sum(query_unit * key_prior, axis=1)
    boundary_prob = jnp.where(later_rows, 0.5 * (1.0 - cosine), 1.0)
    confidence = jnp.where(starts, boundary_prob, 1.0 - boundary_prob)
    weighted_grad = confidence[:, None] * grad_rows
    slot_grad = lax.dot_general(membership, weighted_grad, contract_first, precision=exact)
    lead_grad = jnp.dot(leading[None, :], weighted_grad, precision=exact)
    back_vector = lead_grad + jnp.dot(keep_all[None, :], slot_grad, precision=exact)
    grad_in = seq_scan(last_log, back_vector, "seq", False)
    reach_end = jnp.exp(running[slot_count - 1] - running)
    state_grad = (
        lax.dot_general(decay_table, slot_grad, contract_first, precision=exact)
        + reach_end[:, None] * grad_in
    )
    segment_grad = (smoothing[:, None] * state_grad).astype(jnp.bfloat16)
    unit_q_grad = cos_grad[:, None] * key_prior
    prior_grad = cos_grad[:, None] * query_unit
    query_grad = normalize_grad(queries, query_scale, unit_q_grad).astype(jnp.bfloat16)
    unit_k_grad = jnp.concatenate([prior_grad[1:], next_cos_grad * query_next], axis=0)
    key_grad = normalize_grad(key_rows, key_scale, unit_k_grad).astype(jnp.bfloat16)
    parts = []
    for q_block, k_block in zip(query_blocks, key_blocks):
        part = lax.dot_general(query_grad, q_block, contract_last, preferred_element_type=jnp.float32)
        part = part + lax.dot_general(key_grad, k_block, contract_last, preferred_element_type=jnp.float32)
        parts.append(part.astype(jnp.bfloat16))
    x_grad = jnp.concatenate(parts, axis=1)
    slots = jnp.arange(len(index), dtype=jnp.int32)
    order = jnp.sum(jnp.where(jnp.stack(index)[None, :] == slots[:, None], slots[None, :], 0), axis=1)
    x_grad = permute_cols(x_grad, [order[j] for j in range(len(index))], width)
    return (x_grad[None], segment_grad[None])


def solution(mesh):
    placed = (
        P("dp", "seq", None),
        P("dp", "seq", None),
        P("dp", "seq", None),
        P("dp", "seq"),
        P("dp", "seq"),
        P("dp", "seq"),
        P("dp", None),
        P("dp", None),
    )
    return jax.shard_map(
        per_device,
        mesh=mesh,
        in_specs=placed,
        out_specs=(P("dp", "seq", None), P("dp", "seq", None)),
        check_vma=False,
    )
```

```python
import jax
import jax.numpy as jnp
from jax import lax
from jax.sharding import PartitionSpec as P

prob_scale = 65536.0
norm_eps = 1e-06
exact = lax.Precision.HIGHEST
contract_last = (((1,), (1,)), ((), ()))
contract_first = (((0,), (0,)), ((), ()))


def shifted(block, axis, distance):
    devices = range(lax.axis_size(axis))
    route = [(i - distance, i) for i in devices if i - distance in devices]
    return lax.ppermute(block, axis, route)


def normalize_grad(vectors, scales, unit_grad):
    inner_prod = jnp.sum(vectors * unit_grad, axis=-1, keepdims=True)
    return scales * unit_grad - scales * scales * scales * inner_prod * vectors


def seq_scan(log_keep, vectors, axis, from_lower):
    size = lax.axis_size(axis)
    step = 1
    incl_log, incl_vec = log_keep, vectors
    excl_log = jnp.zeros_like(log_keep)
    excl_vec = jnp.zeros_like(vectors)
    while step < size:
        packed = jnp.concatenate([incl_vec, incl_log], axis=-1)
        got = shifted(packed, axis, step if from_lower else -step)
        got_log, got_vec = got[:, -1:], got[:, :-1]
        excl_vec = jnp.exp(excl_log) * got_vec + excl_vec
        excl_log = excl_log + got_log
        if 2 * step < size:
            incl_vec = jnp.exp(incl_log) * got_vec + incl_vec
            incl_log = incl_log + got_log
        step *= 2
    return excl_vec


def gather_blocks(blocks, axis):
    size = lax.axis_size(axis)
    own = lax.axis_index(axis)
    pairs = [blocks]
    index = [own]
    for k in range(1, size // 2):
        route = [(i, (i + 2 * k) % size) for i in range(size)]
        pairs.append(lax.ppermute(blocks, axis, route))
        index.append((own - 2 * k) % size)
    swap = [(i, i ^ 1) for i in range(size)]
    partner = lax.ppermute(pairs, axis, swap)
    pairs = pairs + partner
    index = index + [i ^ 1 for i in index]
    return pairs, index


def direct_scan(log_keep, vectors, axis):
    size = lax.axis_size(axis)
    packed = jnp.concatenate([vectors, log_keep], axis=-1)
    total = jnp.zeros_like(vectors)
    gap = jnp.zeros_like(log_keep)
    for step in range(1, size):
        got = shifted(packed, axis, -step)
        total = total + jnp.exp(gap) * got[:, :-1]
        gap = gap + got[:, -1:]
    return total


def split_dot(rows, blocks, index, width):
    total = None
    for block, at in zip(blocks, index):
        part = lax.dynamic_slice_in_dim(rows, at * width, width, axis=1)
        term = jnp.dot(part, block, preferred_element_type=jnp.float32)
        total = term if total is None else total + term
    return total


def permute_cols(rows, index, width):
    return jnp.concatenate(
        [lax.dynamic_slice_in_dim(rows, at * width, width, axis=1) for at in index], axis=1
    )


def unit_of(rows):
    scale = lax.rsqrt(jnp.sum(rows * rows, axis=1, keepdims=True) + norm_eps)
    return rows * scale, scale


def per_device(
    encoder_out,
    out_grad,
    segment_states,
    segment_starts,
    segment_counts,
    segment_probs,
    query_weight,
    key_weight,
):
    token_rows = encoder_out[0]
    grad_rows = out_grad[0]
    token_count = token_rows.shape[0]
    slot_count = segment_states.shape[1]
    width = query_weight.shape[0]
    shard_index = lax.axis_index("seq")
    pairs, index = gather_blocks((query_weight, key_weight), "dp")
    query_blocks = [p[0] for p in pairs]
    key_blocks = [p[1] for p in pairs]
    position = jnp.arange(token_count)
    later_rows = (shard_index > 0) | (position > 0)
    segment_total = segment_counts[0, 0]
    slot_index = jnp.arange(slot_count)
    slot_used = slot_index < segment_total
    start_pos = segment_starts[0]
    smoothing = jnp.where(slot_used, segment_probs[0].astype(jnp.float32) / prob_scale, 0.0)
    reached = slot_used[None, :] & (start_pos[None, :] <= position[:, None])
    member_id = jnp.sum(reached.astype(jnp.int32), axis=1) - 1
    membership = (member_id[:, None] == slot_index[None, :]).astype(jnp.float32)
    leading = (member_id < 0).astype(jnp.float32)
    starts = jnp.any(slot_used[None, :] & (start_pos[None, :] == position[:, None]), axis=1)
    running = jnp.cumsum(jnp.log(1.0 - smoothing))
    lower = slot_index[None, :] <= slot_index[:, None]
    decay_table = jnp.where(
        lower, jnp.exp(jnp.where(lower, running[:, None] - running[None, :], 0.0)), 0.0
    )
    weighted_states = smoothing[:, None] * segment_states[0].astype(jnp.float32)
    local_state = jnp.dot(decay_table, weighted_states, precision=exact)
    keep_all = jnp.exp(running)
    last_log = running[slot_count - 1 :][None]
    state_in = seq_scan(last_log, local_state[slot_count - 1 :], "seq", True)
    smoothed = local_state + keep_all[:, None] * state_in
    picked = jnp.dot(membership, smoothed, precision=exact) + leading[:, None] * state_in
    conf_grad = jnp.sum(grad_rows * picked, axis=1)
    cos_grad = jnp.where(later_rows, jnp.where(starts, -0.5 * conf_grad, 0.5 * conf_grad), 0.0)
    owner_keep = jnp.where(member_id >= 0, keep_all[jnp.maximum(member_id, 0)], 1.0)
    level = jnp.where(later_rows, 0.5, jnp.where(starts, 1.0, 0.0))
    rise = jnp.where(later_rows, jnp.where(starts, -0.5, 0.5), 0.0)
    grad_wide = grad_rows.astype(jnp.float32)
    base_vector = jnp.dot((owner_keep * level)[None, :], grad_wide, precision=exact)
    to_prev = jnp.concatenate([token_rows[:1].astype(jnp.float32), cos_grad[:1][None]], axis=1)
    from_next = shifted(to_prev, "seq", -1)
    prev_row = shifted(token_rows[token_count - 1 :], "seq", 1)
    next_row = from_next[:, :-1].astype(token_rows.dtype)
    next_cos_grad = from_next[:, -1:]
    rows_ext = jnp.concatenate([token_rows, prev_row, next_row], axis=0)
    queries_ext = split_dot(rows_ext, query_blocks, index, width)
    keys_ext = split_dot(rows_ext, key_blocks, index, width)
    queries = queries_ext[:token_count]
    key_rows = keys_ext[:token_count]
    query_unit, query_scale = unit_of(queries)
    key_unit, key_scale = unit_of(key_rows)
    key_before, _ = unit_of(keys_ext[token_count : token_count + 1])
    query_next, _ = unit_of(queries_ext[token_count + 1 :])
    key_prior = jnp.concatenate([key_before, key_unit[:-1]], axis=0)
    cosine = jnp.sum(query_unit * key_prior, axis=1)
    boundary_prob = jnp.where(later_rows, 0.5 * (1.0 - cosine), 1.0)
    confidence = jnp.where(starts, boundary_prob, 1.0 - boundary_prob)
    weighted_grad = confidence[:, None] * grad_rows
    slot_grad = lax.dot_general(membership, weighted_grad, contract_first, precision=exact)
    back_vector = base_vector + jnp.dot(
        (owner_keep * rise * cosine)[None, :], grad_wide, precision=exact
    )
    grad_in = seq_scan(last_log, back_vector, "seq", False)
    reach_end = jnp.exp(running[slot_count - 1] - running)
    state_grad = (
        lax.dot_general(decay_table, slot_grad, contract_first, precision=exact)
        + reach_end[:, None] * grad_in
    )
    segment_grad = (smoothing[:, None] * state_grad).astype(jnp.bfloat16)
    unit_q_grad = cos_grad[:, None] * key_prior
    prior_grad = cos_grad[:, None] * query_unit
    query_grad = normalize_grad(queries, query_scale, unit_q_grad).astype(jnp.bfloat16)
    unit_k_grad = jnp.concatenate([prior_grad[1:], next_cos_grad * query_next], axis=0)
    key_grad = normalize_grad(key_rows, key_scale, unit_k_grad).astype(jnp.bfloat16)
    parts = []
    for q_block, k_block in zip(query_blocks, key_blocks):
        part = lax.dot_general(query_grad, q_block, contract_last, preferred_element_type=jnp.float32)
        part = part + lax.dot_general(key_grad, k_block, contract_last, preferred_element_type=jnp.float32)
        parts.append(part.astype(jnp.bfloat16))
    x_grad = jnp.concatenate(parts, axis=1)
    slots = jnp.arange(len(index), dtype=jnp.int32)
    order = jnp.sum(jnp.where(jnp.stack(index)[None, :] == slots[:, None], slots[None, :], 0), axis=1)
    x_grad = permute_cols(x_grad, [order[j] for j in range(len(index))], width)
    return (x_grad[None], segment_grad[None])


def solution(mesh):
    placed = (
        P("dp", "seq", None),
        P("dp", "seq", None),
        P("dp", "seq", None),
        P("dp", "seq"),
        P("dp", "seq"),
        P("dp", "seq"),
        P("dp", None),
        P("dp", None),
    )
    return jax.shard_map(
        per_device,
        mesh=mesh,
        in_specs=placed,
        out_specs=(P("dp", "seq", None), P("dp", "seq", None)),
        check_vma=False,
    )
```

```python
import jax
import jax.numpy as jnp
from jax import lax
from jax.sharding import PartitionSpec as P

prob_scale = 65536.0
norm_eps = 1e-06
exact = lax.Precision.HIGHEST
contract_last = (((1,), (1,)), ((), ()))
contract_first = (((0,), (0,)), ((), ()))


def shifted(block, axis, distance):
    devices = range(lax.axis_size(axis))
    route = [(i - distance, i) for i in devices if i - distance in devices]
    return lax.ppermute(block, axis, route)


def normalize_grad(vectors, scales, unit_grad):
    inner_prod = jnp.sum(vectors * unit_grad, axis=-1, keepdims=True)
    return scales * unit_grad - scales * scales * scales * inner_prod * vectors


def seq_scan(log_keep, vectors, axis, from_lower):
    size = lax.axis_size(axis)
    step = 1
    incl_log, incl_vec = log_keep, vectors
    excl_log = jnp.zeros_like(log_keep)
    excl_vec = jnp.zeros_like(vectors)
    while step < size:
        packed = jnp.concatenate([incl_vec, incl_log], axis=-1)
        got = shifted(packed, axis, step if from_lower else -step)
        got_log, got_vec = got[:, -1:], got[:, :-1]
        excl_vec = jnp.exp(excl_log) * got_vec + excl_vec
        excl_log = excl_log + got_log
        if 2 * step < size:
            incl_vec = jnp.exp(incl_log) * got_vec + incl_vec
            incl_log = incl_log + got_log
        step *= 2
    return excl_vec


def gather_blocks(blocks, axis):
    size = lax.axis_size(axis)
    own = lax.axis_index(axis)
    pairs = [blocks]
    index = [own]
    for k in range(1, size // 2):
        route = [(i, (i + 2 * k) % size) for i in range(size)]
        pairs.append(lax.ppermute(blocks, axis, route))
        index.append((own - 2 * k) % size)
    swap = [(i, i ^ 1) for i in range(size)]
    partner = lax.ppermute(pairs, axis, swap)
    pairs = pairs + partner
    index = index + [i ^ 1 for i in index]
    return pairs, index


def direct_scan(log_keep, vectors, axis):
    size = lax.axis_size(axis)
    packed = jnp.concatenate([vectors, log_keep], axis=-1)
    total = jnp.zeros_like(vectors)
    gap = jnp.zeros_like(log_keep)
    for step in range(1, size):
        got = shifted(packed, axis, -step)
        total = total + jnp.exp(gap) * got[:, :-1]
        gap = gap + got[:, -1:]
    return total


def split_dot(rows, blocks, index, width):
    total = None
    for block, at in zip(blocks, index):
        part = lax.dynamic_slice_in_dim(rows, at * width, width, axis=1)
        term = jnp.dot(part, block, preferred_element_type=jnp.float32)
        total = term if total is None else total + term
    return total


def permute_cols(rows, index, width):
    return jnp.concatenate(
        [lax.dynamic_slice_in_dim(rows, at * width, width, axis=1) for at in index], axis=1
    )


def unit_of(rows):
    scale = lax.rsqrt(jnp.sum(rows * rows, axis=1, keepdims=True) + norm_eps)
    return rows * scale, scale


def per_device(
    encoder_out,
    out_grad,
    segment_states,
    segment_starts,
    segment_counts,
    segment_probs,
    query_weight,
    key_weight,
):
    token_rows = encoder_out[0]
    grad_rows = out_grad[0]
    token_count = token_rows.shape[0]
    slot_count = segment_states.shape[1]
    width = query_weight.shape[0]
    shard_index = lax.axis_index("seq")
    pairs, index = gather_blocks((query_weight, key_weight), "dp")
    query_blocks = [p[0] for p in pairs]
    key_blocks = [p[1] for p in pairs]
    position = jnp.arange(token_count)
    later_rows = (shard_index > 0) | (position > 0)
    segment_total = segment_counts[0, 0]
    slot_index = jnp.arange(slot_count)
    slot_used = slot_index < segment_total
    start_pos = segment_starts[0]
    smoothing = jnp.where(slot_used, segment_probs[0].astype(jnp.float32) / prob_scale, 0.0)
    reached = slot_used[None, :] & (start_pos[None, :] <= position[:, None])
    member_id = jnp.sum(reached.astype(jnp.int32), axis=1) - 1
    membership = (member_id[:, None] == slot_index[None, :]).astype(jnp.float32)
    leading = (member_id < 0).astype(jnp.float32)
    starts = jnp.any(slot_used[None, :] & (start_pos[None, :] == position[:, None]), axis=1)
    running = jnp.cumsum(jnp.log(1.0 - smoothing))
    lower = slot_index[None, :] <= slot_index[:, None]
    decay_table = jnp.where(
        lower, jnp.exp(jnp.where(lower, running[:, None] - running[None, :], 0.0)), 0.0
    )
    weighted_states = smoothing[:, None] * segment_states[0].astype(jnp.float32)
    local_state = jnp.dot(decay_table, weighted_states, precision=exact)
    keep_all = jnp.exp(running)
    last_log = running[slot_count - 1 :][None]
    state_in = seq_scan(last_log, local_state[slot_count - 1 :], "seq", True)
    smoothed = local_state + keep_all[:, None] * state_in
    picked = jnp.dot(membership, smoothed, precision=exact) + leading[:, None] * state_in
    conf_grad = jnp.sum(grad_rows * picked, axis=1)
    cos_grad = jnp.where(later_rows, jnp.where(starts, -0.5 * conf_grad, 0.5 * conf_grad), 0.0)
    owner_keep = jnp.where(member_id >= 0, keep_all[jnp.maximum(member_id, 0)], 1.0)
    level = jnp.where(later_rows, 0.5, jnp.where(starts, 1.0, 0.0))
    rise = jnp.where(later_rows, jnp.where(starts, -0.5, 0.5), 0.0)
    grad_wide = grad_rows.astype(jnp.float32)
    base_vector = jnp.dot((owner_keep * level)[None, :], grad_wide, precision=exact)
    to_prev = jnp.concatenate([token_rows[:1].astype(jnp.float32), cos_grad[:1][None]], axis=1)
    from_next = shifted(to_prev, "seq", -1)
    prev_row = shifted(token_rows[token_count - 1 :], "seq", 1)
    next_row = from_next[:, :-1].astype(token_rows.dtype)
    next_cos_grad = from_next[:, -1:]
    rows_ext = jnp.concatenate([token_rows, prev_row, next_row], axis=0)
    queries_ext = split_dot(rows_ext, query_blocks, index, width)
    keys_ext = split_dot(rows_ext, key_blocks, index, width)
    queries = queries_ext[:token_count]
    key_rows = keys_ext[:token_count]
    query_unit, query_scale = unit_of(queries)
    key_unit, key_scale = unit_of(key_rows)
    key_before, _ = unit_of(keys_ext[token_count : token_count + 1])
    query_next, _ = unit_of(queries_ext[token_count + 1 :])
    key_prior = jnp.concatenate([key_before, key_unit[:-1]], axis=0)
    cosine = jnp.sum(query_unit * key_prior, axis=1)
    boundary_prob = jnp.where(later_rows, 0.5 * (1.0 - cosine), 1.0)
    confidence = jnp.where(starts, boundary_prob, 1.0 - boundary_prob)
    weighted_grad = confidence[:, None] * grad_rows
    slot_grad = lax.dot_general(membership, weighted_grad, contract_first, precision=exact)
    back_vector = base_vector + jnp.dot(
        (owner_keep * rise * cosine)[None, :], grad_wide, precision=exact
    )
    back_vector, queries, query_scale, key_rows, key_scale, key_prior, query_unit, query_next = (
        lax.optimization_barrier(
            (back_vector, queries, query_scale, key_rows, key_scale, key_prior, query_unit, query_next)
        )
    )
    grad_in = seq_scan(last_log, back_vector, "seq", False)
    reach_end = jnp.exp(running[slot_count - 1] - running)
    state_grad = (
        lax.dot_general(decay_table, slot_grad, contract_first, precision=exact)
        + reach_end[:, None] * grad_in
    )
    segment_grad = (smoothing[:, None] * state_grad).astype(jnp.bfloat16)
    unit_q_grad = cos_grad[:, None] * key_prior
    prior_grad = cos_grad[:, None] * query_unit
    query_grad = normalize_grad(queries, query_scale, unit_q_grad).astype(jnp.bfloat16)
    unit_k_grad = jnp.concatenate([prior_grad[1:], next_cos_grad * query_next], axis=0)
    key_grad = normalize_grad(key_rows, key_scale, unit_k_grad).astype(jnp.bfloat16)
    parts = []
    for q_block, k_block in zip(query_blocks, key_blocks):
        part = lax.dot_general(query_grad, q_block, contract_last, preferred_element_type=jnp.float32)
        part = part + lax.dot_general(key_grad, k_block, contract_last, preferred_element_type=jnp.float32)
        parts.append(part.astype(jnp.bfloat16))
    x_grad = jnp.concatenate(parts, axis=1)
    slots = jnp.arange(len(index), dtype=jnp.int32)
    order = jnp.sum(jnp.where(jnp.stack(index)[None, :] == slots[:, None], slots[None, :], 0), axis=1)
    x_grad = permute_cols(x_grad, [order[j] for j in range(len(index))], width)
    return (x_grad[None], segment_grad[None])


def solution(mesh):
    placed = (
        P("dp", "seq", None),
        P("dp", "seq", None),
        P("dp", "seq", None),
        P("dp", "seq"),
        P("dp", "seq"),
        P("dp", "seq"),
        P("dp", None),
        P("dp", None),
    )
    return jax.shard_map(
        per_device,
        mesh=mesh,
        in_specs=placed,
        out_specs=(P("dp", "seq", None), P("dp", "seq", None)),
        check_vma=False,
    )
```

```python
import jax
import jax.numpy as jnp
from jax import lax
from jax.sharding import PartitionSpec as P

prob_scale = 65536.0
norm_eps = 1e-06
exact = lax.Precision.HIGHEST
contract_last = (((1,), (1,)), ((), ()))
contract_first = (((0,), (0,)), ((), ()))


def shifted(block, axis, distance):
    devices = range(lax.axis_size(axis))
    route = [(i - distance, i) for i in devices if i - distance in devices]
    return lax.ppermute(block, axis, route)


def normalize_grad(vectors, scales, unit_grad):
    inner_prod = jnp.sum(vectors * unit_grad, axis=-1, keepdims=True)
    return scales * unit_grad - scales * scales * scales * inner_prod * vectors


def seq_scan(log_keep, vectors, axis, from_lower):
    size = lax.axis_size(axis)
    step = 1
    incl_log, incl_vec = log_keep, vectors
    excl_log = jnp.zeros_like(log_keep)
    excl_vec = jnp.zeros_like(vectors)
    while step < size:
        packed = jnp.concatenate([incl_vec, incl_log], axis=-1)
        got = shifted(packed, axis, step if from_lower else -step)
        got_log, got_vec = got[:, -1:], got[:, :-1]
        excl_vec = jnp.exp(excl_log) * got_vec + excl_vec
        excl_log = excl_log + got_log
        if 2 * step < size:
            incl_vec = jnp.exp(incl_log) * got_vec + incl_vec
            incl_log = incl_log + got_log
        step *= 2
    return excl_vec


def gather_blocks(blocks, axis):
    size = lax.axis_size(axis)
    own = lax.axis_index(axis)
    pairs = [blocks]
    index = [own]
    for k in range(1, size // 2):
        route = [(i, (i + 2 * k) % size) for i in range(size)]
        pairs.append(lax.ppermute(blocks, axis, route))
        index.append((own - 2 * k) % size)
    swap = [(i, i ^ 1) for i in range(size)]
    partner = lax.ppermute(pairs, axis, swap)
    pairs = pairs + partner
    index = index + [i ^ 1 for i in index]
    return pairs, index


def direct_scan(log_keep, vectors, axis):
    size = lax.axis_size(axis)
    packed = jnp.concatenate([vectors, log_keep], axis=-1)
    total = jnp.zeros_like(vectors)
    gap = jnp.zeros_like(log_keep)
    for step in range(1, size):
        got = shifted(packed, axis, -step)
        total = total + jnp.exp(gap) * got[:, :-1]
        gap = gap + got[:, -1:]
    return total


def split_dot(rows, blocks, index, width):
    total = None
    for block, at in zip(blocks, index):
        part = lax.dynamic_slice_in_dim(rows, at * width, width, axis=1)
        term = jnp.dot(part, block, preferred_element_type=jnp.float32)
        total = term if total is None else total + term
    return total


def permute_cols(rows, index, width):
    return jnp.concatenate(
        [lax.dynamic_slice_in_dim(rows, at * width, width, axis=1) for at in index], axis=1
    )


def unit_of(rows):
    scale = lax.rsqrt(jnp.sum(rows * rows, axis=1, keepdims=True) + norm_eps)
    return rows * scale, scale


def per_device(
    encoder_out,
    out_grad,
    segment_states,
    segment_starts,
    segment_counts,
    segment_probs,
    query_weight,
    key_weight,
):
    token_rows = encoder_out[0]
    grad_rows = out_grad[0]
    token_count = token_rows.shape[0]
    slot_count = segment_states.shape[1]
    width = query_weight.shape[0]
    shard_index = lax.axis_index("seq")
    pairs, index = gather_blocks((query_weight, key_weight), "dp")
    query_blocks = [p[0] for p in pairs]
    key_blocks = [p[1] for p in pairs]
    position = jnp.arange(token_count)
    later_rows = (shard_index > 0) | (position > 0)
    segment_total = segment_counts[0, 0]
    slot_index = jnp.arange(slot_count)
    slot_used = slot_index < segment_total
    start_pos = segment_starts[0]
    smoothing = jnp.where(slot_used, segment_probs[0].astype(jnp.float32) / prob_scale, 0.0)
    reached = slot_used[None, :] & (start_pos[None, :] <= position[:, None])
    member_id = jnp.sum(reached.astype(jnp.int32), axis=1) - 1
    membership = (member_id[:, None] == slot_index[None, :]).astype(jnp.float32)
    leading = (member_id < 0).astype(jnp.float32)
    starts = jnp.any(slot_used[None, :] & (start_pos[None, :] == position[:, None]), axis=1)
    running = jnp.cumsum(jnp.log(1.0 - smoothing))
    lower = slot_index[None, :] <= slot_index[:, None]
    decay_table = jnp.where(
        lower, jnp.exp(jnp.where(lower, running[:, None] - running[None, :], 0.0)), 0.0
    )
    weighted_states = smoothing[:, None] * segment_states[0].astype(jnp.float32)
    local_state = jnp.dot(decay_table, weighted_states, precision=exact)
    keep_all = jnp.exp(running)
    last_log = running[slot_count - 1 :][None]
    state_in = seq_scan(last_log, local_state[slot_count - 1 :], "seq", True)
    smoothed = local_state + keep_all[:, None] * state_in
    picked = jnp.dot(membership, smoothed, precision=exact) + leading[:, None] * state_in
    conf_grad = jnp.sum(grad_rows * picked, axis=1)
    cos_grad = jnp.where(later_rows, jnp.where(starts, -0.5 * conf_grad, 0.5 * conf_grad), 0.0)
    owner_keep = jnp.where(member_id >= 0, keep_all[jnp.maximum(member_id, 0)], 1.0)
    level = jnp.where(later_rows, 0.5, jnp.where(starts, 1.0, 0.0))
    rise = jnp.where(later_rows, jnp.where(starts, -0.5, 0.5), 0.0)
    grad_wide = grad_rows.astype(jnp.float32)
    base_vector = jnp.dot((owner_keep * level)[None, :], grad_wide, precision=exact)
    to_prev = jnp.concatenate([token_rows[:1].astype(jnp.float32), cos_grad[:1][None]], axis=1)
    from_next = shifted(to_prev, "seq", -1)
    prev_row = shifted(token_rows[token_count - 1 :], "seq", 1)
    next_row = from_next[:, :-1].astype(token_rows.dtype)
    next_cos_grad = from_next[:, -1:]
    rows_ext = jnp.concatenate([token_rows, prev_row, next_row], axis=0)
    queries_ext = split_dot(rows_ext, query_blocks, index, width)
    keys_ext = split_dot(rows_ext, key_blocks, index, width)
    queries = queries_ext[:token_count]
    key_rows = keys_ext[:token_count]
    query_unit, query_scale = unit_of(queries)
    key_unit, key_scale = unit_of(key_rows)
    key_before, _ = unit_of(keys_ext[token_count : token_count + 1])
    query_next, _ = unit_of(queries_ext[token_count + 1 :])
    key_prior = jnp.concatenate([key_before, key_unit[:-1]], axis=0)
    key_shift = keys_ext[token_count : token_count + 1]
    raw_prior = jnp.concatenate([key_shift, key_rows[:-1]], axis=0)
    prior_sq = jnp.sum(raw_prior * raw_prior, axis=1)
    query_sq = jnp.sum(queries * queries, axis=1)
    cosine = (
        jnp.sum(queries * raw_prior, axis=1) * lax.rsqrt(query_sq + norm_eps) * lax.rsqrt(prior_sq + norm_eps)
    )
    boundary_prob = jnp.where(later_rows, 0.5 * (1.0 - cosine), 1.0)
    confidence = jnp.where(starts, boundary_prob, 1.0 - boundary_prob)
    weighted_grad = confidence[:, None] * grad_rows
    slot_grad = lax.dot_general(membership, weighted_grad, contract_first, precision=exact)
    back_vector = base_vector + jnp.dot(
        (owner_keep * rise * cosine)[None, :], grad_wide, precision=exact
    )
    grad_in = seq_scan(last_log, back_vector, "seq", False)
    reach_end = jnp.exp(running[slot_count - 1] - running)
    state_grad = (
        lax.dot_general(decay_table, slot_grad, contract_first, precision=exact)
        + reach_end[:, None] * grad_in
    )
    segment_grad = (smoothing[:, None] * state_grad).astype(jnp.bfloat16)
    unit_q_grad = cos_grad[:, None] * key_prior
    prior_grad = cos_grad[:, None] * query_unit
    query_grad = normalize_grad(queries, query_scale, unit_q_grad).astype(jnp.bfloat16)
    unit_k_grad = jnp.concatenate([prior_grad[1:], next_cos_grad * query_next], axis=0)
    key_grad = normalize_grad(key_rows, key_scale, unit_k_grad).astype(jnp.bfloat16)
    parts = []
    for q_block, k_block in zip(query_blocks, key_blocks):
        part = lax.dot_general(query_grad, q_block, contract_last, preferred_element_type=jnp.float32)
        part = part + lax.dot_general(key_grad, k_block, contract_last, preferred_element_type=jnp.float32)
        parts.append(part.astype(jnp.bfloat16))
    x_grad = jnp.concatenate(parts, axis=1)
    slots = jnp.arange(len(index), dtype=jnp.int32)
    order = jnp.sum(jnp.where(jnp.stack(index)[None, :] == slots[:, None], slots[None, :], 0), axis=1)
    x_grad = permute_cols(x_grad, [order[j] for j in range(len(index))], width)
    return (x_grad[None], segment_grad[None])


def solution(mesh):
    placed = (
        P("dp", "seq", None),
        P("dp", "seq", None),
        P("dp", "seq", None),
        P("dp", "seq"),
        P("dp", "seq"),
        P("dp", "seq"),
        P("dp", None),
        P("dp", None),
    )
    return jax.shard_map(
        per_device,
        mesh=mesh,
        in_specs=placed,
        out_specs=(P("dp", "seq", None), P("dp", "seq", None)),
        check_vma=False,
    )
```

```python
import jax
import jax.numpy as jnp
from jax import lax
from jax.sharding import PartitionSpec as P

prob_scale = 65536.0
norm_eps = 1e-06
exact = lax.Precision.HIGHEST
contract_last = (((1,), (1,)), ((), ()))
contract_first = (((0,), (0,)), ((), ()))


def shifted(block, axis, distance):
    devices = range(lax.axis_size(axis))
    route = [(i - distance, i) for i in devices if i - distance in devices]
    return lax.ppermute(block, axis, route)


def normalize_grad(vectors, scales, unit_grad):
    inner_prod = jnp.sum(vectors * unit_grad, axis=-1, keepdims=True)
    return scales * unit_grad - scales * scales * scales * inner_prod * vectors


def seq_scan(log_keep, vectors, axis, from_lower):
    size = lax.axis_size(axis)
    step = 1
    incl_log, incl_vec = log_keep, vectors
    excl_log = jnp.zeros_like(log_keep)
    excl_vec = jnp.zeros_like(vectors)
    while step < size:
        packed = jnp.concatenate([incl_vec, incl_log], axis=-1)
        got = shifted(packed, axis, step if from_lower else -step)
        got_log, got_vec = got[:, -1:], got[:, :-1]
        excl_vec = jnp.exp(excl_log) * got_vec + excl_vec
        excl_log = excl_log + got_log
        if 2 * step < size:
            incl_vec = jnp.exp(incl_log) * got_vec + incl_vec
            incl_log = incl_log + got_log
        step *= 2
    return excl_vec


def gather_blocks(blocks, axis):
    size = lax.axis_size(axis)
    own = lax.axis_index(axis)
    pairs = [blocks]
    index = [own]
    for k in range(1, size // 2):
        route = [(i, (i + 2 * k) % size) for i in range(size)]
        pairs.append(lax.ppermute(blocks, axis, route))
        index.append((own - 2 * k) % size)
    swap = [(i, i ^ 1) for i in range(size)]
    partner = lax.ppermute(pairs, axis, swap)
    pairs = pairs + partner
    index = index + [i ^ 1 for i in index]
    return pairs, index


def direct_scan(log_keep, vectors, axis):
    size = lax.axis_size(axis)
    packed = jnp.concatenate([vectors, log_keep], axis=-1)
    total = jnp.zeros_like(vectors)
    gap = jnp.zeros_like(log_keep)
    for step in range(1, size):
        got = shifted(packed, axis, -step)
        total = total + jnp.exp(gap) * got[:, :-1]
        gap = gap + got[:, -1:]
    return total


def split_dot(rows, blocks, index, width):
    total = None
    for block, at in zip(blocks, index):
        part = lax.dynamic_slice_in_dim(rows, at * width, width, axis=1)
        term = jnp.dot(part, block, preferred_element_type=jnp.float32)
        total = term if total is None else total + term
    return total


def permute_cols(rows, index, width):
    return jnp.concatenate(
        [lax.dynamic_slice_in_dim(rows, at * width, width, axis=1) for at in index], axis=1
    )


def unit_of(rows):
    scale = lax.rsqrt(jnp.sum(rows * rows, axis=1, keepdims=True) + norm_eps)
    return rows * scale, scale


def per_device(
    encoder_out,
    out_grad,
    segment_states,
    segment_starts,
    segment_counts,
    segment_probs,
    query_weight,
    key_weight,
):
    token_rows = encoder_out[0]
    grad_rows = out_grad[0]
    token_count = token_rows.shape[0]
    slot_count = segment_states.shape[1]
    width = query_weight.shape[0]
    shard_index = lax.axis_index("seq")
    pairs, index = gather_blocks((query_weight, key_weight), "dp")
    query_blocks = [p[0] for p in pairs]
    key_blocks = [p[1] for p in pairs]
    position = jnp.arange(token_count)
    later_rows = (shard_index > 0) | (position > 0)
    segment_total = segment_counts[0, 0]
    slot_index = jnp.arange(slot_count)
    slot_used = slot_index < segment_total
    start_pos = segment_starts[0]
    smoothing = jnp.where(slot_used, segment_probs[0].astype(jnp.float32) / prob_scale, 0.0)
    reached = slot_used[None, :] & (start_pos[None, :] <= position[:, None])
    member_id = jnp.sum(reached.astype(jnp.int32), axis=1) - 1
    membership = (member_id[:, None] == slot_index[None, :]).astype(jnp.float32)
    leading = (member_id < 0).astype(jnp.float32)
    starts = jnp.any(slot_used[None, :] & (start_pos[None, :] == position[:, None]), axis=1)
    running = jnp.cumsum(jnp.log(1.0 - smoothing))
    lower = slot_index[None, :] <= slot_index[:, None]
    decay_table = jnp.where(
        lower, jnp.exp(jnp.where(lower, running[:, None] - running[None, :], 0.0)), 0.0
    )
    weighted_states = smoothing[:, None] * segment_states[0].astype(jnp.float32)
    local_state = jnp.dot(decay_table, weighted_states, precision=exact)
    keep_all = jnp.exp(running)
    last_log = running[slot_count - 1 :][None]
    state_in = seq_scan(last_log, local_state[slot_count - 1 :], "seq", True)
    smoothed = local_state + keep_all[:, None] * state_in
    picked = jnp.dot(membership, smoothed, precision=exact) + leading[:, None] * state_in
    conf_grad = jnp.sum(grad_rows * picked, axis=1)
    cos_grad = jnp.where(later_rows, jnp.where(starts, -0.5 * conf_grad, 0.5 * conf_grad), 0.0)
    owner_keep = jnp.where(member_id >= 0, keep_all[jnp.maximum(member_id, 0)], 1.0)
    level = jnp.where(later_rows, 0.5, jnp.where(starts, 1.0, 0.0))
    rise = jnp.where(later_rows, jnp.where(starts, -0.5, 0.5), 0.0)
    grad_wide = grad_rows.astype(jnp.float32)
    base_vector = jnp.sum(grad_wide * (owner_keep * level)[:, None], axis=0, keepdims=True)
    rise_rows = lax.optimization_barrier(grad_wide * (owner_keep * rise)[:, None])
    to_prev = jnp.concatenate([token_rows[:1].astype(jnp.float32), cos_grad[:1][None]], axis=1)
    from_next = shifted(to_prev, "seq", -1)
    prev_row = shifted(token_rows[token_count - 1 :], "seq", 1)
    next_row = from_next[:, :-1].astype(token_rows.dtype)
    next_cos_grad = from_next[:, -1:]
    rows_ext = jnp.concatenate([token_rows, prev_row, next_row], axis=0)
    queries_ext = split_dot(rows_ext, query_blocks, index, width)
    keys_ext = split_dot(rows_ext, key_blocks, index, width)
    queries = queries_ext[:token_count]
    key_rows = keys_ext[:token_count]
    query_unit, query_scale = unit_of(queries)
    key_unit, key_scale = unit_of(key_rows)
    key_before, _ = unit_of(keys_ext[token_count : token_count + 1])
    query_next, _ = unit_of(queries_ext[token_count + 1 :])
    key_prior = jnp.concatenate([key_before, key_unit[:-1]], axis=0)
    key_shift = keys_ext[token_count : token_count + 1]
    raw_prior = jnp.concatenate([key_shift, key_rows[:-1]], axis=0)
    prior_sq = jnp.sum(raw_prior * raw_prior, axis=1)
    query_sq = jnp.sum(queries * queries, axis=1)
    cosine = (
        jnp.sum(queries * raw_prior, axis=1) * lax.rsqrt(query_sq + norm_eps) * lax.rsqrt(prior_sq + norm_eps)
    )
    boundary_prob = jnp.where(later_rows, 0.5 * (1.0 - cosine), 1.0)
    confidence = jnp.where(starts, boundary_prob, 1.0 - boundary_prob)
    weighted_grad = confidence[:, None] * grad_rows
    slot_grad = lax.dot_general(membership, weighted_grad, contract_first, precision=exact)
    back_vector = base_vector + jnp.sum(rise_rows * cosine[:, None], axis=0, keepdims=True)
    grad_in = seq_scan(last_log, back_vector, "seq", False)
    reach_end = jnp.exp(running[slot_count - 1] - running)
    state_grad = (
        lax.dot_general(decay_table, slot_grad, contract_first, precision=exact)
        + reach_end[:, None] * grad_in
    )
    segment_grad = (smoothing[:, None] * state_grad).astype(jnp.bfloat16)
    unit_q_grad = cos_grad[:, None] * key_prior
    prior_grad = cos_grad[:, None] * query_unit
    query_grad = normalize_grad(queries, query_scale, unit_q_grad).astype(jnp.bfloat16)
    unit_k_grad = jnp.concatenate([prior_grad[1:], next_cos_grad * query_next], axis=0)
    key_grad = normalize_grad(key_rows, key_scale, unit_k_grad).astype(jnp.bfloat16)
    parts = []
    for q_block, k_block in zip(query_blocks, key_blocks):
        part = lax.dot_general(query_grad, q_block, contract_last, preferred_element_type=jnp.float32)
        part = part + lax.dot_general(key_grad, k_block, contract_last, preferred_element_type=jnp.float32)
        parts.append(part.astype(jnp.bfloat16))
    x_grad = jnp.concatenate(parts, axis=1)
    slots = jnp.arange(len(index), dtype=jnp.int32)
    order = jnp.sum(jnp.where(jnp.stack(index)[None, :] == slots[:, None], slots[None, :], 0), axis=1)
    x_grad = permute_cols(x_grad, [order[j] for j in range(len(index))], width)
    return (x_grad[None], segment_grad[None])


def solution(mesh):
    placed = (
        P("dp", "seq", None),
        P("dp", "seq", None),
        P("dp", "seq", None),
        P("dp", "seq"),
        P("dp", "seq"),
        P("dp", "seq"),
        P("dp", None),
        P("dp", None),
    )
    return jax.shard_map(
        per_device,
        mesh=mesh,
        in_specs=placed,
        out_specs=(P("dp", "seq", None), P("dp", "seq", None)),
        check_vma=False,
    )
```

```python
import jax
import jax.numpy as jnp
from jax import lax
from jax.sharding import PartitionSpec as P

prob_scale = 65536.0
norm_eps = 1e-06
exact = lax.Precision.HIGHEST
contract_last = (((1,), (1,)), ((), ()))
contract_first = (((0,), (0,)), ((), ()))


def shifted(block, axis, distance):
    devices = range(lax.axis_size(axis))
    route = [(i - distance, i) for i in devices if i - distance in devices]
    return lax.ppermute(block, axis, route)


def normalize_grad(vectors, scales, unit_grad):
    inner_prod = jnp.sum(vectors * unit_grad, axis=-1, keepdims=True)
    return scales * unit_grad - scales * scales * scales * inner_prod * vectors


def seq_scan(log_keep, vectors, axis, from_lower):
    size = lax.axis_size(axis)
    step = 1
    incl_log, incl_vec = log_keep, vectors
    excl_log = jnp.zeros_like(log_keep)
    excl_vec = jnp.zeros_like(vectors)
    while step < size:
        packed = jnp.concatenate([incl_vec, incl_log], axis=-1)
        got = shifted(packed, axis, step if from_lower else -step)
        got_log, got_vec = got[:, -1:], got[:, :-1]
        excl_vec = jnp.exp(excl_log) * got_vec + excl_vec
        excl_log = excl_log + got_log
        if 2 * step < size:
            incl_vec = jnp.exp(incl_log) * got_vec + incl_vec
            incl_log = incl_log + got_log
        step *= 2
    return excl_vec


def gather_blocks(blocks, axis):
    size = lax.axis_size(axis)
    own = lax.axis_index(axis)
    pairs = [blocks]
    index = [own]
    for k in range(1, size // 2):
        route = [(i, (i + 2 * k) % size) for i in range(size)]
        pairs.append(lax.ppermute(blocks, axis, route))
        index.append((own - 2 * k) % size)
    swap = [(i, i ^ 1) for i in range(size)]
    partner = lax.ppermute(pairs, axis, swap)
    pairs = pairs + partner
    index = index + [i ^ 1 for i in index]
    return pairs, index


def direct_scan(log_keep, vectors, axis):
    size = lax.axis_size(axis)
    packed = jnp.concatenate([vectors, log_keep], axis=-1)
    total = jnp.zeros_like(vectors)
    gap = jnp.zeros_like(log_keep)
    for step in range(1, size):
        got = shifted(packed, axis, -step)
        total = total + jnp.exp(gap) * got[:, :-1]
        gap = gap + got[:, -1:]
    return total


def split_dot(rows, blocks, index, width):
    total = None
    for block, at in zip(blocks, index):
        part = lax.dynamic_slice_in_dim(rows, at * width, width, axis=1)
        term = jnp.dot(part, block, preferred_element_type=jnp.float32)
        total = term if total is None else total + term
    return total


def permute_cols(rows, index, width):
    return jnp.concatenate(
        [lax.dynamic_slice_in_dim(rows, at * width, width, axis=1) for at in index], axis=1
    )


def unit_of(rows):
    scale = lax.rsqrt(jnp.sum(rows * rows, axis=1, keepdims=True) + norm_eps)
    return rows * scale, scale


def per_device(
    encoder_out,
    out_grad,
    segment_states,
    segment_starts,
    segment_counts,
    segment_probs,
    query_weight,
    key_weight,
):
    token_rows = encoder_out[0]
    grad_rows = out_grad[0]
    token_count = token_rows.shape[0]
    slot_count = segment_states.shape[1]
    width = query_weight.shape[0]
    shard_index = lax.axis_index("seq")
    pairs, index = gather_blocks((query_weight, key_weight), "dp")
    query_blocks = [p[0] for p in pairs]
    key_blocks = [p[1] for p in pairs]
    position = jnp.arange(token_count)
    later_rows = (shard_index > 0) | (position > 0)
    segment_total = segment_counts[0, 0]
    slot_index = jnp.arange(slot_count)
    slot_used = slot_index < segment_total
    start_pos = segment_starts[0]
    smoothing = jnp.where(slot_used, segment_probs[0].astype(jnp.float32) / prob_scale, 0.0)
    reached = slot_used[None, :] & (start_pos[None, :] <= position[:, None])
    member_id = jnp.sum(reached.astype(jnp.int32), axis=1) - 1
    membership = (member_id[:, None] == slot_index[None, :]).astype(jnp.float32)
    leading = (member_id < 0).astype(jnp.float32)
    starts = jnp.any(slot_used[None, :] & (start_pos[None, :] == position[:, None]), axis=1)
    running = jnp.cumsum(jnp.log(1.0 - smoothing))
    lower = slot_index[None, :] <= slot_index[:, None]
    decay_table = jnp.where(
        lower, jnp.exp(jnp.where(lower, running[:, None] - running[None, :], 0.0)), 0.0
    )
    weighted_states = smoothing[:, None] * segment_states[0].astype(jnp.float32)
    local_state = jnp.dot(decay_table, weighted_states, precision=exact)
    keep_all = jnp.exp(running)
    last_log = running[slot_count - 1 :][None]
    state_in = seq_scan(last_log, local_state[slot_count - 1 :], "seq", True)
    smoothed = local_state + keep_all[:, None] * state_in
    picked = jnp.dot(membership, smoothed, precision=exact) + leading[:, None] * state_in
    conf_grad = jnp.sum(grad_rows * picked, axis=1)
    cos_grad = jnp.where(later_rows, jnp.where(starts, -0.5 * conf_grad, 0.5 * conf_grad), 0.0)
    owner_keep = jnp.where(member_id >= 0, keep_all[jnp.maximum(member_id, 0)], 1.0)
    level = jnp.where(later_rows, 0.5, jnp.where(starts, 1.0, 0.0))
    rise = jnp.where(later_rows, jnp.where(starts, -0.5, 0.5), 0.0)
    grad_wide = grad_rows.astype(jnp.float32)
    base_vector = jnp.sum(grad_wide * (owner_keep * level)[:, None], axis=0, keepdims=True)
    rise_rows = lax.optimization_barrier(grad_wide * (owner_keep * rise)[:, None])
    to_prev = jnp.concatenate([token_rows[:1].astype(jnp.float32), cos_grad[:1][None]], axis=1)
    from_next = shifted(to_prev, "seq", -1)
    prev_row = shifted(token_rows[token_count - 1 :], "seq", 1)
    next_row = from_next[:, :-1].astype(token_rows.dtype)
    next_cos_grad = from_next[:, -1:]
    rows_ext = jnp.concatenate([token_rows, prev_row, next_row], axis=0)
    queries_ext = split_dot(rows_ext, query_blocks, index, width)
    keys_ext = split_dot(rows_ext, key_blocks, index, width)
    queries = queries_ext[:token_count]
    key_rows = keys_ext[:token_count]
    query_unit, query_scale = unit_of(queries)
    key_unit, key_scale = unit_of(key_rows)
    key_before, _ = unit_of(keys_ext[token_count : token_count + 1])
    query_next, _ = unit_of(queries_ext[token_count + 1 :])
    key_prior = jnp.concatenate([key_before, key_unit[:-1]], axis=0)
    key_shift = keys_ext[token_count : token_count + 1]
    raw_prior = jnp.concatenate([key_shift, key_rows[:-1]], axis=0)
    prior_sq = jnp.sum(raw_prior * raw_prior, axis=1)
    query_sq = jnp.sum(queries * queries, axis=1)
    cosine = (
        jnp.sum(queries * raw_prior, axis=1) * lax.rsqrt(query_sq + norm_eps) * lax.rsqrt(prior_sq + norm_eps)
    )
    boundary_prob = jnp.where(later_rows, 0.5 * (1.0 - cosine), 1.0)
    confidence = jnp.where(starts, boundary_prob, 1.0 - boundary_prob)
    weighted_grad = confidence[:, None] * grad_rows
    slot_grad = lax.dot_general(membership, weighted_grad, contract_first, precision=exact)
    back_vector = base_vector + jnp.dot(cosine[None, :], rise_rows, precision=exact)
    grad_in = seq_scan(last_log, back_vector, "seq", False)
    reach_end = jnp.exp(running[slot_count - 1] - running)
    state_grad = (
        lax.dot_general(decay_table, slot_grad, contract_first, precision=exact)
        + reach_end[:, None] * grad_in
    )
    segment_grad = (smoothing[:, None] * state_grad).astype(jnp.bfloat16)
    unit_q_grad = cos_grad[:, None] * key_prior
    prior_grad = cos_grad[:, None] * query_unit
    query_grad = normalize_grad(queries, query_scale, unit_q_grad).astype(jnp.bfloat16)
    unit_k_grad = jnp.concatenate([prior_grad[1:], next_cos_grad * query_next], axis=0)
    key_grad = normalize_grad(key_rows, key_scale, unit_k_grad).astype(jnp.bfloat16)
    parts = []
    for q_block, k_block in zip(query_blocks, key_blocks):
        part = lax.dot_general(query_grad, q_block, contract_last, preferred_element_type=jnp.float32)
        part = part + lax.dot_general(key_grad, k_block, contract_last, preferred_element_type=jnp.float32)
        parts.append(part.astype(jnp.bfloat16))
    x_grad = jnp.concatenate(parts, axis=1)
    slots = jnp.arange(len(index), dtype=jnp.int32)
    order = jnp.sum(jnp.where(jnp.stack(index)[None, :] == slots[:, None], slots[None, :], 0), axis=1)
    x_grad = permute_cols(x_grad, [order[j] for j in range(len(index))], width)
    return (x_grad[None], segment_grad[None])


def solution(mesh):
    placed = (
        P("dp", "seq", None),
        P("dp", "seq", None),
        P("dp", "seq", None),
        P("dp", "seq"),
        P("dp", "seq"),
        P("dp", "seq"),
        P("dp", None),
        P("dp", None),
    )
    return jax.shard_map(
        per_device,
        mesh=mesh,
        in_specs=placed,
        out_specs=(P("dp", "seq", None), P("dp", "seq", None)),
        check_vma=False,
    )
```

```python
import jax
import jax.numpy as jnp
from jax import lax
from jax.sharding import PartitionSpec as P

prob_scale = 65536.0
norm_eps = 1e-06
exact = lax.Precision.HIGHEST
contract_last = (((1,), (1,)), ((), ()))
contract_first = (((0,), (0,)), ((), ()))


def shifted(block, axis, distance):
    devices = range(lax.axis_size(axis))
    route = [(i - distance, i) for i in devices if i - distance in devices]
    return lax.ppermute(block, axis, route)


def normalize_grad(vectors, scales, unit_grad):
    inner_prod = jnp.sum(vectors * unit_grad, axis=-1, keepdims=True)
    return scales * unit_grad - scales * scales * scales * inner_prod * vectors


def seq_scan(log_keep, vectors, axis, from_lower, held=None):
    size = lax.axis_size(axis)
    step = 1
    incl_log, incl_vec = log_keep, vectors
    excl_log = jnp.zeros_like(log_keep)
    excl_vec = jnp.zeros_like(vectors)
    while step < size:
        packed = jnp.concatenate([incl_vec, incl_log], axis=-1)
        got = shifted(packed, axis, step if from_lower else -step)
        if held is not None and step == 1:
            got, held = lax.optimization_barrier((got, held))
        got_log, got_vec = got[:, -1:], got[:, :-1]
        excl_vec = jnp.exp(excl_log) * got_vec + excl_vec
        excl_log = excl_log + got_log
        if 2 * step < size:
            incl_vec = jnp.exp(incl_log) * got_vec + incl_vec
            incl_log = incl_log + got_log
        step *= 2
    if held is not None:
        return excl_vec, held
    return excl_vec


def gather_blocks(blocks, axis):
    size = lax.axis_size(axis)
    own = lax.axis_index(axis)
    pairs = [blocks]
    index = [own]
    for k in range(1, size // 2):
        route = [(i, (i + 2 * k) % size) for i in range(size)]
        pairs.append(lax.ppermute(blocks, axis, route))
        index.append((own - 2 * k) % size)
    swap = [(i, i ^ 1) for i in range(size)]
    partner = lax.ppermute(pairs, axis, swap)
    pairs = pairs + partner
    index = index + [i ^ 1 for i in index]
    return pairs, index


def direct_scan(log_keep, vectors, axis):
    size = lax.axis_size(axis)
    packed = jnp.concatenate([vectors, log_keep], axis=-1)
    total = jnp.zeros_like(vectors)
    gap = jnp.zeros_like(log_keep)
    for step in range(1, size):
        got = shifted(packed, axis, -step)
        total = total + jnp.exp(gap) * got[:, :-1]
        gap = gap + got[:, -1:]
    return total


def split_dot(rows, blocks, index, width):
    total = None
    for block, at in zip(blocks, index):
        part = lax.dynamic_slice_in_dim(rows, at * width, width, axis=1)
        term = jnp.dot(part, block, preferred_element_type=jnp.float32)
        total = term if total is None else total + term
    return total


def permute_cols(rows, index, width):
    return jnp.concatenate(
        [lax.dynamic_slice_in_dim(rows, at * width, width, axis=1) for at in index], axis=1
    )


def unit_of(rows):
    scale = lax.rsqrt(jnp.sum(rows * rows, axis=1, keepdims=True) + norm_eps)
    return rows * scale, scale


def per_device(
    encoder_out,
    out_grad,
    segment_states,
    segment_starts,
    segment_counts,
    segment_probs,
    query_weight,
    key_weight,
):
    token_rows = encoder_out[0]
    grad_rows = out_grad[0]
    token_count = token_rows.shape[0]
    slot_count = segment_states.shape[1]
    width = query_weight.shape[0]
    shard_index = lax.axis_index("seq")
    pairs, index = gather_blocks((query_weight, key_weight), "dp")
    query_blocks = [p[0] for p in pairs]
    key_blocks = [p[1] for p in pairs]
    position = jnp.arange(token_count)
    later_rows = (shard_index > 0) | (position > 0)
    segment_total = segment_counts[0, 0]
    slot_index = jnp.arange(slot_count)
    slot_used = slot_index < segment_total
    start_pos = segment_starts[0]
    smoothing = jnp.where(slot_used, segment_probs[0].astype(jnp.float32) / prob_scale, 0.0)
    reached = slot_used[None, :] & (start_pos[None, :] <= position[:, None])
    member_id = jnp.sum(reached.astype(jnp.int32), axis=1) - 1
    membership = (member_id[:, None] == slot_index[None, :]).astype(jnp.float32)
    leading = (member_id < 0).astype(jnp.float32)
    starts = jnp.any(slot_used[None, :] & (start_pos[None, :] == position[:, None]), axis=1)
    running = jnp.cumsum(jnp.log(1.0 - smoothing))
    lower = slot_index[None, :] <= slot_index[:, None]
    decay_table = jnp.where(
        lower, jnp.exp(jnp.where(lower, running[:, None] - running[None, :], 0.0)), 0.0
    )
    weighted_states = smoothing[:, None] * segment_states[0].astype(jnp.float32)
    local_state = jnp.dot(decay_table, weighted_states, precision=exact)
    keep_all = jnp.exp(running)
    last_log = running[slot_count - 1 :][None]
    state_in = seq_scan(last_log, local_state[slot_count - 1 :], "seq", True)
    smoothed = local_state + keep_all[:, None] * state_in
    picked = jnp.dot(membership, smoothed, precision=exact) + leading[:, None] * state_in
    conf_grad = jnp.sum(grad_rows * picked, axis=1)
    cos_grad = jnp.where(later_rows, jnp.where(starts, -0.5 * conf_grad, 0.5 * conf_grad), 0.0)
    owner_keep = jnp.where(member_id >= 0, keep_all[jnp.maximum(member_id, 0)], 1.0)
    level = jnp.where(later_rows, 0.5, jnp.where(starts, 1.0, 0.0))
    rise = jnp.where(later_rows, jnp.where(starts, -0.5, 0.5), 0.0)
    grad_wide = grad_rows.astype(jnp.float32)
    base_vector = jnp.sum(grad_wide * (owner_keep * level)[:, None], axis=0, keepdims=True)
    rise_rows = lax.optimization_barrier(grad_wide * (owner_keep * rise)[:, None])
    to_prev = jnp.concatenate([token_rows[:1].astype(jnp.float32), cos_grad[:1][None]], axis=1)
    from_next = shifted(to_prev, "seq", -1)
    prev_row = shifted(token_rows[token_count - 1 :], "seq", 1)
    next_row = from_next[:, :-1].astype(token_rows.dtype)
    next_cos_grad = from_next[:, -1:]
    rows_ext = jnp.concatenate([token_rows, prev_row, next_row], axis=0)
    queries_ext = split_dot(rows_ext, query_blocks, index, width)
    keys_ext = split_dot(rows_ext, key_blocks, index, width)
    queries = queries_ext[:token_count]
    key_rows = keys_ext[:token_count]
    query_unit, query_scale = unit_of(queries)
    key_unit, key_scale = unit_of(key_rows)
    key_before, _ = unit_of(keys_ext[token_count : token_count + 1])
    query_next, _ = unit_of(queries_ext[token_count + 1 :])
    key_prior = jnp.concatenate([key_before, key_unit[:-1]], axis=0)
    key_shift = keys_ext[token_count : token_count + 1]
    raw_prior = jnp.concatenate([key_shift, key_rows[:-1]], axis=0)
    prior_sq = jnp.sum(raw_prior * raw_prior, axis=1)
    query_sq = jnp.sum(queries * queries, axis=1)
    cosine = (
        jnp.sum(queries * raw_prior, axis=1) * lax.rsqrt(query_sq + norm_eps) * lax.rsqrt(prior_sq + norm_eps)
    )
    boundary_prob = jnp.where(later_rows, 0.5 * (1.0 - cosine), 1.0)
    confidence = jnp.where(starts, boundary_prob, 1.0 - boundary_prob)
    weighted_grad = confidence[:, None] * grad_rows
    slot_grad = lax.dot_general(membership, weighted_grad, contract_first, precision=exact)
    back_vector = base_vector + jnp.dot(cosine[None, :], rise_rows, precision=exact)
    held = (queries, query_scale, key_rows, key_scale, key_prior, query_unit, query_next)
    grad_in, held = seq_scan(last_log, back_vector, "seq", False, held)
    queries, query_scale, key_rows, key_scale, key_prior, query_unit, query_next = held
    reach_end = jnp.exp(running[slot_count - 1] - running)
    state_grad = (
        lax.dot_general(decay_table, slot_grad, contract_first, precision=exact)
        + reach_end[:, None] * grad_in
    )
    segment_grad = (smoothing[:, None] * state_grad).astype(jnp.bfloat16)
    unit_q_grad = cos_grad[:, None] * key_prior
    prior_grad = cos_grad[:, None] * query_unit
    query_grad = normalize_grad(queries, query_scale, unit_q_grad).astype(jnp.bfloat16)
    unit_k_grad = jnp.concatenate([prior_grad[1:], next_cos_grad * query_next], axis=0)
    key_grad = normalize_grad(key_rows, key_scale, unit_k_grad).astype(jnp.bfloat16)
    parts = []
    for q_block, k_block in zip(query_blocks, key_blocks):
        part = lax.dot_general(query_grad, q_block, contract_last, preferred_element_type=jnp.float32)
        part = part + lax.dot_general(key_grad, k_block, contract_last, preferred_element_type=jnp.float32)
        parts.append(part.astype(jnp.bfloat16))
    x_grad = jnp.concatenate(parts, axis=1)
    slots = jnp.arange(len(index), dtype=jnp.int32)
    order = jnp.sum(jnp.where(jnp.stack(index)[None, :] == slots[:, None], slots[None, :], 0), axis=1)
    x_grad = permute_cols(x_grad, [order[j] for j in range(len(index))], width)
    return (x_grad[None], segment_grad[None])


def solution(mesh):
    placed = (
        P("dp", "seq", None),
        P("dp", "seq", None),
        P("dp", "seq", None),
        P("dp", "seq"),
        P("dp", "seq"),
        P("dp", "seq"),
        P("dp", None),
        P("dp", None),
    )
    return jax.shard_map(
        per_device,
        mesh=mesh,
        in_specs=placed,
        out_specs=(P("dp", "seq", None), P("dp", "seq", None)),
        check_vma=False,
    )
```

```python
import jax
import jax.numpy as jnp
from jax import lax
from jax.sharding import PartitionSpec as P

prob_scale = 65536.0
norm_eps = 1e-06
exact = lax.Precision.HIGHEST
contract_last = (((1,), (1,)), ((), ()))
contract_first = (((0,), (0,)), ((), ()))


def shifted(block, axis, distance):
    devices = range(lax.axis_size(axis))
    route = [(i - distance, i) for i in devices if i - distance in devices]
    return lax.ppermute(block, axis, route)


def normalize_grad(vectors, scales, unit_grad):
    inner_prod = jnp.sum(vectors * unit_grad, axis=-1, keepdims=True)
    return scales * unit_grad - scales * scales * scales * inner_prod * vectors


def seq_scan(log_keep, vectors, axis, from_lower):
    size = lax.axis_size(axis)
    step = 1
    incl_log, incl_vec = log_keep, vectors
    excl_log = jnp.zeros_like(log_keep)
    excl_vec = jnp.zeros_like(vectors)
    while step < size:
        packed = jnp.concatenate([incl_vec, incl_log], axis=-1)
        got = shifted(packed, axis, step if from_lower else -step)
        got_log, got_vec = got[:, -1:], got[:, :-1]
        excl_vec = jnp.exp(excl_log) * got_vec + excl_vec
        excl_log = excl_log + got_log
        if 2 * step < size:
            incl_vec = jnp.exp(incl_log) * got_vec + incl_vec
            incl_log = incl_log + got_log
        step *= 2
    return excl_vec


def gather_blocks(blocks, axis, pair_axis):
    size = lax.axis_size(axis)
    own = lax.axis_index(axis)
    side = lax.axis_index(pair_axis) % 2
    cols = blocks[0].shape[1] // 2
    swap = [(i, i ^ 1) for i in range(size)]
    swap_pair = [(i, i ^ 1) for i in range(lax.axis_size(pair_axis))]
    partner_own = lax.ppermute(blocks, axis, swap)
    pairs = [blocks, partner_own]
    index = [own, own ^ 1]
    last = None
    for k in range(1, size // 2):
        route = [(i, (i + 2 * k) % size) for i in range(size)]
        mine, theirs = [], []
        for block in blocks:
            half = lax.dynamic_slice_in_dim(block, side * cols, cols, axis=1)
            if last is not None:
                half, _ = lax.optimization_barrier((half, last))
            fetched = lax.ppermute(half, axis, route)
            last = fetched
            other = lax.ppermute(fetched, pair_axis, swap_pair)
            fetched_fwd = lax.ppermute(fetched, axis, swap)
            other_fwd = lax.ppermute(other, axis, swap)
            first = side == 0
            mine.append(jnp.where(first, jnp.concatenate([fetched, other], 1), jnp.concatenate([other, fetched], 1)))
            theirs.append(
                jnp.where(first, jnp.concatenate([fetched_fwd, other_fwd], 1), jnp.concatenate([other_fwd, fetched_fwd], 1))
            )
        pairs += [tuple(mine), tuple(theirs)]
        index += [(own - 2 * k) % size, ((own - 2 * k) % size) ^ 1]
    return pairs, index


def direct_scan(log_keep, vectors, axis):
    size = lax.axis_size(axis)
    packed = jnp.concatenate([vectors, log_keep], axis=-1)
    total = jnp.zeros_like(vectors)
    gap = jnp.zeros_like(log_keep)
    for step in range(1, size):
        got = shifted(packed, axis, -step)
        total = total + jnp.exp(gap) * got[:, :-1]
        gap = gap + got[:, -1:]
    return total


def split_dot(rows, blocks, index, width):
    total = None
    for block, at in zip(blocks, index):
        part = lax.dynamic_slice_in_dim(rows, at * width, width, axis=1)
        term = jnp.dot(part, block, preferred_element_type=jnp.float32)
        total = term if total is None else total + term
    return total


def permute_cols(rows, index, width):
    return jnp.concatenate(
        [lax.dynamic_slice_in_dim(rows, at * width, width, axis=1) for at in index], axis=1
    )


def unit_of(rows):
    scale = lax.rsqrt(jnp.sum(rows * rows, axis=1, keepdims=True) + norm_eps)
    return rows * scale, scale


def per_device(
    encoder_out,
    out_grad,
    segment_states,
    segment_starts,
    segment_counts,
    segment_probs,
    query_weight,
    key_weight,
):
    token_rows = encoder_out[0]
    grad_rows = out_grad[0]
    token_count = token_rows.shape[0]
    slot_count = segment_states.shape[1]
    width = query_weight.shape[0]
    shard_index = lax.axis_index("seq")
    pairs, index = gather_blocks((query_weight, key_weight), "dp", "seq")
    query_blocks = [p[0] for p in pairs]
    key_blocks = [p[1] for p in pairs]
    position = jnp.arange(token_count)
    later_rows = (shard_index > 0) | (position > 0)
    segment_total = segment_counts[0, 0]
    slot_index = jnp.arange(slot_count)
    slot_used = slot_index < segment_total
    start_pos = segment_starts[0]
    smoothing = jnp.where(slot_used, segment_probs[0].astype(jnp.float32) / prob_scale, 0.0)
    reached = slot_used[None, :] & (start_pos[None, :] <= position[:, None])
    member_id = jnp.sum(reached.astype(jnp.int32), axis=1) - 1
    membership = (member_id[:, None] == slot_index[None, :]).astype(jnp.float32)
    leading = (member_id < 0).astype(jnp.float32)
    starts = jnp.any(slot_used[None, :] & (start_pos[None, :] == position[:, None]), axis=1)
    running = jnp.cumsum(jnp.log(1.0 - smoothing))
    lower = slot_index[None, :] <= slot_index[:, None]
    decay_table = jnp.where(
        lower, jnp.exp(jnp.where(lower, running[:, None] - running[None, :], 0.0)), 0.0
    )
    weighted_states = smoothing[:, None] * segment_states[0].astype(jnp.float32)
    local_state = jnp.dot(decay_table, weighted_states, precision=exact)
    keep_all = jnp.exp(running)
    last_log = running[slot_count - 1 :][None]
    state_in = seq_scan(last_log, local_state[slot_count - 1 :], "seq", True)
    smoothed = local_state + keep_all[:, None] * state_in
    picked = jnp.dot(membership, smoothed, precision=exact) + leading[:, None] * state_in
    conf_grad = jnp.sum(grad_rows * picked, axis=1)
    cos_grad = jnp.where(later_rows, jnp.where(starts, -0.5 * conf_grad, 0.5 * conf_grad), 0.0)
    owner_keep = jnp.where(member_id >= 0, keep_all[jnp.maximum(member_id, 0)], 1.0)
    level = jnp.where(later_rows, 0.5, jnp.where(starts, 1.0, 0.0))
    rise = jnp.where(later_rows, jnp.where(starts, -0.5, 0.5), 0.0)
    grad_wide = grad_rows.astype(jnp.float32)
    base_vector = jnp.dot((owner_keep * level)[None, :], grad_wide, precision=exact)
    to_prev = jnp.concatenate([token_rows[:1].astype(jnp.float32), cos_grad[:1][None]], axis=1)
    from_next = shifted(to_prev, "seq", -1)
    prev_row = shifted(token_rows[token_count - 1 :], "seq", 1)
    next_row = from_next[:, :-1].astype(token_rows.dtype)
    next_cos_grad = from_next[:, -1:]
    rows_ext = jnp.concatenate([token_rows, prev_row, next_row], axis=0)
    queries_ext = split_dot(rows_ext, query_blocks, index, width)
    keys_ext = split_dot(rows_ext, key_blocks, index, width)
    queries = queries_ext[:token_count]
    key_rows = keys_ext[:token_count]
    query_unit, query_scale = unit_of(queries)
    key_unit, key_scale = unit_of(key_rows)
    key_before, _ = unit_of(keys_ext[token_count : token_count + 1])
    query_next, _ = unit_of(queries_ext[token_count + 1 :])
    key_prior = jnp.concatenate([key_before, key_unit[:-1]], axis=0)
    cosine = jnp.sum(query_unit * key_prior, axis=1)
    boundary_prob = jnp.where(later_rows, 0.5 * (1.0 - cosine), 1.0)
    confidence = jnp.where(starts, boundary_prob, 1.0 - boundary_prob)
    weighted_grad = confidence[:, None] * grad_rows
    slot_grad = lax.dot_general(membership, weighted_grad, contract_first, precision=exact)
    back_vector = base_vector + jnp.dot(
        (owner_keep * rise * cosine)[None, :], grad_wide, precision=exact
    )
    grad_in = seq_scan(last_log, back_vector, "seq", False)
    reach_end = jnp.exp(running[slot_count - 1] - running)
    state_grad = (
        lax.dot_general(decay_table, slot_grad, contract_first, precision=exact)
        + reach_end[:, None] * grad_in
    )
    segment_grad = (smoothing[:, None] * state_grad).astype(jnp.bfloat16)
    unit_q_grad = cos_grad[:, None] * key_prior
    prior_grad = cos_grad[:, None] * query_unit
    query_grad = normalize_grad(queries, query_scale, unit_q_grad).astype(jnp.bfloat16)
    unit_k_grad = jnp.concatenate([prior_grad[1:], next_cos_grad * query_next], axis=0)
    key_grad = normalize_grad(key_rows, key_scale, unit_k_grad).astype(jnp.bfloat16)
    parts = []
    for q_block, k_block in zip(query_blocks, key_blocks):
        part = lax.dot_general(query_grad, q_block, contract_last, preferred_element_type=jnp.float32)
        part = part + lax.dot_general(key_grad, k_block, contract_last, preferred_element_type=jnp.float32)
        parts.append(part.astype(jnp.bfloat16))
    x_grad = jnp.concatenate(parts, axis=1)
    slots = jnp.arange(len(index), dtype=jnp.int32)
    order = jnp.sum(jnp.where(jnp.stack(index)[None, :] == slots[:, None], slots[None, :], 0), axis=1)
    x_grad = permute_cols(x_grad, [order[j] for j in range(len(index))], width)
    return (x_grad[None], segment_grad[None])


def solution(mesh):
    placed = (
        P("dp", "seq", None),
        P("dp", "seq", None),
        P("dp", "seq", None),
        P("dp", "seq"),
        P("dp", "seq"),
        P("dp", "seq"),
        P("dp", None),
        P("dp", None),
    )
    return jax.shard_map(
        per_device,
        mesh=mesh,
        in_specs=placed,
        out_specs=(P("dp", "seq", None), P("dp", "seq", None)),
        check_vma=False,
    )
```

```python
import jax
import jax.numpy as jnp
from jax import lax
from jax.sharding import PartitionSpec as P

prob_scale = 65536.0
norm_eps = 1e-06
exact = lax.Precision.HIGHEST
contract_last = (((1,), (1,)), ((), ()))
contract_first = (((0,), (0,)), ((), ()))


def shifted(block, axis, distance):
    devices = range(lax.axis_size(axis))
    route = [(i - distance, i) for i in devices if i - distance in devices]
    return lax.ppermute(block, axis, route)


def normalize_grad(vectors, scales, unit_grad):
    inner_prod = jnp.sum(vectors * unit_grad, axis=-1, keepdims=True)
    return scales * unit_grad - scales * scales * scales * inner_prod * vectors


def seq_scan(log_keep, vectors, axis, from_lower):
    size = lax.axis_size(axis)
    width = vectors.shape[-1]
    tail = jnp.zeros(vectors.shape[:-1] + (128,), vectors.dtype)
    is_vec = jnp.arange(width + 128) < width
    incl = jnp.concatenate([vectors, tail + log_keep], axis=-1)
    excl = jnp.zeros_like(incl)
    step = 1
    while step < size:
        got = shifted(incl, axis, step if from_lower else -step)
        excl = jnp.where(is_vec, jnp.exp(excl[:, width:width + 1]) * got, got) + excl
        if 2 * step < size:
            incl = jnp.where(is_vec, jnp.exp(incl[:, width:width + 1]) * got, got) + incl
        step *= 2
    return excl[:, :width]


def gather_blocks(blocks, axis):
    size = lax.axis_size(axis)
    own = lax.axis_index(axis)
    pairs = [blocks]
    index = [own]
    for k in range(1, size // 2):
        route = [(i, (i + 2 * k) % size) for i in range(size)]
        pairs.append(lax.ppermute(blocks, axis, route))
        index.append((own - 2 * k) % size)
    swap = [(i, i ^ 1) for i in range(size)]
    partner = lax.ppermute(pairs, axis, swap)
    pairs = pairs + partner
    index = index + [i ^ 1 for i in index]
    return pairs, index


def direct_scan(log_keep, vectors, axis):
    size = lax.axis_size(axis)
    packed = jnp.concatenate([vectors, log_keep], axis=-1)
    total = jnp.zeros_like(vectors)
    gap = jnp.zeros_like(log_keep)
    for step in range(1, size):
        got = shifted(packed, axis, -step)
        total = total + jnp.exp(gap) * got[:, :-1]
        gap = gap + got[:, -1:]
    return total


def split_dot(rows, blocks, index, width):
    total = None
    for block, at in zip(blocks, index):
        part = lax.dynamic_slice_in_dim(rows, at * width, width, axis=1)
        term = jnp.dot(part, block, preferred_element_type=jnp.float32)
        total = term if total is None else total + term
    return total


def permute_cols(rows, index, width):
    return jnp.concatenate(
        [lax.dynamic_slice_in_dim(rows, at * width, width, axis=1) for at in index], axis=1
    )


def unit_of(rows):
    scale = lax.rsqrt(jnp.sum(rows * rows, axis=1, keepdims=True) + norm_eps)
    return rows * scale, scale


def per_device(
    encoder_out,
    out_grad,
    segment_states,
    segment_starts,
    segment_counts,
    segment_probs,
    query_weight,
    key_weight,
):
    token_rows = encoder_out[0]
    grad_rows = out_grad[0]
    token_count = token_rows.shape[0]
    slot_count = segment_states.shape[1]
    width = query_weight.shape[0]
    shard_index = lax.axis_index("seq")
    pairs, index = gather_blocks((query_weight, key_weight), "dp")
    query_blocks = [p[0] for p in pairs]
    key_blocks = [p[1] for p in pairs]
    position = jnp.arange(token_count)
    later_rows = (shard_index > 0) | (position > 0)
    segment_total = segment_counts[0, 0]
    slot_index = jnp.arange(slot_count)
    slot_used = slot_index < segment_total
    start_pos = segment_starts[0]
    smoothing = jnp.where(slot_used, segment_probs[0].astype(jnp.float32) / prob_scale, 0.0)
    reached = slot_used[None, :] & (start_pos[None, :] <= position[:, None])
    member_id = jnp.sum(reached.astype(jnp.int32), axis=1) - 1
    membership = (member_id[:, None] == slot_index[None, :]).astype(jnp.float32)
    leading = (member_id < 0).astype(jnp.float32)
    starts = jnp.any(slot_used[None, :] & (start_pos[None, :] == position[:, None]), axis=1)
    running = jnp.cumsum(jnp.log(1.0 - smoothing))
    lower = slot_index[None, :] <= slot_index[:, None]
    decay_table = jnp.where(
        lower, jnp.exp(jnp.where(lower, running[:, None] - running[None, :], 0.0)), 0.0
    )
    weighted_states = smoothing[:, None] * segment_states[0].astype(jnp.float32)
    local_state = jnp.dot(decay_table, weighted_states, precision=exact)
    keep_all = jnp.exp(running)
    last_log = running[slot_count - 1 :][None]
    state_in = seq_scan(last_log, local_state[slot_count - 1 :], "seq", True)
    smoothed = local_state + keep_all[:, None] * state_in
    picked = jnp.dot(membership, smoothed, precision=exact) + leading[:, None] * state_in
    conf_grad = jnp.sum(grad_rows * picked, axis=1)
    cos_grad = jnp.where(later_rows, jnp.where(starts, -0.5 * conf_grad, 0.5 * conf_grad), 0.0)
    owner_keep = jnp.where(member_id >= 0, keep_all[jnp.maximum(member_id, 0)], 1.0)
    level = jnp.where(later_rows, 0.5, jnp.where(starts, 1.0, 0.0))
    rise = jnp.where(later_rows, jnp.where(starts, -0.5, 0.5), 0.0)
    grad_wide = grad_rows.astype(jnp.float32)
    base_vector = jnp.dot((owner_keep * level)[None, :], grad_wide, precision=exact)
    to_prev = jnp.concatenate([token_rows[:1].astype(jnp.float32), cos_grad[:1][None]], axis=1)
    from_next = shifted(to_prev, "seq", -1)
    prev_row = shifted(token_rows[token_count - 1 :], "seq", 1)
    next_row = from_next[:, :-1].astype(token_rows.dtype)
    next_cos_grad = from_next[:, -1:]
    rows_ext = jnp.concatenate([token_rows, prev_row, next_row], axis=0)
    queries_ext = split_dot(rows_ext, query_blocks, index, width)
    keys_ext = split_dot(rows_ext, key_blocks, index, width)
    queries = queries_ext[:token_count]
    key_rows = keys_ext[:token_count]
    query_unit, query_scale = unit_of(queries)
    key_unit, key_scale = unit_of(key_rows)
    key_before, _ = unit_of(keys_ext[token_count : token_count + 1])
    query_next, _ = unit_of(queries_ext[token_count + 1 :])
    key_prior = jnp.concatenate([key_before, key_unit[:-1]], axis=0)
    cosine = jnp.sum(query_unit * key_prior, axis=1)
    boundary_prob = jnp.where(later_rows, 0.5 * (1.0 - cosine), 1.0)
    confidence = jnp.where(starts, boundary_prob, 1.0 - boundary_prob)
    weighted_grad = confidence[:, None] * grad_rows
    slot_grad = lax.dot_general(membership, weighted_grad, contract_first, precision=exact)
    back_vector = base_vector + jnp.dot(
        (owner_keep * rise * cosine)[None, :], grad_wide, precision=exact
    )
    grad_in = seq_scan(last_log, back_vector, "seq", False)
    reach_end = jnp.exp(running[slot_count - 1] - running)
    state_grad = (
        lax.dot_general(decay_table, slot_grad, contract_first, precision=exact)
        + reach_end[:, None] * grad_in
    )
    segment_grad = (smoothing[:, None] * state_grad).astype(jnp.bfloat16)
    unit_q_grad = cos_grad[:, None] * key_prior
    prior_grad = cos_grad[:, None] * query_unit
    query_grad = normalize_grad(queries, query_scale, unit_q_grad).astype(jnp.bfloat16)
    unit_k_grad = jnp.concatenate([prior_grad[1:], next_cos_grad * query_next], axis=0)
    key_grad = normalize_grad(key_rows, key_scale, unit_k_grad).astype(jnp.bfloat16)
    parts = []
    for q_block, k_block in zip(query_blocks, key_blocks):
        part = lax.dot_general(query_grad, q_block, contract_last, preferred_element_type=jnp.float32)
        part = part + lax.dot_general(key_grad, k_block, contract_last, preferred_element_type=jnp.float32)
        parts.append(part.astype(jnp.bfloat16))
    x_grad = jnp.concatenate(parts, axis=1)
    slots = jnp.arange(len(index), dtype=jnp.int32)
    order = jnp.sum(jnp.where(jnp.stack(index)[None, :] == slots[:, None], slots[None, :], 0), axis=1)
    x_grad = permute_cols(x_grad, [order[j] for j in range(len(index))], width)
    return (x_grad[None], segment_grad[None])


def solution(mesh):
    placed = (
        P("dp", "seq", None),
        P("dp", "seq", None),
        P("dp", "seq", None),
        P("dp", "seq"),
        P("dp", "seq"),
        P("dp", "seq"),
        P("dp", None),
        P("dp", None),
    )
    return jax.shard_map(
        per_device,
        mesh=mesh,
        in_specs=placed,
        out_specs=(P("dp", "seq", None), P("dp", "seq", None)),
        check_vma=False,
    )
```

```python
import jax
import jax.numpy as jnp
from jax import lax
from jax.sharding import PartitionSpec as P

prob_scale = 65536.0
norm_eps = 1e-06
exact = lax.Precision.HIGHEST
contract_last = (((1,), (1,)), ((), ()))
contract_first = (((0,), (0,)), ((), ()))


def shifted(block, axis, distance):
    devices = range(lax.axis_size(axis))
    route = [(i - distance, i) for i in devices if i - distance in devices]
    return lax.ppermute(block, axis, route)


def normalize_grad(vectors, scales, unit_grad):
    inner_prod = jnp.sum(vectors * unit_grad, axis=-1, keepdims=True)
    return scales * unit_grad - scales * scales * scales * inner_prod * vectors


def seq_scan(log_keep, vectors, axis, from_lower):
    size = lax.axis_size(axis)
    width = vectors.shape[-1]
    is_vec = jnp.arange(width + 128) < width
    incl = jnp.pad(vectors, ((0, 0), (0, 128))) + jnp.where(is_vec, 0.0, log_keep)
    excl = jnp.zeros_like(incl)
    step = 1
    while step < size:
        got = shifted(incl, axis, step if from_lower else -step)
        excl = jnp.where(is_vec, jnp.exp(excl[:, width:width + 1]) * got, got) + excl
        if 2 * step < size:
            incl = jnp.where(is_vec, jnp.exp(incl[:, width:width + 1]) * got, got) + incl
        step *= 2
    return excl[:, :width]


def gather_blocks(blocks, axis):
    size = lax.axis_size(axis)
    own = lax.axis_index(axis)
    pairs = [blocks]
    index = [own]
    for k in range(1, size // 2):
        route = [(i, (i + 2 * k) % size) for i in range(size)]
        pairs.append(lax.ppermute(blocks, axis, route))
        index.append((own - 2 * k) % size)
    swap = [(i, i ^ 1) for i in range(size)]
    partner = lax.ppermute(pairs, axis, swap)
    pairs = pairs + partner
    index = index + [i ^ 1 for i in index]
    return pairs, index


def direct_scan(log_keep, vectors, axis):
    size = lax.axis_size(axis)
    packed = jnp.concatenate([vectors, log_keep], axis=-1)
    total = jnp.zeros_like(vectors)
    gap = jnp.zeros_like(log_keep)
    for step in range(1, size):
        got = shifted(packed, axis, -step)
        total = total + jnp.exp(gap) * got[:, :-1]
        gap = gap + got[:, -1:]
    return total


def split_dot(rows, blocks, index, width):
    total = None
    for block, at in zip(blocks, index):
        part = lax.dynamic_slice_in_dim(rows, at * width, width, axis=1)
        term = jnp.dot(part, block, preferred_element_type=jnp.float32)
        total = term if total is None else total + term
    return total


def permute_cols(rows, index, width):
    return jnp.concatenate(
        [lax.dynamic_slice_in_dim(rows, at * width, width, axis=1) for at in index], axis=1
    )


def unit_of(rows):
    scale = lax.rsqrt(jnp.sum(rows * rows, axis=1, keepdims=True) + norm_eps)
    return rows * scale, scale


def per_device(
    encoder_out,
    out_grad,
    segment_states,
    segment_starts,
    segment_counts,
    segment_probs,
    query_weight,
    key_weight,
):
    token_rows = encoder_out[0]
    grad_rows = out_grad[0]
    token_count = token_rows.shape[0]
    slot_count = segment_states.shape[1]
    width = query_weight.shape[0]
    shard_index = lax.axis_index("seq")
    pairs, index = gather_blocks((query_weight, key_weight), "dp")
    query_blocks = [p[0] for p in pairs]
    key_blocks = [p[1] for p in pairs]
    position = jnp.arange(token_count)
    later_rows = (shard_index > 0) | (position > 0)
    segment_total = segment_counts[0, 0]
    slot_index = jnp.arange(slot_count)
    slot_used = slot_index < segment_total
    start_pos = segment_starts[0]
    smoothing = jnp.where(slot_used, segment_probs[0].astype(jnp.float32) / prob_scale, 0.0)
    reached = slot_used[None, :] & (start_pos[None, :] <= position[:, None])
    member_id = jnp.sum(reached.astype(jnp.int32), axis=1) - 1
    membership = (member_id[:, None] == slot_index[None, :]).astype(jnp.float32)
    leading = (member_id < 0).astype(jnp.float32)
    starts = jnp.any(slot_used[None, :] & (start_pos[None, :] == position[:, None]), axis=1)
    running = jnp.cumsum(jnp.log(1.0 - smoothing))
    lower = slot_index[None, :] <= slot_index[:, None]
    decay_table = jnp.where(
        lower, jnp.exp(jnp.where(lower, running[:, None] - running[None, :], 0.0)), 0.0
    )
    weighted_states = smoothing[:, None] * segment_states[0].astype(jnp.float32)
    local_state = jnp.dot(decay_table, weighted_states, precision=exact)
    keep_all = jnp.exp(running)
    last_log = running[slot_count - 1 :][None]
    state_in = seq_scan(last_log, local_state[slot_count - 1 :], "seq", True)
    smoothed = local_state + keep_all[:, None] * state_in
    picked = jnp.dot(membership, smoothed, precision=exact) + leading[:, None] * state_in
    conf_grad = jnp.sum(grad_rows * picked, axis=1)
    cos_grad = jnp.where(later_rows, jnp.where(starts, -0.5 * conf_grad, 0.5 * conf_grad), 0.0)
    owner_keep = jnp.where(member_id >= 0, keep_all[jnp.maximum(member_id, 0)], 1.0)
    level = jnp.where(later_rows, 0.5, jnp.where(starts, 1.0, 0.0))
    rise = jnp.where(later_rows, jnp.where(starts, -0.5, 0.5), 0.0)
    grad_wide = grad_rows.astype(jnp.float32)
    base_vector = jnp.dot((owner_keep * level)[None, :], grad_wide, precision=exact)
    to_prev = jnp.concatenate([token_rows[:1].astype(jnp.float32), cos_grad[:1][None]], axis=1)
    from_next = shifted(to_prev, "seq", -1)
    prev_row = shifted(token_rows[token_count - 1 :], "seq", 1)
    next_row = from_next[:, :-1].astype(token_rows.dtype)
    next_cos_grad = from_next[:, -1:]
    rows_ext = jnp.concatenate([token_rows, prev_row, next_row], axis=0)
    queries_ext = split_dot(rows_ext, query_blocks, index, width)
    keys_ext = split_dot(rows_ext, key_blocks, index, width)
    queries = queries_ext[:token_count]
    key_rows = keys_ext[:token_count]
    query_unit, query_scale = unit_of(queries)
    key_unit, key_scale = unit_of(key_rows)
    key_before, _ = unit_of(keys_ext[token_count : token_count + 1])
    query_next, _ = unit_of(queries_ext[token_count + 1 :])
    key_prior = jnp.concatenate([key_before, key_unit[:-1]], axis=0)
    cosine = jnp.sum(query_unit * key_prior, axis=1)
    boundary_prob = jnp.where(later_rows, 0.5 * (1.0 - cosine), 1.0)
    confidence = jnp.where(starts, boundary_prob, 1.0 - boundary_prob)
    weighted_grad = confidence[:, None] * grad_rows
    slot_grad = lax.dot_general(membership, weighted_grad, contract_first, precision=exact)
    back_vector = base_vector + jnp.dot(
        (owner_keep * rise * cosine)[None, :], grad_wide, precision=exact
    )
    grad_in = seq_scan(last_log, back_vector, "seq", False)
    reach_end = jnp.exp(running[slot_count - 1] - running)
    state_grad = (
        lax.dot_general(decay_table, slot_grad, contract_first, precision=exact)
        + reach_end[:, None] * grad_in
    )
    segment_grad = (smoothing[:, None] * state_grad).astype(jnp.bfloat16)
    unit_q_grad = cos_grad[:, None] * key_prior
    prior_grad = cos_grad[:, None] * query_unit
    query_grad = normalize_grad(queries, query_scale, unit_q_grad).astype(jnp.bfloat16)
    unit_k_grad = jnp.concatenate([prior_grad[1:], next_cos_grad * query_next], axis=0)
    key_grad = normalize_grad(key_rows, key_scale, unit_k_grad).astype(jnp.bfloat16)
    parts = []
    for q_block, k_block in zip(query_blocks, key_blocks):
        part = lax.dot_general(query_grad, q_block, contract_last, preferred_element_type=jnp.float32)
        part = part + lax.dot_general(key_grad, k_block, contract_last, preferred_element_type=jnp.float32)
        parts.append(part.astype(jnp.bfloat16))
    x_grad = jnp.concatenate(parts, axis=1)
    slots = jnp.arange(len(index), dtype=jnp.int32)
    order = jnp.sum(jnp.where(jnp.stack(index)[None, :] == slots[:, None], slots[None, :], 0), axis=1)
    x_grad = permute_cols(x_grad, [order[j] for j in range(len(index))], width)
    return (x_grad[None], segment_grad[None])


def solution(mesh):
    placed = (
        P("dp", "seq", None),
        P("dp", "seq", None),
        P("dp", "seq", None),
        P("dp", "seq"),
        P("dp", "seq"),
        P("dp", "seq"),
        P("dp", None),
        P("dp", None),
    )
    return jax.shard_map(
        per_device,
        mesh=mesh,
        in_specs=placed,
        out_specs=(P("dp", "seq", None), P("dp", "seq", None)),
        check_vma=False,
    )
```

```python
import jax
import jax.numpy as jnp
from jax import lax
from jax.sharding import PartitionSpec as P

prob_scale = 65536.0
norm_eps = 1e-06
exact = lax.Precision.HIGHEST
contract_last = (((1,), (1,)), ((), ()))
contract_first = (((0,), (0,)), ((), ()))


def shifted(block, axis, distance):
    devices = range(lax.axis_size(axis))
    route = [(i - distance, i) for i in devices if i - distance in devices]
    return lax.ppermute(block, axis, route)


def normalize_grad(vectors, scales, unit_grad):
    inner_prod = jnp.sum(vectors * unit_grad, axis=-1, keepdims=True)
    return scales * unit_grad - scales * scales * scales * inner_prod * vectors


def seq_scan(log_keep, vectors, axis, from_lower):
    size = lax.axis_size(axis)
    width = vectors.shape[-1]
    tail = jnp.zeros(vectors.shape[:-1] + (128,), vectors.dtype)
    is_vec = jnp.arange(width + 128) < width
    incl = jnp.concatenate([vectors, tail + log_keep], axis=-1)
    excl = jnp.zeros_like(incl)
    step = 1
    while step < size:
        got = shifted(incl, axis, step if from_lower else -step)
        excl = jnp.where(is_vec, jnp.exp(excl[:, width:width + 1]) * got, got) + excl
        if 2 * step < size:
            incl = jnp.where(is_vec, jnp.exp(incl[:, width:width + 1]) * got, got) + incl
        step *= 2
    return excl[:, :width]


def gather_blocks(blocks, axis):
    size = lax.axis_size(axis)
    own = lax.axis_index(axis)
    pairs = [blocks]
    index = [own]
    for k in range(1, size // 2):
        route = [(i, (i + 2 * k) % size) for i in range(size)]
        pairs.append(lax.ppermute(blocks, axis, route))
        index.append((own - 2 * k) % size)
    swap = [(i, i ^ 1) for i in range(size)]
    partner = lax.ppermute(pairs, axis, swap)
    pairs = pairs + partner
    index = index + [i ^ 1 for i in index]
    return pairs, index


def direct_scan(log_keep, vectors, axis):
    size = lax.axis_size(axis)
    packed = jnp.concatenate([vectors, log_keep], axis=-1)
    total = jnp.zeros_like(vectors)
    gap = jnp.zeros_like(log_keep)
    for step in range(1, size):
        got = shifted(packed, axis, -step)
        total = total + jnp.exp(gap) * got[:, :-1]
        gap = gap + got[:, -1:]
    return total


def split_dot(rows, blocks, index, width):
    total = None
    for block, at in zip(blocks, index):
        part = lax.dynamic_slice_in_dim(rows, at * width, width, axis=1)
        term = jnp.dot(part, block, preferred_element_type=jnp.float32)
        total = term if total is None else total + term
    return total


def permute_cols(rows, index, width):
    return jnp.concatenate(
        [lax.dynamic_slice_in_dim(rows, at * width, width, axis=1) for at in index], axis=1
    )


def unit_of(rows):
    scale = lax.rsqrt(jnp.sum(rows * rows, axis=1, keepdims=True) + norm_eps)
    return rows * scale, scale


def per_device(
    encoder_out,
    out_grad,
    segment_states,
    segment_starts,
    segment_counts,
    segment_probs,
    query_weight,
    key_weight,
):
    token_rows = encoder_out[0]
    grad_rows = out_grad[0]
    token_count = token_rows.shape[0]
    slot_count = segment_states.shape[1]
    width = query_weight.shape[0]
    shard_index = lax.axis_index("seq")
    pairs, index = gather_blocks((query_weight, key_weight), "dp")
    query_blocks = [p[0] for p in pairs]
    key_blocks = [p[1] for p in pairs]
    position = jnp.arange(token_count)
    later_rows = (shard_index > 0) | (position > 0)
    segment_total = segment_counts[0, 0]
    slot_index = jnp.arange(slot_count)
    slot_used = slot_index < segment_total
    start_pos = segment_starts[0]
    smoothing = jnp.where(slot_used, segment_probs[0].astype(jnp.float32) / prob_scale, 0.0)
    reached = slot_used[None, :] & (start_pos[None, :] <= position[:, None])
    member_id = jnp.sum(reached.astype(jnp.int32), axis=1) - 1
    membership = (member_id[:, None] == slot_index[None, :]).astype(jnp.float32)
    leading = (member_id < 0).astype(jnp.float32)
    starts = jnp.any(slot_used[None, :] & (start_pos[None, :] == position[:, None]), axis=1)
    running = jnp.cumsum(jnp.log(1.0 - smoothing))
    lower = slot_index[None, :] <= slot_index[:, None]
    decay_table = jnp.where(
        lower, jnp.exp(jnp.where(lower, running[:, None] - running[None, :], 0.0)), 0.0
    )
    weighted_states = smoothing[:, None] * segment_states[0].astype(jnp.float32)
    local_state = jnp.dot(decay_table, weighted_states, precision=exact)
    keep_all = jnp.exp(running)
    last_log = running[slot_count - 1 :][None]
    state_in = seq_scan(last_log, local_state[slot_count - 1 :], "seq", True)
    smoothed = local_state + keep_all[:, None] * state_in
    picked = jnp.dot(membership, smoothed, precision=exact) + leading[:, None] * state_in
    conf_grad = jnp.sum(grad_rows * picked, axis=1)
    cos_grad = jnp.where(later_rows, jnp.where(starts, -0.5 * conf_grad, 0.5 * conf_grad), 0.0)
    owner_keep = jnp.where(member_id >= 0, keep_all[jnp.maximum(member_id, 0)], 1.0)
    level = jnp.where(later_rows, 0.5, jnp.where(starts, 1.0, 0.0))
    rise = jnp.where(later_rows, jnp.where(starts, -0.5, 0.5), 0.0)
    grad_wide = grad_rows.astype(jnp.float32)
    base_vector = jnp.dot((owner_keep * level)[None, :], grad_wide, precision=exact)
    to_prev = jnp.concatenate([token_rows[:1].astype(jnp.float32), cos_grad[:1][None]], axis=1)
    from_next = shifted(to_prev, "seq", -1)
    prev_row = shifted(token_rows[token_count - 1 :], "seq", 1)
    next_row = from_next[:, :-1].astype(token_rows.dtype)
    next_cos_grad = from_next[:, -1:]
    rows_ext = jnp.concatenate([token_rows, prev_row, next_row], axis=0)
    queries_ext = split_dot(rows_ext, query_blocks, index, width)
    keys_ext = split_dot(rows_ext, key_blocks, index, width)
    queries = queries_ext[:token_count]
    key_rows = keys_ext[:token_count]
    query_unit, query_scale = unit_of(queries)
    key_unit, key_scale = unit_of(key_rows)
    key_before, _ = unit_of(keys_ext[token_count : token_count + 1])
    query_next, _ = unit_of(queries_ext[token_count + 1 :])
    key_prior = jnp.concatenate([key_before, key_unit[:-1]], axis=0)
    cosine = jnp.sum(query_unit * key_prior, axis=1)
    boundary_prob = jnp.where(later_rows, 0.5 * (1.0 - cosine), 1.0)
    confidence = jnp.where(starts, boundary_prob, 1.0 - boundary_prob)
    weighted_grad = confidence[:, None] * grad_rows
    slot_grad = lax.dot_general(membership, weighted_grad, contract_first, precision=exact)
    back_vector = base_vector + jnp.dot(
        (owner_keep * rise * cosine)[None, :], grad_wide, precision=exact
    )
    grad_in = seq_scan(last_log, back_vector, "seq", False)
    reach_end = jnp.exp(running[slot_count - 1] - running)
    state_local = lax.optimization_barrier(
        lax.dot_general(decay_table, slot_grad, contract_first, precision=exact)
    )
    state_grad = state_local + reach_end[:, None] * grad_in
    segment_grad = (smoothing[:, None] * state_grad).astype(jnp.bfloat16)
    unit_q_grad = cos_grad[:, None] * key_prior
    prior_grad = cos_grad[:, None] * query_unit
    query_grad = normalize_grad(queries, query_scale, unit_q_grad).astype(jnp.bfloat16)
    unit_k_grad = jnp.concatenate([prior_grad[1:], next_cos_grad * query_next], axis=0)
    key_grad = normalize_grad(key_rows, key_scale, unit_k_grad).astype(jnp.bfloat16)
    parts = []
    for q_block, k_block in zip(query_blocks, key_blocks):
        part = lax.dot_general(query_grad, q_block, contract_last, preferred_element_type=jnp.float32)
        part = part + lax.dot_general(key_grad, k_block, contract_last, preferred_element_type=jnp.float32)
        parts.append(part.astype(jnp.bfloat16))
    x_grad = jnp.concatenate(parts, axis=1)
    slots = jnp.arange(len(index), dtype=jnp.int32)
    order = jnp.sum(jnp.where(jnp.stack(index)[None, :] == slots[:, None], slots[None, :], 0), axis=1)
    x_grad = permute_cols(x_grad, [order[j] for j in range(len(index))], width)
    return (x_grad[None], segment_grad[None])


def solution(mesh):
    placed = (
        P("dp", "seq", None),
        P("dp", "seq", None),
        P("dp", "seq", None),
        P("dp", "seq"),
        P("dp", "seq"),
        P("dp", "seq"),
        P("dp", None),
        P("dp", None),
    )
    return jax.shard_map(
        per_device,
        mesh=mesh,
        in_specs=placed,
        out_specs=(P("dp", "seq", None), P("dp", "seq", None)),
        check_vma=False,
    )
```

```python
import jax
import jax.numpy as jnp
from jax import lax
from jax.sharding import PartitionSpec as P

prob_scale = 65536.0
norm_eps = 1e-06
exact = lax.Precision.HIGHEST
contract_last = (((1,), (1,)), ((), ()))
contract_first = (((0,), (0,)), ((), ()))


def shifted(block, axis, distance):
    devices = range(lax.axis_size(axis))
    route = [(i - distance, i) for i in devices if i - distance in devices]
    return lax.ppermute(block, axis, route)


def normalize_grad(vectors, scales, unit_grad):
    inner_prod = jnp.sum(vectors * unit_grad, axis=-1, keepdims=True)
    return scales * unit_grad - scales * scales * scales * inner_prod * vectors


def seq_scan(log_keep, vectors, axis, from_lower):
    size = lax.axis_size(axis)
    width = vectors.shape[-1]
    tail = jnp.zeros(vectors.shape[:-1] + (128,), vectors.dtype)
    is_vec = jnp.arange(width + 128) < width
    incl = jnp.concatenate([vectors, tail + log_keep], axis=-1)
    excl = jnp.zeros_like(incl)
    step = 1
    while step < size:
        got = shifted(incl, axis, step if from_lower else -step)
        excl = jnp.where(is_vec, jnp.exp(excl[:, width:width + 1]) * got, got) + excl
        if 2 * step < size:
            incl = jnp.where(is_vec, jnp.exp(incl[:, width:width + 1]) * got, got) + incl
        step *= 2
    return excl[:, :width]


def gather_blocks(blocks, axis):
    size = lax.axis_size(axis)
    own = lax.axis_index(axis)
    pairs = [blocks]
    index = [own]
    for k in range(1, size // 2):
        route = [(i, (i + 2 * k) % size) for i in range(size)]
        first = lax.ppermute(blocks[0], axis, route)
        later, _ = lax.optimization_barrier((blocks[1], first))
        pairs.append((first, lax.ppermute(later, axis, route)))
        index.append((own - 2 * k) % size)
    swap = [(i, i ^ 1) for i in range(size)]
    partner = lax.ppermute(pairs, axis, swap)
    pairs = pairs + partner
    index = index + [i ^ 1 for i in index]
    return pairs, index


def direct_scan(log_keep, vectors, axis):
    size = lax.axis_size(axis)
    packed = jnp.concatenate([vectors, log_keep], axis=-1)
    total = jnp.zeros_like(vectors)
    gap = jnp.zeros_like(log_keep)
    for step in range(1, size):
        got = shifted(packed, axis, -step)
        total = total + jnp.exp(gap) * got[:, :-1]
        gap = gap + got[:, -1:]
    return total


def split_dot(rows, blocks, index, width):
    total = None
    for block, at in zip(blocks, index):
        part = lax.dynamic_slice_in_dim(rows, at * width, width, axis=1)
        term = jnp.dot(part, block, preferred_element_type=jnp.float32)
        total = term if total is None else total + term
    return total


def permute_cols(rows, index, width):
    return jnp.concatenate(
        [lax.dynamic_slice_in_dim(rows, at * width, width, axis=1) for at in index], axis=1
    )


def unit_of(rows):
    scale = lax.rsqrt(jnp.sum(rows * rows, axis=1, keepdims=True) + norm_eps)
    return rows * scale, scale


def per_device(
    encoder_out,
    out_grad,
    segment_states,
    segment_starts,
    segment_counts,
    segment_probs,
    query_weight,
    key_weight,
):
    token_rows = encoder_out[0]
    grad_rows = out_grad[0]
    token_count = token_rows.shape[0]
    slot_count = segment_states.shape[1]
    width = query_weight.shape[0]
    shard_index = lax.axis_index("seq")
    pairs, index = gather_blocks((query_weight, key_weight), "dp")
    query_blocks = [p[0] for p in pairs]
    key_blocks = [p[1] for p in pairs]
    position = jnp.arange(token_count)
    later_rows = (shard_index > 0) | (position > 0)
    segment_total = segment_counts[0, 0]
    slot_index = jnp.arange(slot_count)
    slot_used = slot_index < segment_total
    start_pos = segment_starts[0]
    smoothing = jnp.where(slot_used, segment_probs[0].astype(jnp.float32) / prob_scale, 0.0)
    reached = slot_used[None, :] & (start_pos[None, :] <= position[:, None])
    member_id = jnp.sum(reached.astype(jnp.int32), axis=1) - 1
    membership = (member_id[:, None] == slot_index[None, :]).astype(jnp.float32)
    leading = (member_id < 0).astype(jnp.float32)
    starts = jnp.any(slot_used[None, :] & (start_pos[None, :] == position[:, None]), axis=1)
    running = jnp.cumsum(jnp.log(1.0 - smoothing))
    lower = slot_index[None, :] <= slot_index[:, None]
    decay_table = jnp.where(
        lower, jnp.exp(jnp.where(lower, running[:, None] - running[None, :], 0.0)), 0.0
    )
    weighted_states = smoothing[:, None] * segment_states[0].astype(jnp.float32)
    local_state = jnp.dot(decay_table, weighted_states, precision=exact)
    keep_all = jnp.exp(running)
    last_log = running[slot_count - 1 :][None]
    state_in = seq_scan(last_log, local_state[slot_count - 1 :], "seq", True)
    smoothed = local_state + keep_all[:, None] * state_in
    picked = jnp.dot(membership, smoothed, precision=exact) + leading[:, None] * state_in
    conf_grad = jnp.sum(grad_rows * picked, axis=1)
    cos_grad = jnp.where(later_rows, jnp.where(starts, -0.5 * conf_grad, 0.5 * conf_grad), 0.0)
    owner_keep = jnp.where(member_id >= 0, keep_all[jnp.maximum(member_id, 0)], 1.0)
    level = jnp.where(later_rows, 0.5, jnp.where(starts, 1.0, 0.0))
    rise = jnp.where(later_rows, jnp.where(starts, -0.5, 0.5), 0.0)
    grad_wide = grad_rows.astype(jnp.float32)
    base_vector = jnp.dot((owner_keep * level)[None, :], grad_wide, precision=exact)
    to_prev = jnp.concatenate([token_rows[:1].astype(jnp.float32), cos_grad[:1][None]], axis=1)
    from_next = shifted(to_prev, "seq", -1)
    prev_row = shifted(token_rows[token_count - 1 :], "seq", 1)
    next_row = from_next[:, :-1].astype(token_rows.dtype)
    next_cos_grad = from_next[:, -1:]
    rows_ext = jnp.concatenate([token_rows, prev_row, next_row], axis=0)
    queries_ext = split_dot(rows_ext, query_blocks, index, width)
    keys_ext = split_dot(rows_ext, key_blocks, index, width)
    queries = queries_ext[:token_count]
    key_rows = keys_ext[:token_count]
    query_unit, query_scale = unit_of(queries)
    key_unit, key_scale = unit_of(key_rows)
    key_before, _ = unit_of(keys_ext[token_count : token_count + 1])
    query_next, _ = unit_of(queries_ext[token_count + 1 :])
    key_prior = jnp.concatenate([key_before, key_unit[:-1]], axis=0)
    cosine = jnp.sum(query_unit * key_prior, axis=1)
    boundary_prob = jnp.where(later_rows, 0.5 * (1.0 - cosine), 1.0)
    confidence = jnp.where(starts, boundary_prob, 1.0 - boundary_prob)
    weighted_grad = confidence[:, None] * grad_rows
    slot_grad = lax.dot_general(membership, weighted_grad, contract_first, precision=exact)
    back_vector = base_vector + jnp.dot(
        (owner_keep * rise * cosine)[None, :], grad_wide, precision=exact
    )
    grad_in = seq_scan(last_log, back_vector, "seq", False)
    reach_end = jnp.exp(running[slot_count - 1] - running)
    state_grad = (
        lax.dot_general(decay_table, slot_grad, contract_first, precision=exact)
        + reach_end[:, None] * grad_in
    )
    segment_grad = (smoothing[:, None] * state_grad).astype(jnp.bfloat16)
    unit_q_grad = cos_grad[:, None] * key_prior
    prior_grad = cos_grad[:, None] * query_unit
    query_grad = normalize_grad(queries, query_scale, unit_q_grad).astype(jnp.bfloat16)
    unit_k_grad = jnp.concatenate([prior_grad[1:], next_cos_grad * query_next], axis=0)
    key_grad = normalize_grad(key_rows, key_scale, unit_k_grad).astype(jnp.bfloat16)
    parts = []
    for q_block, k_block in zip(query_blocks, key_blocks):
        part = lax.dot_general(query_grad, q_block, contract_last, preferred_element_type=jnp.float32)
        part = part + lax.dot_general(key_grad, k_block, contract_last, preferred_element_type=jnp.float32)
        parts.append(part.astype(jnp.bfloat16))
    x_grad = jnp.concatenate(parts, axis=1)
    slots = jnp.arange(len(index), dtype=jnp.int32)
    order = jnp.sum(jnp.where(jnp.stack(index)[None, :] == slots[:, None], slots[None, :], 0), axis=1)
    x_grad = permute_cols(x_grad, [order[j] for j in range(len(index))], width)
    return (x_grad[None], segment_grad[None])


def solution(mesh):
    placed = (
        P("dp", "seq", None),
        P("dp", "seq", None),
        P("dp", "seq", None),
        P("dp", "seq"),
        P("dp", "seq"),
        P("dp", "seq"),
        P("dp", None),
        P("dp", None),
    )
    return jax.shard_map(
        per_device,
        mesh=mesh,
        in_specs=placed,
        out_specs=(P("dp", "seq", None), P("dp", "seq", None)),
        check_vma=False,
    )
```

```python
import jax
import jax.numpy as jnp
from jax import lax
from jax.sharding import PartitionSpec as P

prob_scale = 65536.0
norm_eps = 1e-06
exact = lax.Precision.HIGHEST
contract_last = (((1,), (1,)), ((), ()))
contract_first = (((0,), (0,)), ((), ()))


def shifted(block, axis, distance):
    devices = range(lax.axis_size(axis))
    route = [(i - distance, i) for i in devices if i - distance in devices]
    return lax.ppermute(block, axis, route)


def normalize_grad(vectors, scales, unit_grad):
    inner_prod = jnp.sum(vectors * unit_grad, axis=-1, keepdims=True)
    return scales * unit_grad - scales * scales * scales * inner_prod * vectors


def seq_scan(log_keep, vectors, axis, from_lower):
    size = lax.axis_size(axis)
    width = vectors.shape[-1]
    tail = jnp.zeros(vectors.shape[:-1] + (128,), vectors.dtype)
    is_vec = jnp.arange(width + 128) < width
    incl = jnp.concatenate([vectors, tail + log_keep], axis=-1)
    excl = jnp.zeros_like(incl)
    step = 1
    while step < size:
        got = shifted(incl, axis, step if from_lower else -step)
        excl = jnp.where(is_vec, jnp.exp(excl[:, width:width + 1]) * got, got) + excl
        if 2 * step < size:
            incl = jnp.where(is_vec, jnp.exp(incl[:, width:width + 1]) * got, got) + incl
        step *= 2
    return excl[:, :width]


def gather_blocks(blocks, axis):
    size = lax.axis_size(axis)
    own = lax.axis_index(axis)
    pairs = [blocks]
    index = [own]
    for k in range(1, size // 2):
        route = [(i, (i + 2 * k) % size) for i in range(size)]
        pairs.append(lax.ppermute(blocks, axis, route))
        index.append((own - 2 * k) % size)
    swap = [(i, i ^ 1) for i in range(size)]
    partner = lax.ppermute(pairs, axis, swap)
    pairs = pairs + partner
    index = index + [i ^ 1 for i in index]
    return pairs, index


def direct_scan(log_keep, vectors, axis):
    size = lax.axis_size(axis)
    packed = jnp.concatenate([vectors, log_keep], axis=-1)
    total = jnp.zeros_like(vectors)
    gap = jnp.zeros_like(log_keep)
    for step in range(1, size):
        got = shifted(packed, axis, -step)
        total = total + jnp.exp(gap) * got[:, :-1]
        gap = gap + got[:, -1:]
    return total


def split_dot(rows, blocks, index, width):
    total = None
    for block, at in zip(blocks, index):
        part = lax.dynamic_slice_in_dim(rows, at * width, width, axis=1)
        term = jnp.dot(part, block, preferred_element_type=jnp.float32)
        total = term if total is None else total + term
    return total


def permute_cols(rows, index, width):
    return jnp.concatenate(
        [lax.dynamic_slice_in_dim(rows, at * width, width, axis=1) for at in index], axis=1
    )


def unit_of(rows):
    scale = lax.rsqrt(jnp.sum(rows * rows, axis=1, keepdims=True) + norm_eps)
    return rows * scale, scale


def per_device(
    encoder_out,
    out_grad,
    segment_states,
    segment_starts,
    segment_counts,
    segment_probs,
    query_weight,
    key_weight,
):
    token_rows = encoder_out[0]
    grad_rows = out_grad[0]
    token_count = token_rows.shape[0]
    slot_count = segment_states.shape[1]
    width = query_weight.shape[0]
    shard_index = lax.axis_index("seq")
    pairs, index = gather_blocks((query_weight, key_weight), "dp")
    query_blocks = [p[0] for p in pairs]
    key_blocks = [p[1] for p in pairs]
    position = jnp.arange(token_count)
    later_rows = (shard_index > 0) | (position > 0)
    segment_total = segment_counts[0, 0]
    slot_index = jnp.arange(slot_count)
    slot_used = slot_index < segment_total
    start_pos = segment_starts[0]
    smoothing = jnp.where(slot_used, segment_probs[0].astype(jnp.float32) / prob_scale, 0.0)
    reached = slot_used[None, :] & (start_pos[None, :] <= position[:, None])
    member_id = jnp.sum(reached.astype(jnp.int32), axis=1) - 1
    membership = (member_id[:, None] == slot_index[None, :]).astype(jnp.float32)
    leading = (member_id < 0).astype(jnp.float32)
    starts = jnp.any(slot_used[None, :] & (start_pos[None, :] == position[:, None]), axis=1)
    running = jnp.cumsum(jnp.log(1.0 - smoothing))
    lower = slot_index[None, :] <= slot_index[:, None]
    decay_table = jnp.where(
        lower, jnp.exp(jnp.where(lower, running[:, None] - running[None, :], 0.0)), 0.0
    )
    weighted_states = smoothing[:, None] * segment_states[0].astype(jnp.float32)
    local_state = jnp.dot(decay_table, weighted_states, precision=exact)
    keep_all = jnp.exp(running)
    last_log = running[slot_count - 1 :][None]
    state_in = seq_scan(last_log, local_state[slot_count - 1 :], "seq", True)
    smoothed = local_state + keep_all[:, None] * state_in
    picked = jnp.dot(membership, smoothed, precision=exact) + leading[:, None] * state_in
    conf_grad = jnp.sum(grad_rows * picked, axis=1)
    cos_grad = jnp.where(later_rows, jnp.where(starts, -0.5 * conf_grad, 0.5 * conf_grad), 0.0)
    owner_keep = jnp.where(member_id >= 0, keep_all[jnp.maximum(member_id, 0)], 1.0)
    level = jnp.where(later_rows, 0.5, jnp.where(starts, 1.0, 0.0))
    rise = jnp.where(later_rows, jnp.where(starts, -0.5, 0.5), 0.0)
    grad_wide = grad_rows.astype(jnp.float32)
    base_vector = jnp.dot((owner_keep * level)[None, :], grad_wide, precision=exact)
    to_prev = jnp.concatenate([token_rows[:1].astype(jnp.float32), cos_grad[:1][None]], axis=1)
    from_next = shifted(to_prev, "seq", -1)
    prev_row = shifted(token_rows[token_count - 1 :], "seq", 1)
    next_row = from_next[:, :-1].astype(token_rows.dtype)
    next_cos_grad = from_next[:, -1:]
    spare = jnp.zeros((6, token_rows.shape[1]), token_rows.dtype)
    rows_ext = jnp.concatenate([token_rows, prev_row, next_row, spare], axis=0)
    queries_ext = split_dot(rows_ext, query_blocks, index, width)
    keys_ext = split_dot(rows_ext, key_blocks, index, width)
    queries = queries_ext[:token_count]
    key_rows = keys_ext[:token_count]
    query_unit, query_scale = unit_of(queries)
    key_unit, key_scale = unit_of(key_rows)
    key_before, _ = unit_of(keys_ext[token_count : token_count + 1])
    query_next, _ = unit_of(queries_ext[token_count + 1 : token_count + 2])
    key_prior = jnp.concatenate([key_before, key_unit[:-1]], axis=0)
    cosine = jnp.sum(query_unit * key_prior, axis=1)
    boundary_prob = jnp.where(later_rows, 0.5 * (1.0 - cosine), 1.0)
    confidence = jnp.where(starts, boundary_prob, 1.0 - boundary_prob)
    weighted_grad = confidence[:, None] * grad_rows
    slot_grad = lax.dot_general(membership, weighted_grad, contract_first, precision=exact)
    back_vector = base_vector + jnp.dot(
        (owner_keep * rise * cosine)[None, :], grad_wide, precision=exact
    )
    grad_in = seq_scan(last_log, back_vector, "seq", False)
    reach_end = jnp.exp(running[slot_count - 1] - running)
    state_grad = (
        lax.dot_general(decay_table, slot_grad, contract_first, precision=exact)
        + reach_end[:, None] * grad_in
    )
    segment_grad = (smoothing[:, None] * state_grad).astype(jnp.bfloat16)
    unit_q_grad = cos_grad[:, None] * key_prior
    prior_grad = cos_grad[:, None] * query_unit
    query_grad = normalize_grad(queries, query_scale, unit_q_grad).astype(jnp.bfloat16)
    unit_k_grad = jnp.concatenate([prior_grad[1:], next_cos_grad * query_next], axis=0)
    key_grad = normalize_grad(key_rows, key_scale, unit_k_grad).astype(jnp.bfloat16)
    parts = []
    for q_block, k_block in zip(query_blocks, key_blocks):
        part = lax.dot_general(query_grad, q_block, contract_last, preferred_element_type=jnp.float32)
        part = part + lax.dot_general(key_grad, k_block, contract_last, preferred_element_type=jnp.float32)
        parts.append(part.astype(jnp.bfloat16))
    x_grad = jnp.concatenate(parts, axis=1)
    slots = jnp.arange(len(index), dtype=jnp.int32)
    order = jnp.sum(jnp.where(jnp.stack(index)[None, :] == slots[:, None], slots[None, :], 0), axis=1)
    x_grad = permute_cols(x_grad, [order[j] for j in range(len(index))], width)
    return (x_grad[None], segment_grad[None])


def solution(mesh):
    placed = (
        P("dp", "seq", None),
        P("dp", "seq", None),
        P("dp", "seq", None),
        P("dp", "seq"),
        P("dp", "seq"),
        P("dp", "seq"),
        P("dp", None),
        P("dp", None),
    )
    return jax.shard_map(
        per_device,
        mesh=mesh,
        in_specs=placed,
        out_specs=(P("dp", "seq", None), P("dp", "seq", None)),
        check_vma=False,
    )
```

```python
import jax
import jax.numpy as jnp
from jax import lax
from jax.sharding import PartitionSpec as P

prob_scale = 65536.0
norm_eps = 1e-06
exact = lax.Precision.HIGHEST
contract_last = (((1,), (1,)), ((), ()))
contract_first = (((0,), (0,)), ((), ()))


def shifted(block, axis, distance):
    devices = range(lax.axis_size(axis))
    route = [(i - distance, i) for i in devices if i - distance in devices]
    return lax.ppermute(block, axis, route)


def normalize_grad(vectors, scales, unit_grad):
    inner_prod = jnp.sum(vectors * unit_grad, axis=-1, keepdims=True)
    return scales * unit_grad - scales * scales * scales * inner_prod * vectors


def seq_scan(log_keep, vectors, axis, from_lower, held=None):
    size = lax.axis_size(axis)
    width = vectors.shape[-1]
    tail = jnp.zeros(vectors.shape[:-1] + (128,), vectors.dtype)
    is_vec = jnp.arange(width + 128) < width
    incl = jnp.concatenate([vectors, tail + log_keep], axis=-1)
    excl = jnp.zeros_like(incl)
    step = 1
    while step < size:
        got = shifted(incl, axis, step if from_lower else -step)
        if held is not None and step == 1:
            got, held = lax.optimization_barrier((got, held))
        excl = jnp.where(is_vec, jnp.exp(excl[:, width:width + 1]) * got, got) + excl
        if 2 * step < size:
            incl = jnp.where(is_vec, jnp.exp(incl[:, width:width + 1]) * got, got) + incl
        step *= 2
    if held is not None:
        return excl[:, :width], held
    return excl[:, :width]


def gather_blocks(blocks, axis):
    size = lax.axis_size(axis)
    own = lax.axis_index(axis)
    pairs = [blocks]
    index = [own]
    for k in range(1, size // 2):
        route = [(i, (i + 2 * k) % size) for i in range(size)]
        pairs.append(lax.ppermute(blocks, axis, route))
        index.append((own - 2 * k) % size)
    swap = [(i, i ^ 1) for i in range(size)]
    partner = lax.ppermute(pairs, axis, swap)
    pairs = pairs + partner
    index = index + [i ^ 1 for i in index]
    return pairs, index


def direct_scan(log_keep, vectors, axis):
    size = lax.axis_size(axis)
    packed = jnp.concatenate([vectors, log_keep], axis=-1)
    total = jnp.zeros_like(vectors)
    gap = jnp.zeros_like(log_keep)
    for step in range(1, size):
        got = shifted(packed, axis, -step)
        total = total + jnp.exp(gap) * got[:, :-1]
        gap = gap + got[:, -1:]
    return total


def split_dot(rows, blocks, index, width):
    total = None
    for block, at in zip(blocks, index):
        part = lax.dynamic_slice_in_dim(rows, at * width, width, axis=1)
        term = jnp.dot(part, block, preferred_element_type=jnp.float32)
        total = term if total is None else total + term
    return total


def permute_cols(rows, index, width):
    return jnp.concatenate(
        [lax.dynamic_slice_in_dim(rows, at * width, width, axis=1) for at in index], axis=1
    )


def unit_of(rows):
    scale = lax.rsqrt(jnp.sum(rows * rows, axis=1, keepdims=True) + norm_eps)
    return rows * scale, scale


def per_device(
    encoder_out,
    out_grad,
    segment_states,
    segment_starts,
    segment_counts,
    segment_probs,
    query_weight,
    key_weight,
):
    token_rows = encoder_out[0]
    grad_rows = out_grad[0]
    token_count = token_rows.shape[0]
    slot_count = segment_states.shape[1]
    width = query_weight.shape[0]
    shard_index = lax.axis_index("seq")
    pairs, index = gather_blocks((query_weight, key_weight), "dp")
    query_blocks = [p[0] for p in pairs]
    key_blocks = [p[1] for p in pairs]
    position = jnp.arange(token_count)
    later_rows = (shard_index > 0) | (position > 0)
    segment_total = segment_counts[0, 0]
    slot_index = jnp.arange(slot_count)
    slot_used = slot_index < segment_total
    start_pos = segment_starts[0]
    smoothing = jnp.where(slot_used, segment_probs[0].astype(jnp.float32) / prob_scale, 0.0)
    reached = slot_used[None, :] & (start_pos[None, :] <= position[:, None])
    member_id = jnp.sum(reached.astype(jnp.int32), axis=1) - 1
    membership = (member_id[:, None] == slot_index[None, :]).astype(jnp.float32)
    leading = (member_id < 0).astype(jnp.float32)
    starts = jnp.any(slot_used[None, :] & (start_pos[None, :] == position[:, None]), axis=1)
    running = jnp.cumsum(jnp.log(1.0 - smoothing))
    lower = slot_index[None, :] <= slot_index[:, None]
    decay_table = jnp.where(
        lower, jnp.exp(jnp.where(lower, running[:, None] - running[None, :], 0.0)), 0.0
    )
    weighted_states = smoothing[:, None] * segment_states[0].astype(jnp.float32)
    local_state = jnp.dot(decay_table, weighted_states, precision=exact)
    keep_all = jnp.exp(running)
    last_log = running[slot_count - 1 :][None]
    state_in = seq_scan(last_log, local_state[slot_count - 1 :], "seq", True)
    smoothed = local_state + keep_all[:, None] * state_in
    picked = jnp.dot(membership, smoothed, precision=exact) + leading[:, None] * state_in
    conf_grad = jnp.sum(grad_rows * picked, axis=1)
    cos_grad = jnp.where(later_rows, jnp.where(starts, -0.5 * conf_grad, 0.5 * conf_grad), 0.0)
    owner_keep = jnp.where(member_id >= 0, keep_all[jnp.maximum(member_id, 0)], 1.0)
    level = jnp.where(later_rows, 0.5, jnp.where(starts, 1.0, 0.0))
    rise = jnp.where(later_rows, jnp.where(starts, -0.5, 0.5), 0.0)
    grad_wide = grad_rows.astype(jnp.float32)
    base_vector = jnp.dot((owner_keep * level)[None, :], grad_wide, precision=exact)
    to_prev = jnp.concatenate([token_rows[:1].astype(jnp.float32), cos_grad[:1][None]], axis=1)
    from_next = shifted(to_prev, "seq", -1)
    prev_row = shifted(token_rows[token_count - 1 :], "seq", 1)
    next_row = from_next[:, :-1].astype(token_rows.dtype)
    next_cos_grad = from_next[:, -1:]
    rows_ext = jnp.concatenate([token_rows, prev_row, next_row], axis=0)
    queries_ext = split_dot(rows_ext, query_blocks, index, width)
    keys_ext = split_dot(rows_ext, key_blocks, index, width)
    queries = queries_ext[:token_count]
    key_rows = keys_ext[:token_count]
    query_unit, query_scale = unit_of(queries)
    key_unit, key_scale = unit_of(key_rows)
    key_before, _ = unit_of(keys_ext[token_count : token_count + 1])
    query_next, _ = unit_of(queries_ext[token_count + 1 :])
    key_prior = jnp.concatenate([key_before, key_unit[:-1]], axis=0)
    cosine = jnp.sum(query_unit * key_prior, axis=1)
    boundary_prob = jnp.where(later_rows, 0.5 * (1.0 - cosine), 1.0)
    confidence = jnp.where(starts, boundary_prob, 1.0 - boundary_prob)
    weighted_grad = confidence[:, None] * grad_rows
    slot_grad = lax.dot_general(membership, weighted_grad, contract_first, precision=exact)
    back_vector = base_vector + jnp.dot(
        (owner_keep * rise * cosine)[None, :], grad_wide, precision=exact
    )
    grad_in, (key_rows, key_scale, query_unit, query_next) = seq_scan(
        last_log, back_vector, "seq", False, (key_rows, key_scale, query_unit, query_next)
    )
    reach_end = jnp.exp(running[slot_count - 1] - running)
    state_grad = (
        lax.dot_general(decay_table, slot_grad, contract_first, precision=exact)
        + reach_end[:, None] * grad_in
    )
    segment_grad = (smoothing[:, None] * state_grad).astype(jnp.bfloat16)
    unit_q_grad = cos_grad[:, None] * key_prior
    prior_grad = cos_grad[:, None] * query_unit
    query_grad = normalize_grad(queries, query_scale, unit_q_grad).astype(jnp.bfloat16)
    unit_k_grad = jnp.concatenate([prior_grad[1:], next_cos_grad * query_next], axis=0)
    key_grad = normalize_grad(key_rows, key_scale, unit_k_grad).astype(jnp.bfloat16)
    parts = []
    for q_block, k_block in zip(query_blocks, key_blocks):
        part = lax.dot_general(query_grad, q_block, contract_last, preferred_element_type=jnp.float32)
        part = part + lax.dot_general(key_grad, k_block, contract_last, preferred_element_type=jnp.float32)
        parts.append(part.astype(jnp.bfloat16))
    x_grad = jnp.concatenate(parts, axis=1)
    slots = jnp.arange(len(index), dtype=jnp.int32)
    order = jnp.sum(jnp.where(jnp.stack(index)[None, :] == slots[:, None], slots[None, :], 0), axis=1)
    x_grad = permute_cols(x_grad, [order[j] for j in range(len(index))], width)
    return (x_grad[None], segment_grad[None])


def solution(mesh):
    placed = (
        P("dp", "seq", None),
        P("dp", "seq", None),
        P("dp", "seq", None),
        P("dp", "seq"),
        P("dp", "seq"),
        P("dp", "seq"),
        P("dp", None),
        P("dp", None),
    )
    return jax.shard_map(
        per_device,
        mesh=mesh,
        in_specs=placed,
        out_specs=(P("dp", "seq", None), P("dp", "seq", None)),
        check_vma=False,
    )
```

```python
import jax
import jax.numpy as jnp
from jax import lax
from jax.sharding import PartitionSpec as P

prob_scale = 65536.0
norm_eps = 1e-06
exact = lax.Precision.HIGHEST
contract_last = (((1,), (1,)), ((), ()))
contract_first = (((0,), (0,)), ((), ()))


def shifted(block, axis, distance):
    devices = range(lax.axis_size(axis))
    route = [(i - distance, i) for i in devices if i - distance in devices]
    return lax.ppermute(block, axis, route)


def normalize_grad(vectors, scales, unit_grad):
    inner_prod = jnp.sum(vectors * unit_grad, axis=-1, keepdims=True)
    return scales * unit_grad - scales * scales * scales * inner_prod * vectors


def seq_scan(log_keep, vectors, axis, from_lower):
    size = lax.axis_size(axis)
    width = vectors.shape[-1]
    tail = jnp.zeros(vectors.shape[:-1] + (128,), vectors.dtype)
    is_vec = jnp.arange(width + 128) < width
    incl = jnp.concatenate([vectors, tail + log_keep], axis=-1)
    excl = jnp.zeros_like(incl)
    step = 1
    while step < size:
        got = shifted(incl, axis, step if from_lower else -step)
        excl = jnp.where(is_vec, jnp.exp(excl[:, width:width + 1]) * got, got) + excl
        if 2 * step < size:
            incl = jnp.where(is_vec, jnp.exp(incl[:, width:width + 1]) * got, got) + incl
        step *= 2
    return excl[:, :width]


def gather_blocks(blocks, axis):
    size = lax.axis_size(axis)
    own = lax.axis_index(axis)
    pairs = [blocks]
    index = [own]
    for k in range(1, size // 2):
        route = [(i, (i + 2 * k) % size) for i in range(size)]
        pairs.append(lax.ppermute(blocks, axis, route))
        index.append((own - 2 * k) % size)
    swap = [(i, i ^ 1) for i in range(size)]
    partner = lax.ppermute(pairs, axis, swap)
    pairs = pairs + partner
    index = index + [i ^ 1 for i in index]
    return pairs, index


def direct_scan(log_keep, vectors, axis):
    size = lax.axis_size(axis)
    packed = jnp.concatenate([vectors, log_keep], axis=-1)
    total = jnp.zeros_like(vectors)
    gap = jnp.zeros_like(log_keep)
    for step in range(1, size):
        got = shifted(packed, axis, -step)
        total = total + jnp.exp(gap) * got[:, :-1]
        gap = gap + got[:, -1:]
    return total


def split_dot(rows, blocks, index, width):
    total = None
    for block, at in zip(blocks, index):
        part = lax.dynamic_slice_in_dim(rows, at * width, width, axis=1)
        term = jnp.dot(part, block, preferred_element_type=jnp.float32)
        total = term if total is None else total + term
    return total


def permute_cols(rows, index, width):
    return jnp.concatenate(
        [lax.dynamic_slice_in_dim(rows, at * width, width, axis=1) for at in index], axis=1
    )


def unit_of(rows):
    scale = lax.rsqrt(jnp.sum(rows * rows, axis=1, keepdims=True) + norm_eps)
    return rows * scale, scale


def per_device(
    encoder_out,
    out_grad,
    segment_states,
    segment_starts,
    segment_counts,
    segment_probs,
    query_weight,
    key_weight,
):
    token_rows = encoder_out[0]
    grad_rows = out_grad[0]
    token_count = token_rows.shape[0]
    slot_count = segment_states.shape[1]
    width = query_weight.shape[0]
    shard_index = lax.axis_index("seq")
    pairs, index = gather_blocks((query_weight, key_weight), "dp")
    query_blocks = [p[0] for p in pairs]
    key_blocks = [p[1] for p in pairs]
    position = jnp.arange(token_count)
    later_rows = (shard_index > 0) | (position > 0)
    segment_total = segment_counts[0, 0]
    slot_index = jnp.arange(slot_count)
    slot_used = slot_index < segment_total
    start_pos = segment_starts[0]
    smoothing = jnp.where(slot_used, segment_probs[0].astype(jnp.float32) / prob_scale, 0.0)
    reached = slot_used[None, :] & (start_pos[None, :] <= position[:, None])
    member_id = jnp.sum(reached.astype(jnp.int32), axis=1) - 1
    membership = (member_id[:, None] == slot_index[None, :]).astype(jnp.float32)
    leading = (member_id < 0).astype(jnp.float32)
    starts = jnp.any(slot_used[None, :] & (start_pos[None, :] == position[:, None]), axis=1)
    running = jnp.cumsum(jnp.log(1.0 - smoothing))
    lower = slot_index[None, :] <= slot_index[:, None]
    decay_table = jnp.where(
        lower, jnp.exp(jnp.where(lower, running[:, None] - running[None, :], 0.0)), 0.0
    )
    weighted_states = smoothing[:, None] * segment_states[0].astype(jnp.float32)
    local_state = jnp.dot(decay_table, weighted_states, precision=exact)
    keep_all = jnp.exp(running)
    last_log = running[slot_count - 1 :][None]
    state_in = seq_scan(last_log, local_state[slot_count - 1 :], "seq", True)
    smoothed = local_state + keep_all[:, None] * state_in
    picked = jnp.dot(membership, smoothed, precision=exact) + leading[:, None] * state_in
    conf_grad = jnp.sum(grad_rows * picked, axis=1)
    cos_grad = jnp.where(later_rows, jnp.where(starts, -0.5 * conf_grad, 0.5 * conf_grad), 0.0)
    owner_keep = jnp.where(member_id >= 0, keep_all[jnp.maximum(member_id, 0)], 1.0)
    level = jnp.where(later_rows, 0.5, jnp.where(starts, 1.0, 0.0))
    rise = jnp.where(later_rows, jnp.where(starts, -0.5, 0.5), 0.0)
    grad_wide = grad_rows.astype(jnp.float32)
    base_vector = jnp.dot((owner_keep * level)[None, :], grad_wide, precision=exact)
    to_prev = jnp.concatenate([token_rows[:1].astype(jnp.float32), cos_grad[:1][None]], axis=1)
    from_next = shifted(to_prev, "seq", -1)
    prev_row = shifted(token_rows[token_count - 1 :], "seq", 1)
    next_row = from_next[:, :-1].astype(token_rows.dtype)
    next_cos_grad = from_next[:, -1:]
    rows_ext = jnp.concatenate([token_rows, prev_row, next_row], axis=0)
    queries_ext = split_dot(rows_ext, query_blocks, index, width)
    keys_ext = split_dot(rows_ext, key_blocks, index, width)
    queries = queries_ext[:token_count]
    key_rows = keys_ext[:token_count]
    query_unit, query_scale = unit_of(queries)
    key_unit, key_scale = unit_of(key_rows)
    key_before, _ = unit_of(keys_ext[token_count : token_count + 1])
    query_next, _ = unit_of(queries_ext[token_count + 1 :])
    key_prior = jnp.concatenate([key_before, key_unit[:-1]], axis=0)
    raw_prior = jnp.concatenate([keys_ext[token_count : token_count + 1], key_rows[:-1]], axis=0)
    prior_sq = jnp.sum(raw_prior * raw_prior, axis=1)
    query_sq = jnp.sum(queries * queries, axis=1)
    cosine = (
        jnp.sum(queries * raw_prior, axis=1) * lax.rsqrt(query_sq + norm_eps) * lax.rsqrt(prior_sq + norm_eps)
    )
    boundary_prob = jnp.where(later_rows, 0.5 * (1.0 - cosine), 1.0)
    confidence = jnp.where(starts, boundary_prob, 1.0 - boundary_prob)
    weighted_grad = confidence[:, None] * grad_rows
    slot_grad = lax.dot_general(membership, weighted_grad, contract_first, precision=exact)
    back_vector = base_vector + jnp.dot(
        (owner_keep * rise * cosine)[None, :], grad_wide, precision=exact
    )
    grad_in = seq_scan(last_log, back_vector, "seq", False)
    reach_end = jnp.exp(running[slot_count - 1] - running)
    state_grad = (
        lax.dot_general(decay_table, slot_grad, contract_first, precision=exact)
        + reach_end[:, None] * grad_in
    )
    segment_grad = (smoothing[:, None] * state_grad).astype(jnp.bfloat16)
    unit_q_grad = cos_grad[:, None] * key_prior
    prior_grad = cos_grad[:, None] * query_unit
    query_grad = normalize_grad(queries, query_scale, unit_q_grad).astype(jnp.bfloat16)
    unit_k_grad = jnp.concatenate([prior_grad[1:], next_cos_grad * query_next], axis=0)
    key_grad = normalize_grad(key_rows, key_scale, unit_k_grad).astype(jnp.bfloat16)
    parts = []
    for q_block, k_block in zip(query_blocks, key_blocks):
        part = lax.dot_general(query_grad, q_block, contract_last, preferred_element_type=jnp.float32)
        part = part + lax.dot_general(key_grad, k_block, contract_last, preferred_element_type=jnp.float32)
        parts.append(part.astype(jnp.bfloat16))
    x_grad = jnp.concatenate(parts, axis=1)
    slots = jnp.arange(len(index), dtype=jnp.int32)
    order = jnp.sum(jnp.where(jnp.stack(index)[None, :] == slots[:, None], slots[None, :], 0), axis=1)
    x_grad = permute_cols(x_grad, [order[j] for j in range(len(index))], width)
    return (x_grad[None], segment_grad[None])


def solution(mesh):
    placed = (
        P("dp", "seq", None),
        P("dp", "seq", None),
        P("dp", "seq", None),
        P("dp", "seq"),
        P("dp", "seq"),
        P("dp", "seq"),
        P("dp", None),
        P("dp", None),
    )
    return jax.shard_map(
        per_device,
        mesh=mesh,
        in_specs=placed,
        out_specs=(P("dp", "seq", None), P("dp", "seq", None)),
        check_vma=False,
    )
```

```python
import jax
import jax.numpy as jnp
from jax import lax
from jax.sharding import PartitionSpec as P

prob_scale = 65536.0
norm_eps = 1e-06
exact = lax.Precision.HIGHEST
contract_last = (((1,), (1,)), ((), ()))
contract_first = (((0,), (0,)), ((), ()))


def shifted(block, axis, distance):
    devices = range(lax.axis_size(axis))
    route = [(i - distance, i) for i in devices if i - distance in devices]
    return lax.ppermute(block, axis, route)


def normalize_grad(vectors, scales, unit_grad):
    inner_prod = jnp.sum(vectors * unit_grad, axis=-1, keepdims=True)
    return scales * unit_grad - scales * scales * scales * inner_prod * vectors


def seq_scan(log_keep, vectors, axis, from_lower):
    size = lax.axis_size(axis)
    width = vectors.shape[-1]
    tail = jnp.zeros(vectors.shape[:-1] + (128,), vectors.dtype)
    is_vec = jnp.arange(width + 128) < width
    incl = jnp.concatenate([vectors, tail + log_keep], axis=-1)
    excl = jnp.zeros_like(incl)
    step = 1
    while step < size:
        got = shifted(incl, axis, step if from_lower else -step)
        excl = jnp.where(is_vec, jnp.exp(excl[:, width:width + 1]) * got, got) + excl
        if 2 * step < size:
            incl = jnp.where(is_vec, jnp.exp(incl[:, width:width + 1]) * got, got) + incl
        step *= 2
    return excl[:, :width]


def gather_blocks(blocks, axis):
    size = lax.axis_size(axis)
    own = lax.axis_index(axis)
    pairs = [blocks]
    index = [own]
    for k in range(1, size // 2):
        route = [(i, (i + 2 * k) % size) for i in range(size)]
        pairs.append(lax.ppermute(blocks, axis, route))
        index.append((own - 2 * k) % size)
    swap = [(i, i ^ 1) for i in range(size)]
    partner = lax.ppermute(pairs, axis, swap)
    pairs = pairs + partner
    index = index + [i ^ 1 for i in index]
    return pairs, index


def direct_scan(log_keep, vectors, axis):
    size = lax.axis_size(axis)
    packed = jnp.concatenate([vectors, log_keep], axis=-1)
    total = jnp.zeros_like(vectors)
    gap = jnp.zeros_like(log_keep)
    for step in range(1, size):
        got = shifted(packed, axis, -step)
        total = total + jnp.exp(gap) * got[:, :-1]
        gap = gap + got[:, -1:]
    return total


def split_dot(rows, blocks, index, width):
    total = None
    for block, at in zip(blocks, index):
        part = lax.dynamic_slice_in_dim(rows, at * width, width, axis=1)
        term = jnp.dot(part, block, preferred_element_type=jnp.float32)
        total = term if total is None else total + term
    return total


def permute_cols(rows, index, width):
    return jnp.concatenate(
        [lax.dynamic_slice_in_dim(rows, at * width, width, axis=1) for at in index], axis=1
    )


def unit_of(rows):
    scale = lax.rsqrt(jnp.sum(rows * rows, axis=1, keepdims=True) + norm_eps)
    return rows * scale, scale


def per_device(
    encoder_out,
    out_grad,
    segment_states,
    segment_starts,
    segment_counts,
    segment_probs,
    query_weight,
    key_weight,
):
    token_rows = encoder_out[0]
    grad_rows = out_grad[0]
    token_count = token_rows.shape[0]
    slot_count = segment_states.shape[1]
    width = query_weight.shape[0]
    shard_index = lax.axis_index("seq")
    pairs, index = gather_blocks((query_weight, key_weight), "dp")
    query_blocks = [p[0] for p in pairs]
    key_blocks = [p[1] for p in pairs]
    position = jnp.arange(token_count)
    later_rows = (shard_index > 0) | (position > 0)
    segment_total = segment_counts[0, 0]
    slot_index = jnp.arange(slot_count)
    slot_used = slot_index < segment_total
    start_pos = segment_starts[0]
    smoothing = jnp.where(slot_used, segment_probs[0].astype(jnp.float32) / prob_scale, 0.0)
    reached = slot_used[None, :] & (start_pos[None, :] <= position[:, None])
    member_id = jnp.sum(reached.astype(jnp.int32), axis=1) - 1
    membership = (member_id[:, None] == slot_index[None, :]).astype(jnp.float32)
    leading = (member_id < 0).astype(jnp.float32)
    starts = jnp.any(slot_used[None, :] & (start_pos[None, :] == position[:, None]), axis=1)
    running = jnp.cumsum(jnp.log(1.0 - smoothing))
    lower = slot_index[None, :] <= slot_index[:, None]
    decay_table = jnp.where(
        lower, jnp.exp(jnp.where(lower, running[:, None] - running[None, :], 0.0)), 0.0
    )
    weighted_states = smoothing[:, None] * segment_states[0].astype(jnp.float32)
    local_state = jnp.dot(decay_table, weighted_states, precision=exact)
    keep_all = jnp.exp(running)
    last_log = running[slot_count - 1 :][None]
    state_in = seq_scan(last_log, local_state[slot_count - 1 :], "seq", True)
    smoothed = local_state + keep_all[:, None] * state_in
    picked = jnp.dot(membership, smoothed, precision=exact) + leading[:, None] * state_in
    conf_grad = jnp.sum(grad_rows * picked, axis=1)
    cos_grad = jnp.where(later_rows, jnp.where(starts, -0.5 * conf_grad, 0.5 * conf_grad), 0.0)
    owner_keep = jnp.where(member_id >= 0, keep_all[jnp.maximum(member_id, 0)], 1.0)
    level = jnp.where(later_rows, 0.5, jnp.where(starts, 1.0, 0.0))
    rise = jnp.where(later_rows, jnp.where(starts, -0.5, 0.5), 0.0)
    grad_wide = grad_rows.astype(jnp.float32)
    base_vector = jnp.dot((owner_keep * level)[None, :], grad_wide, precision=exact)
    to_prev = jnp.concatenate([token_rows[:1].astype(jnp.float32), cos_grad[:1][None]], axis=1)
    from_next = shifted(to_prev, "seq", -1)
    prev_row = shifted(token_rows[token_count - 1 :], "seq", 1)
    next_row = from_next[:, :-1].astype(token_rows.dtype)
    next_cos_grad = from_next[:, -1:]
    rows_ext = jnp.concatenate([token_rows, prev_row, next_row], axis=0)
    queries_ext = split_dot(rows_ext, query_blocks, index, width)
    keys_ext = split_dot(rows_ext, key_blocks, index, width)
    queries = queries_ext[:token_count]
    key_rows = keys_ext[:token_count]
    query_unit, query_scale = unit_of(queries)
    key_unit, key_scale = unit_of(key_rows)
    key_before, _ = unit_of(keys_ext[token_count : token_count + 1])
    query_next, _ = unit_of(queries_ext[token_count + 1 :])
    key_prior = jnp.concatenate([key_before, key_unit[:-1]], axis=0)
    cosine = jnp.sum(query_unit * key_prior, axis=1)
    boundary_prob = jnp.where(later_rows, 0.5 * (1.0 - cosine), 1.0)
    confidence = jnp.where(starts, boundary_prob, 1.0 - boundary_prob)
    weighted_grad = confidence[:, None] * grad_rows
    slot_grad = lax.dot_general(membership, weighted_grad, contract_first, precision=exact)
    back_vector = base_vector + jnp.dot(
        (owner_keep * rise * cosine)[None, :], grad_wide, precision=exact
    )
    grad_in = seq_scan(last_log, back_vector, "seq", False)
    reach_end = jnp.exp(running[slot_count - 1] - running)
    local_part = lax.optimization_barrier(
        smoothing[:, None] * lax.dot_general(decay_table, slot_grad, contract_first, precision=exact)
    )
    segment_grad = (local_part + (smoothing * reach_end)[:, None] * grad_in).astype(jnp.bfloat16)
    unit_q_grad = cos_grad[:, None] * key_prior
    prior_grad = cos_grad[:, None] * query_unit
    query_grad = normalize_grad(queries, query_scale, unit_q_grad).astype(jnp.bfloat16)
    unit_k_grad = jnp.concatenate([prior_grad[1:], next_cos_grad * query_next], axis=0)
    key_grad = normalize_grad(key_rows, key_scale, unit_k_grad).astype(jnp.bfloat16)
    parts = []
    for q_block, k_block in zip(query_blocks, key_blocks):
        part = lax.dot_general(query_grad, q_block, contract_last, preferred_element_type=jnp.float32)
        part = part + lax.dot_general(key_grad, k_block, contract_last, preferred_element_type=jnp.float32)
        parts.append(part.astype(jnp.bfloat16))
    x_grad = jnp.concatenate(parts, axis=1)
    slots = jnp.arange(len(index), dtype=jnp.int32)
    order = jnp.sum(jnp.where(jnp.stack(index)[None, :] == slots[:, None], slots[None, :], 0), axis=1)
    x_grad = permute_cols(x_grad, [order[j] for j in range(len(index))], width)
    return (x_grad[None], segment_grad[None])


def solution(mesh):
    placed = (
        P("dp", "seq", None),
        P("dp", "seq", None),
        P("dp", "seq", None),
        P("dp", "seq"),
        P("dp", "seq"),
        P("dp", "seq"),
        P("dp", None),
        P("dp", None),
    )
    return jax.shard_map(
        per_device,
        mesh=mesh,
        in_specs=placed,
        out_specs=(P("dp", "seq", None), P("dp", "seq", None)),
        check_vma=False,
    )
```
